32 devices in a mesh: group: 1, ctx: 16 (over z, y, x), head: 2 (over core).
Axes of the slice: x: 2, y: 2, z: 4, core: 2. Of those that a mesh axis runs over, the one named last changes fastest.
Arguments:
- pair_raw: bfloat16 [4096, 2, 1024], P(('group', 'ctx'), None, 'head'), may hold values from -6 to 6
- value_raw: bfloat16 [4096, 2048], P(('group', 'ctx'), 'head'), may hold values from -6 to 6
- gate_raw: bfloat16 [4096, 2048], P(('group', 'ctx'), 'head'), may hold values from -6 to 6
- write_strength: float32 [4096, 16], P(('group', 'ctx'), 'head'), may hold values from 0.05 to 0.95
- log_decay: float32 [4096, 16], P(('group', 'ctx'), 'head'), may hold values from -2.6 to 0
- segment_ids: int32 [4096], P('group'), may hold values from 0 to 1, never falling along the last dimension, each value on 1 to 3968 neighbouring positions
- pair_filter: float32 [4, 2, 1024], P(None, None, 'head'), may hold values from -3 to 3
- value_filter: float32 [4, 2048], P(None, 'head'), may hold values from -3 to 3
- norm_gain: float32 [128], replicated, may hold values from 0.1 to 1.9
- out_weight: bfloat16 [2048, 2048], P('head'), may hold values from -0.125 to 0.125
- residual: bfloat16 [4096, 2048], P(('group', 'ctx', 'head')), may hold values from -27 to 27
- post_gain: float32 [2048], replicated, may hold values from 0.1 to 1.9
- routes: int32 [4096, 10], P(('group', 'ctx', 'head')), may hold values from 0 to 31, all different within a row; in each aligned block of 128 rows (0 to 127, 128 to 255, ...) at most 50 rows name the same one
- route_weights: float32 [4096, 10], P(('group', 'ctx', 'head')), may hold values from 0.05 to 0.3
- expert_up: bfloat16 [32, 2048, 1024], P(('ctx', 'head')), may hold values from -0.125 to 0.125
- expert_down: bfloat16 [32, 512, 2048], P(('ctx', 'head')), may hold values from -0.25 to 0.25
Outputs:
- layer_out: bfloat16 [4096, 2048], P(('group', 'ctx', 'head'))
The draws below stay inside these ranges and needn't reach their ends.
Inputs may be any that keep to these rules, and one draw needn't show every extreme that they name: `routes`: in each aligned block of 128 rows (the rows of one device) no expert is named by more than 50 rows; a row names 10 different experts. `segment_ids`: rollout numbers never fall along the slab; a rollout holds 1 to 3968 tokens of the slab.
All inputs are finite; a program needn't handle non-finite values.
Results may differ from the reference program's by a relative error of at most 0.012.
Values may be sent and summed in bfloat16 or wider, within the bound.
No kernel may reach another device: no remote copies, remote signals or barrier semaphores. Data moves between devices by JAX's collectives and lax.ppermute only.
A program may use at most 128 MiB of HBM per device.

```python
import math
import jax
import jax.numpy as jnp
import numpy as np
from jax import lax

D = 2048
HK = 8
VALUE_HEADS = 16
DK = 128
DV = 128
FFE = 512
TOPK = 10
KW = 4
BLOCK = 64
SEGS = 2
TOK_CTX = 256
SLAB_TOKENS = 4096
TOK_DEV = 128
EXPERTS = 32
CAP = 50
SEG_MOST = 3968
N_CTX = 16
N_HEAD = 2


def draw_log_decay(key, part):
    key_sequence = jax.random.split(jax.random.fold_in(key, 11), 7)
    fast_share = 0.5
    fast_heads = jax.random.uniform(key_sequence[0], (VALUE_HEADS,)) < fast_share
    fast_rate = jax.random.uniform(key_sequence[1], (VALUE_HEADS,), minval=0.08, maxval=0.15)
    slow_rate = 0.3 / SLAB_TOKENS * jax.random.uniform(key_sequence[2], (VALUE_HEADS,), minval=0.5, maxval=1.0)
    head_decay_rate = jnp.where(fast_heads, fast_rate, slow_rate)
    block_count = SLAB_TOKENS // TOK_CTX
    block_multiplier = jnp.exp(jax.random.uniform(key_sequence[3], (block_count, 1, VALUE_HEADS), minval=math.log(0.5), maxval=math.log(2.0)))
    block_multiplier = jnp.broadcast_to(block_multiplier, (block_count, TOK_CTX, VALUE_HEADS)).reshape(SLAB_TOKENS, VALUE_HEADS)
    element_multiplier = jnp.exp(jax.random.uniform(key_sequence[4], (SLAB_TOKENS, VALUE_HEADS), minval=math.log(0.7), maxval=math.log(1.4)))
    spike_position = jax.random.randint(key_sequence[5], (3,), 0, SLAB_TOKENS)
    spike_penalty = jax.random.uniform(key_sequence[6], (3, VALUE_HEADS), minval=0.2, maxval=0.5)
    token_positions = jnp.arange(SLAB_TOKENS)
    match_count = (token_positions[None, :, None] == spike_position[:, None, None]).astype(jnp.float32)
    spike_events = jnp.sum(match_count * jnp.log1p(-spike_penalty)[:, None, :], axis=0)
    return (-head_decay_rate[None, :] * block_multiplier * element_multiplier + spike_events).astype(jnp.float32)


def draw_residual(key, part):
    key_sequence = jax.random.split(jax.random.fold_in(key, 23), 3)
    row_scale = jnp.exp(jax.random.uniform(key_sequence[0], (SLAB_TOKENS, 1), minval=0.0, maxval=math.log(10.0))) / 3.0
    col_scale = jnp.exp(jax.random.uniform(key_sequence[1], (1, D), minval=math.log(0.5), maxval=math.log(2.0)))
    base = jnp.clip(jax.random.normal(key_sequence[2], (SLAB_TOKENS, D)), -4.0, 4.0)
    return (base * row_scale * col_scale).astype(jnp.bfloat16)


def block_scale(key, shape, cuts, smallest, top_value):
    def one(axis_at, blocks):
        draws = jax.random.uniform(jax.random.fold_in(jax.random.fold_in(key, 6), axis_at), (blocks,), jnp.float32, smallest / len(cuts), top_value / len(cuts))
        return jnp.repeat(jnp.exp(draws), shape[axis_at] // blocks).reshape((-1,) + (1,) * (len(shape) - axis_at - 1))

    factor_of = one(*cuts[0])
    for cut in cuts[1:]:
        factor_of = factor_of * one(*cut)
    return factor_of


def profile(amount, total, limit, lean):
    weights = [(1 << 20) // math.isqrt(rank ** lean) + 1 for rank in range(2, amount + 1)]
    spare, holding = total - limit - (amount - 1), [1] * (amount - 1)
    while spare > 0:
        free = [i for i in range(amount - 1) if holding[i] < limit]
        pool, budget = sum([weights[i] for i in free]), spare
        for i in free:
            addition = min(limit - holding[i], max(1, budget * weights[i] // pool), spare)
            holding[i] = holding[i] + addition
            spare = spare - addition
    return np.array([limit] + holding)


def ragged(own_key, amount, total, reach, lean):
    if amount == 2:
        one = jax.random.randint(own_key, (), max(1, total - reach), min(reach, total - 1) + 1)
        return jnp.stack([one, total - one])
    sizes = jnp.asarray(profile(amount, total, reach, lean), jnp.int32)
    pairs = (amount - 1) // 2
    donor, sink = sizes[1:1 + 2 * pairs:2], sizes[2:2 + 2 * pairs:2]
    room = jnp.minimum(donor - 1, reach - sink)
    moved = jax.random.randint(jax.random.fold_in(own_key, 1), (pairs,), 0, 1 << 20) % (room + 1)
    sizes = sizes.at[1:1 + 2 * pairs:2].set(donor - moved).at[2:2 + 2 * pairs:2].set(sink + moved)
    return sizes[jax.random.permutation(jax.random.fold_in(own_key, 2), amount)]


def shared_out(key, own, number, rows, amount, top, bound, lean):
    sequence = jax.random.permutation(key, amount)
    packed, usual = portions_of(amount, rows * top, bound, lean, True), portions_of(amount, rows * top, bound, lean, False)
    places = jnp.arange(amount)

    def named(sizes, offset_by):
        used = int((sizes > 0).sum())
        fixed = max(1, used // 4)
        moved = fixed + (places - fixed + offset_by * (used - fixed)) % max(1, amount - fixed)
        return jnp.zeros((amount,), jnp.int32).at[sequence[jnp.where(places < fixed, places, moved)]].set(jnp.asarray(sizes, jnp.int32))

    sizes = jnp.where(number % 4 == 0, named(packed, number // 4), named(usual, number - number // 4 - 1))
    mixed = jax.random.permutation(jax.random.fold_in(own, 3), amount)
    source_of, taker = mixed[0:amount // 2 * 2:2], mixed[1:amount // 2 * 2:2]
    slack = jnp.minimum(sizes[source_of] - 1, bound - sizes[taker]) // 2
    slack = jnp.where((source_of == sequence[0]) | (taker == sequence[0]) | (sizes[taker] == 0), 0, jnp.maximum(slack, 0))
    moved = jax.random.randint(jax.random.fold_in(own, 4), (amount // 2,), 0, 1 << 20) % (slack + 1)
    sizes = sizes.at[source_of].add(-moved).at[taker].add(moved)
    members = jnp.searchsorted(jnp.cumsum(sizes), jnp.arange(rows * top), side="right").astype(jnp.int32)
    table = members.reshape(top, rows).T
    table = table[jax.random.permutation(jax.random.fold_in(own, 1), rows)]
    offset_by = jax.random.randint(jax.random.fold_in(own, 2), (rows, 1), 0, top)
    return jnp.take_along_axis(table, (jnp.arange(top)[None, :] + offset_by) % top, axis=1)


def portions_of(number_of, total, limit, slope, full):
    portions = [(1 << 20) // math.isqrt(rank ** slope) + 1 for rank in range(1, number_of + 1)]
    largest = limit if full else min(limit, max(-(-total // number_of), total * portions[0] // sum(portions)))
    least = 1 if total - largest >= number_of - 1 else 0
    counts, surplus = [largest] + [least] * (number_of - 1), total - largest - least * (number_of - 1)
    while surplus > 0:
        free = [i for i in range(1, number_of) if counts[i] < largest] or [i for i in range(1, number_of) if counts[i] < limit]
        whole, budget = sum([portions[i] for i in free]), surplus
        for i in free:
            more = min(limit - counts[i], max(1, budget * portions[i] // whole), surplus)
            counts[i] = counts[i] + more
            surplus = surplus - more
    return np.array(counts)


def gaussian(own_key, shape, spread, bound, cuts=(), held_as=jnp.bfloat16):
    entries = jax.random.normal(own_key, shape, jnp.float32) * spread
    if len(cuts) > 0:
        entries = block_scale(own_key, shape, cuts, -0.22, 0.18) * entries
    return jnp.clip(entries, min=-bound, max=bound).astype(held_as)


def setup_inputs(seed: int = 0, part: int = 0) -> dict:
    arg_keys = jax.random.split(jax.random.key(seed), 17)
    part_keys = jax.random.split(jax.random.fold_in(arg_keys[16], part), 17)
    pair_raw = gaussian(part_keys[0], (SLAB_TOKENS, 2, HK * DK), 1.0, 6.0, ((0, 16), (2, 2)))
    value_raw = gaussian(part_keys[1], (SLAB_TOKENS, VALUE_HEADS * DV), 1.0, 6.0, ((0, 16), (1, 2)))
    gate_raw = gaussian(part_keys[2], (SLAB_TOKENS, VALUE_HEADS * DV), 1.0, 6.0, ((0, 16), (1, 2)))
    write_strength = jnp.clip(0.05 + 0.9 * jax.random.uniform(part_keys[3], (SLAB_TOKENS, VALUE_HEADS), jnp.float32) ** block_scale(part_keys[3], (SLAB_TOKENS, VALUE_HEADS), ((0, 16), (1, 2)), -0.2, 0.2), 0.05, 0.95)
    log_decay = draw_log_decay(jax.random.fold_in(jax.random.fold_in(arg_keys[16], part), 71), part)
    segment_ids = jnp.searchsorted(jnp.cumsum(ragged(part_keys[5], SEGS, SLAB_TOKENS, SEG_MOST, 1)), jnp.arange(SLAB_TOKENS), side="right").astype(jnp.int32)
    pair_filter = gaussian(arg_keys[6], (KW, 2, HK * DK), KW ** -0.5, 3.0, ((2, 2),), jnp.float32)
    value_filter = gaussian(arg_keys[7], (KW, VALUE_HEADS * DV), KW ** -0.5, 3.0, ((1, 2),), jnp.float32)
    norm_gain = jnp.clip(1.0 + 0.18 * jax.random.normal(arg_keys[8], (DV,), jnp.float32), 0.1, 1.9)
    out_weight = gaussian(arg_keys[9], (VALUE_HEADS * DV, D), (VALUE_HEADS * DV) ** -0.5, 0.125, ((0, 2),))
    residual = draw_residual(jax.random.fold_in(jax.random.fold_in(arg_keys[16], part), 71), part)
    post_gain = jnp.clip(1.0 + 0.18 * jax.random.normal(arg_keys[11], (D,), jnp.float32), 0.1, 1.9)
    routes_keys = jax.random.split(jax.random.fold_in(part_keys[12], 1), SLAB_TOKENS // TOK_DEV)
    routes_turns = jax.random.permutation(jax.random.fold_in(part_keys[12], 3), SLAB_TOKENS // TOK_DEV)
    routes = jax.vmap(lambda own, number: shared_out(jax.random.fold_in(part_keys[12], 2), own, number, TOK_DEV, EXPERTS, TOPK, CAP, 2))(routes_keys, routes_turns).reshape((SLAB_TOKENS, TOPK))
    route_weights = jnp.clip(0.05 + 0.25 * jax.random.uniform(part_keys[13], (SLAB_TOKENS, TOPK), jnp.float32) ** block_scale(part_keys[13], (SLAB_TOKENS, TOPK), ((0, 32),), -0.2, 0.2), 0.05, 0.3)
    expert_up = gaussian(arg_keys[14], (EXPERTS, D, 2 * FFE), D ** -0.5, 0.125, ((0, 32),))
    expert_down = gaussian(arg_keys[15], (EXPERTS, FFE, D), FFE ** -0.5, 0.25, ((0, 32),))
    return dict(pair_raw=pair_raw, value_raw=value_raw, gate_raw=gate_raw, write_strength=write_strength, log_decay=log_decay, segment_ids=segment_ids, pair_filter=pair_filter, value_filter=value_filter, norm_gain=norm_gain, out_weight=out_weight, residual=residual, post_gain=post_gain, routes=routes, route_weights=route_weights, expert_up=expert_up, expert_down=expert_down)


HIGHEST = lax.Precision.HIGHEST

def precise_dot(left, right):
    return jnp.dot(left.astype(jnp.float32), right.astype(jnp.float32), precision=HIGHEST, preferred_element_type=jnp.float32)

def causal_filter(padded_raw, filter_taps, padded_ids, kernel):
    length = padded_raw.shape[0] - (kernel - 1)
    source = padded_raw.astype(jnp.float32)
    current_ids = padded_ids[kernel - 1:]
    summed = jnp.zeros((length, padded_raw.shape[1]), jnp.float32)
    for lag_step in range(kernel):
        offset_start = kernel - 1 - lag_step
        shifted = source[offset_start:offset_start + length]
        matching = (padded_ids[offset_start:offset_start + length] == current_ids).astype(jnp.float32)
        summed = summed + filter_taps[lag_step] * shifted * matching[:, None]
    return jax.nn.silu(summed)

def unit_rows(values_in):
    return values_in / jnp.sqrt(lax.optimization_barrier(jnp.sum(values_in * values_in, axis=-1, keepdims=True)) + 1e-06)

def mixer_inputs(pair_padded, value_padded, pair_filter, value_filter, padded_ids, kernel):
    pair_act = causal_filter(pair_padded, pair_filter.reshape(kernel, -1), padded_ids, kernel)
    length = pair_act.shape[0]
    pair_heads = pair_act.reshape(length, 2, -1, DK)
    queries = unit_rows(pair_heads[:, 0]) * DK ** (-0.5)
    key_rows = unit_rows(pair_heads[:, 1])
    value_rows = causal_filter(value_padded, value_filter, padded_ids, kernel).reshape(length, -1, DV)
    repeat_factor = value_rows.shape[1] // key_rows.shape[1]
    return (jnp.repeat(queries, repeat_factor, axis=1), jnp.repeat(key_rows, repeat_factor, axis=1), value_rows)

def block_setup(queries, key_rows, value_rows, strength, decay_rows, segment_here, prior_id):
    cumulative = jnp.cumsum(decay_rows)
    row_index = lax.broadcasted_iota(jnp.int32, (BLOCK, BLOCK), 0)
    col_index = lax.broadcasted_iota(jnp.int32, (BLOCK, BLOCK), 1)
    same_segment = segment_here[:, None] == segment_here[None, :]
    causal = (row_index >= col_index) & same_segment
    strictly = (row_index > col_index) & same_segment
    decay_matrix = jnp.where(causal, jnp.exp(jnp.where(causal, cumulative[:, None] - cumulative[None, :], 0.0)), 0.0)
    carried_in = (segment_here == prior_id).astype(jnp.float32)
    keyed_beta = key_rows * strength[:, None]
    coupling = jnp.where(strictly, precise_dot(keyed_beta, key_rows.T) * decay_matrix, 0.0)
    system = jnp.eye(BLOCK, dtype=jnp.float32) + coupling
    stacked = jnp.concatenate([value_rows * strength[:, None], keyed_beta * (jnp.exp(cumulative) * carried_in)[:, None]], axis=1)
    solved = lax.linalg.triangular_solve(system, stacked, left_side=True, lower=True, unit_diagonal=True)
    targets = solved[:, :DV]
    corrector = solved[:, DV:]
    within = jnp.where(causal, precise_dot(queries, key_rows.T) * decay_matrix, 0.0)
    query_decayed = queries * (jnp.exp(cumulative) * carried_in)[:, None]
    final_log = cumulative[BLOCK - 1]
    weighting = (segment_here == segment_here[BLOCK - 1]).astype(jnp.float32) * jnp.exp(final_log - cumulative)
    keys_weighted = key_rows * weighting[:, None]
    transition = jnp.exp(final_log) * carried_in[BLOCK - 1] * jnp.eye(DK, dtype=jnp.float32) - precise_dot(keys_weighted.T, corrector)
    increment = precise_dot(keys_weighted.T, targets)
    return (within, query_decayed, targets, corrector, transition, increment)

def head_major(array_in, block_count):
    moved = jnp.moveaxis(array_in, 1, 0)
    return moved.reshape((array_in.shape[1], block_count, BLOCK) + array_in.shape[2:])

def block_tables(queries, key_rows, value_rows, strength, decay_rows, padded_ids, kernel):
    length = queries.shape[0]
    block_count = length // BLOCK
    current_ids = padded_ids[kernel - 1:].reshape(block_count, BLOCK)
    prior_ids = padded_ids[kernel - 2:kernel - 2 + length:BLOCK]
    per_block = jax.vmap(block_setup, in_axes=(0, 0, 0, 0, 0, 0, 0))
    per_head = jax.vmap(per_block, in_axes=(0, 0, 0, 0, 0, None, None))
    return per_head(head_major(queries, block_count), head_major(key_rows, block_count), head_major(value_rows, block_count), head_major(strength, block_count), head_major(decay_rows, block_count), current_ids, prior_ids)

def batched(left, right):
    return jnp.einsum('hij,hjk->hik', left, right, precision=HIGHEST)

def sweep_blocks(block_terms, start_state):
    blocks_first = tuple((jnp.swapaxes(member, 0, 1) for member in block_terms))

    def advance(carry_state, pieces):
        within, query_decayed, targets, corrector, transition, increment = pieces
        fresh_values = targets - batched(corrector, carry_state)
        emitted = batched(query_decayed, carry_state) + batched(within, fresh_values)
        updated = batched(transition, carry_state) + increment
        return (updated, emitted)
    final_state, emitted = lax.scan(advance, start_state, blocks_first)
    return emitted

def tokens_first(emitted):
    heads_count = emitted.shape[1]
    return jnp.transpose(emitted, (0, 2, 1, 3)).reshape(-1, heads_count, emitted.shape[3])

def gate_output(mixed_heads, gate_raw, norm_gain):
    square_mean = lax.optimization_barrier(jnp.mean(mixed_heads * mixed_heads, axis=-1, keepdims=True))
    gate_values = jax.nn.silu(gate_raw.reshape(mixed_heads.shape).astype(jnp.float32))
    normed = mixed_heads / jnp.sqrt(square_mean + 1e-06) * norm_gain * gate_values
    return normed.astype(jnp.bfloat16).reshape(mixed_heads.shape[0], -1)

def post_norm(hidden, post_gain):
    hidden_full = hidden.astype(jnp.float32)
    square_mean = lax.optimization_barrier(jnp.mean(hidden_full * hidden_full, axis=-1, keepdims=True))
    return (hidden_full / jnp.sqrt(square_mean + 1e-06) * post_gain).astype(jnp.bfloat16)

def expert_apply_rows(rows_in, up_matrix, down_matrix):
    hidden_units = down_matrix.shape[0]
    gate_up = jnp.dot(rows_in.astype(jnp.float32), up_matrix.astype(jnp.float32), preferred_element_type=jnp.float32)
    activated = (jax.nn.silu(gate_up[:, :hidden_units]) * gate_up[:, hidden_units:]).astype(jnp.bfloat16)
    return jnp.dot(activated.astype(jnp.float32), down_matrix.astype(jnp.float32), preferred_element_type=jnp.float32).astype(jnp.bfloat16)

def reference(pair_raw, value_raw, gate_raw, write_strength, log_decay, segment_ids, pair_filter, value_filter, norm_gain, out_weight, residual, post_gain, routes, route_weights, expert_up, expert_down):
    kernel = value_filter.shape[0]
    padded_ids = jnp.concatenate([jnp.full((kernel - 1,), -1, jnp.int32), segment_ids.astype(jnp.int32)])
    pair_flat = pair_raw.reshape(SLAB_TOKENS, -1)
    pair_padded = jnp.concatenate([jnp.zeros((kernel - 1, pair_flat.shape[1]), jnp.bfloat16), pair_flat])
    value_padded = jnp.concatenate([jnp.zeros((kernel - 1, value_raw.shape[1]), jnp.bfloat16), value_raw])
    queries, key_rows, value_rows = mixer_inputs(pair_padded, value_padded, pair_filter, value_filter, padded_ids, kernel)
    block_terms = block_tables(queries, key_rows, value_rows, write_strength, log_decay, padded_ids, kernel)
    start_state = jnp.zeros((VALUE_HEADS, DK, DV), jnp.float32)
    emitted = sweep_blocks(block_terms, start_state)
    gated_out = gate_output(tokens_first(emitted), gate_raw, norm_gain)
    attention = jnp.dot(gated_out.astype(jnp.float32), out_weight.astype(jnp.float32), preferred_element_type=jnp.float32)
    hidden = (residual.astype(jnp.float32) + attention).astype(jnp.bfloat16)
    expert_in = post_norm(hidden, post_gain)
    blocks = N_CTX * N_HEAD
    rows_each = SLAB_TOKENS // blocks
    assigned = routes.reshape(blocks, rows_each * TOPK)
    expert_ids = jnp.arange(EXPERTS, dtype=jnp.int32)
    onehot = (assigned[:, :, None] == expert_ids[None, None, :]).astype(jnp.int32)
    slot_rank = lax.optimization_barrier(jnp.sum((jnp.cumsum(onehot, axis=1) - 1) * onehot, axis=2))
    source_ids = jnp.arange(blocks, dtype=jnp.int32)[:, None]
    slot_index = assigned * (blocks * CAP) + source_ids * CAP + slot_rank
    owners = jnp.arange(blocks * rows_each * TOPK, dtype=jnp.int32) // TOPK + 1
    owner_table = jnp.zeros((EXPERTS * blocks * CAP,), jnp.int32).at[slot_index.reshape(-1)].set(owners)

    def one_expert(operands):
        table_row, up_matrix, down_matrix = operands
        picked = jnp.where((table_row > 0)[:, None], expert_in[jnp.maximum(table_row - 1, 0)], jnp.zeros((), jnp.bfloat16))
        return expert_apply_rows(picked, up_matrix, down_matrix)
    results = lax.map(one_expert, (owner_table.reshape(EXPERTS, blocks * CAP), expert_up, expert_down)).reshape(-1, D)
    chosen_slots = slot_index.reshape(SLAB_TOKENS, TOPK)
    combined = hidden.astype(jnp.float32)
    for column in range(TOPK):
        combined = combined + route_weights[:, column:column + 1] * results[chosen_slots[:, column]].astype(jnp.float32)
    return combined.astype(jnp.bfloat16)
```

```python
import jax
import jax.numpy as jnp
from jax import lax
from jax.sharding import PartitionSpec as P

D = 2048
DK = 128
DV = 128
BLOCK = 64


HIGHEST = lax.Precision.HIGHEST


def passed_along(block, axis, distance):
    devices = range(lax.axis_size(axis))
    route = [(i - distance, i) for i in devices if i - distance in devices]
    return lax.ppermute(block, axis, route)


def scanned_entry(whole_map, whole_shift, axis):
    peers, position = (lax.axis_size(axis), lax.axis_index(axis))
    distance = 1
    while distance < peers:
        last = 2 * distance >= peers
        shift_in = passed_along(whole_shift.astype(jnp.bfloat16), axis, distance).astype(jnp.float32)
        reached = position >= distance
        new_shift = batched(whole_map, shift_in) + whole_shift
        if not last:
            map_in = passed_along(whole_map.astype(jnp.bfloat16), axis, distance).astype(jnp.float32)
            whole_map = jnp.where(reached, batched(whole_map, map_in), whole_map)
        whole_shift = jnp.where(reached, new_shift, whole_shift)
        distance *= 2
    return passed_along(whole_shift.astype(jnp.bfloat16), axis, 1).astype(jnp.float32)


def precise_dot(left, right):
    return jnp.dot(left, right, precision=HIGHEST, preferred_element_type=jnp.float32)


def causal_filter(padded_raw, filter_taps, padded_ids, kernel):
    length = padded_raw.shape[0] - (kernel - 1)
    source = padded_raw.astype(jnp.float32)
    current_ids = padded_ids[kernel - 1 :]
    summed = jnp.zeros((length, padded_raw.shape[1]), jnp.float32)
    for lag_step in range(kernel):
        offset_start = kernel - 1 - lag_step
        shifted = source[offset_start : offset_start + length]
        matching = (padded_ids[offset_start : offset_start + length] == current_ids).astype(
            jnp.float32
        )
        summed = summed + filter_taps[lag_step] * shifted * matching[:, None]
    return jax.nn.silu(summed)


def unit_rows(values_in):
    return values_in / jnp.sqrt(jnp.sum(values_in * values_in, axis=-1, keepdims=True) + 1e-06)


def mixer_inputs(pair_padded, value_padded, pair_filter, value_filter, padded_ids, kernel):
    pair_act = causal_filter(pair_padded, pair_filter.reshape(kernel, -1), padded_ids, kernel)
    length = pair_act.shape[0]
    pair_heads = pair_act.reshape(length, 2, -1, DK)
    queries = unit_rows(pair_heads[:, 0]) * DK ** (-0.5)
    key_rows = unit_rows(pair_heads[:, 1])
    value_rows = causal_filter(value_padded, value_filter, padded_ids, kernel).reshape(
        length, -1, DV
    )
    repeat_factor = value_rows.shape[1] // key_rows.shape[1]
    return (
        jnp.repeat(queries, repeat_factor, axis=1),
        jnp.repeat(key_rows, repeat_factor, axis=1),
        value_rows,
    )


def unit_lower_inverse(system):
    size = system.shape[-1]
    lead = system.shape[:-2]
    blocks = jnp.ones(lead + (size, 1, 1), system.dtype)
    width = 1
    while width < size:
        count = size // (2 * width)
        grid = system.reshape(lead + (count, 2 * width, count, 2 * width))
        diagonal = jnp.moveaxis(jnp.diagonal(grid, axis1=-4, axis2=-2), -1, -3)
        lower_left = diagonal[..., width:, :width]
        upper = blocks[..., 0::2, :, :]
        lower = blocks[..., 1::2, :, :]
        linked = -jnp.einsum(
            "...jab,...jbc->...jac",
            lower,
            jnp.einsum("...jab,...jbc->...jac", lower_left, upper, precision=HIGHEST),
            precision=HIGHEST,
        )
        top = jnp.concatenate([upper, jnp.zeros_like(upper)], axis=-1)
        bottom = jnp.concatenate([linked, lower], axis=-1)
        blocks = jnp.concatenate([top, bottom], axis=-2)
        width *= 2
    return blocks.reshape(lead + (size, size))


def block_setup(queries, key_rows, value_rows, strength, decay_rows, segment_here, prior_id):
    cumulative = jnp.cumsum(decay_rows)
    row_index = lax.broadcasted_iota(jnp.int32, (BLOCK, BLOCK), 0)
    col_index = lax.broadcasted_iota(jnp.int32, (BLOCK, BLOCK), 1)
    same_segment = segment_here[:, None] == segment_here[None, :]
    causal = (row_index >= col_index) & same_segment
    strictly = (row_index > col_index) & same_segment
    decay_matrix = jnp.where(
        causal, jnp.exp(jnp.where(causal, cumulative[:, None] - cumulative[None, :], 0.0)), 0.0
    )
    carried_in = (segment_here == prior_id).astype(jnp.float32)
    keyed_beta = key_rows * strength[:, None]
    coupling = jnp.where(strictly, precise_dot(keyed_beta, key_rows.T) * decay_matrix, 0.0)
    system = jnp.eye(BLOCK, dtype=jnp.float32) + coupling
    stacked = jnp.concatenate(
        [value_rows * strength[:, None], keyed_beta * (jnp.exp(cumulative) * carried_in)[:, None]],
        axis=1,
    )
    solved = precise_dot(unit_lower_inverse(system), stacked)
    targets = solved[:, :DV]
    corrector = solved[:, DV:]
    within = jnp.where(causal, precise_dot(queries, key_rows.T) * decay_matrix, 0.0)
    query_decayed = queries * (jnp.exp(cumulative) * carried_in)[:, None]
    final_log = cumulative[BLOCK - 1]
    weighting = (segment_here == segment_here[BLOCK - 1]).astype(jnp.float32) * jnp.exp(
        final_log - cumulative
    )
    keys_weighted = key_rows * weighting[:, None]
    transition = jnp.exp(final_log) * carried_in[BLOCK - 1] * jnp.eye(
        DK, dtype=jnp.float32
    ) - precise_dot(keys_weighted.T, corrector)
    increment = precise_dot(keys_weighted.T, targets)
    return (within, query_decayed, targets, corrector, transition, increment)


def head_major(array_in, block_count):
    moved = jnp.moveaxis(array_in, 1, 0)
    return moved.reshape((array_in.shape[1], block_count, BLOCK) + array_in.shape[2:])


def block_tables(queries, key_rows, value_rows, strength, decay_rows, padded_ids, kernel):
    length = queries.shape[0]
    block_count = length // BLOCK
    current_ids = padded_ids[kernel - 1 :].reshape(block_count, BLOCK)
    prior_ids = padded_ids[kernel - 2 : kernel - 2 + length : BLOCK]
    per_block = jax.vmap(block_setup, in_axes=(0, 0, 0, 0, 0, 0, 0))
    per_head = jax.vmap(per_block, in_axes=(0, 0, 0, 0, 0, None, None))
    return per_head(
        head_major(queries, block_count),
        head_major(key_rows, block_count),
        head_major(value_rows, block_count),
        head_major(strength, block_count),
        head_major(decay_rows, block_count),
        current_ids,
        prior_ids,
    )


def batched(left, right):
    return jnp.einsum("hij,hjk->hik", left, right, precision=HIGHEST)


def sweep_blocks(block_terms, start_state):
    blocks_first = tuple((jnp.swapaxes(member, 0, 1) for member in block_terms))

    def advance(carry_state, pieces):
        within, query_decayed, targets, corrector, transition, increment = pieces
        fresh_values = targets - batched(corrector, carry_state)
        emitted = batched(query_decayed, carry_state) + batched(within, fresh_values)
        updated = batched(transition, carry_state) + increment
        return (updated, emitted)

    final_state, emitted = lax.scan(advance, start_state, blocks_first)
    return emitted


def tokens_first(emitted):
    heads_count = emitted.shape[1]
    return jnp.transpose(emitted, (0, 2, 1, 3)).reshape(-1, heads_count, emitted.shape[3])


def gate_output(mixed_heads, gate_raw, norm_gain):
    square_mean = jnp.mean(mixed_heads * mixed_heads, axis=-1, keepdims=True)
    gate_values = jax.nn.silu(gate_raw.reshape(mixed_heads.shape).astype(jnp.float32))
    normed = mixed_heads / jnp.sqrt(square_mean + 1e-06) * norm_gain * gate_values
    return normed.astype(jnp.bfloat16).reshape(mixed_heads.shape[0], -1)


def post_norm(hidden, post_gain):
    hidden_full = hidden.astype(jnp.float32)
    square_mean = jnp.mean(hidden_full * hidden_full, axis=-1, keepdims=True)
    return (hidden_full / jnp.sqrt(square_mean + 1e-06) * post_gain).astype(jnp.bfloat16)


def expert_apply_rows(rows_in, up_matrix, down_matrix):
    hidden_units = down_matrix.shape[0]
    gate_up = jnp.dot(rows_in, up_matrix, preferred_element_type=jnp.float32)
    activated = (jax.nn.silu(gate_up[:, :hidden_units]) * gate_up[:, hidden_units:]).astype(
        jnp.bfloat16
    )
    return jnp.dot(activated, down_matrix, preferred_element_type=jnp.float32).astype(jnp.bfloat16)


def expert_apply(arrived, expert_up, expert_down):
    member_rows = arrived[:, 0]
    flattened = member_rows.reshape(-1, member_rows.shape[-1])
    result = expert_apply_rows(flattened, expert_up[0], expert_down[0])
    outputs = [result.reshape(member_rows.shape)]
    return jnp.stack(outputs, axis=1)


def route_slots(routes, experts_all, capacity):
    assigned = routes.reshape(-1)
    expert_ids = jnp.arange(experts_all, dtype=jnp.int32)
    onehot = (assigned[:, None] == expert_ids[None, :]).astype(jnp.int32)
    slot_rank = jnp.sum((jnp.cumsum(onehot, axis=0) - 1) * onehot, axis=1)
    return assigned * capacity + slot_rank


def per_device(
    pair_raw,
    value_raw,
    gate_raw,
    write_strength,
    log_decay,
    segment_ids,
    pair_filter,
    value_filter,
    norm_gain,
    out_weight,
    residual,
    post_gain,
    routes,
    route_weights,
    expert_up,
    expert_down,
):
    local_tokens = pair_raw.shape[0]
    kernel = value_filter.shape[0]
    pair_flat = pair_raw.reshape(local_tokens, -1)
    pair_width = pair_flat.shape[1]
    rim_rows = jnp.concatenate(
        [pair_flat[local_tokens - (kernel - 1) :], value_raw[local_tokens - (kernel - 1) :]], axis=1
    )
    before = passed_along(rim_rows, "ctx", 1)
    first_token = lax.axis_index("ctx") * local_tokens
    padded_ids = jnp.concatenate([jnp.full((kernel - 1,), -1, jnp.int32), segment_ids])
    window_ids = lax.dynamic_slice_in_dim(padded_ids, first_token, local_tokens + kernel - 1)
    pair_padded = jnp.concatenate([before[:, :pair_width], pair_flat])
    value_padded = jnp.concatenate([before[:, pair_width:], value_raw])
    queries, key_rows, value_rows = mixer_inputs(
        pair_padded, value_padded, pair_filter, value_filter, window_ids, kernel
    )
    block_terms = block_tables(
        queries, key_rows, value_rows, write_strength, log_decay, window_ids, kernel
    )
    heads_here = value_rows.shape[1]
    identity_maps = jnp.broadcast_to(jnp.eye(DK, dtype=jnp.float32), (heads_here, DK, DK))
    empty_state = jnp.zeros((heads_here, DK, DV), jnp.float32)

    def fold_block(totals, pieces):
        transition, increment = pieces
        return ((batched(transition, totals[0]), batched(transition, totals[1]) + increment), None)

    whole_pair, unused = lax.scan(
        fold_block,
        (identity_maps, empty_state),
        (jnp.swapaxes(block_terms[4], 0, 1), jnp.swapaxes(block_terms[5], 0, 1)),
    )
    whole_map, whole_shift = whole_pair

    entering = scanned_entry(whole_map, whole_shift, "ctx")
    emitted = sweep_blocks(block_terms, entering)
    gated_out = gate_output(tokens_first(emitted), gate_raw, norm_gain)
    attention = lax.psum_scatter(
        jnp.dot(gated_out, out_weight, preferred_element_type=jnp.float32).astype(jnp.bfloat16),
        "head",
        scatter_dimension=0,
        tiled=True,
    ).astype(jnp.float32)
    hidden = (residual.astype(jnp.float32) + attention).astype(jnp.bfloat16)
    expert_in = post_norm(hidden, post_gain)
    devices_all = lax.axis_size("ctx") * lax.axis_size("head")
    local_experts = expert_up.shape[0]
    experts_all = devices_all * local_experts
    local_rows = routes.shape[0]
    top_count = routes.shape[1]
    capacity = local_rows * top_count * 5 // (4 * experts_all)
    slot_index = route_slots(routes, experts_all, capacity)
    chosen_slots = slot_index.reshape(local_rows, top_count)
    slot_ids = jnp.arange(experts_all * capacity, dtype=jnp.int32)
    hits = chosen_slots[:, :, None] == slot_ids[None, None, :]
    picker = jnp.any(hits, axis=1).astype(jnp.bfloat16)
    outgoing = lax.dot_general(
        picker, expert_in, (((0,), (0,)), ((), ())), preferred_element_type=jnp.float32
    ).astype(jnp.bfloat16)
    outgoing = outgoing.reshape(devices_all, local_experts, capacity, D)
    answered = expert_apply(
        lax.all_to_all(outgoing, ("ctx", "head"), split_axis=0, concat_axis=0, tiled=True),
        expert_up,
        expert_down,
    )
    returned = lax.all_to_all(answered, ("ctx", "head"), split_axis=0, concat_axis=0, tiled=True)
    result_rows = returned.reshape(-1, D)
    weight_table = jnp.sum(jnp.where(hits, route_weights[:, :, None], 0.0), axis=1)
    weight_high = weight_table.astype(jnp.bfloat16)
    weight_low = (weight_table - weight_high.astype(jnp.float32)).astype(jnp.bfloat16)
    routed = jnp.dot(weight_high, result_rows, preferred_element_type=jnp.float32) + jnp.dot(
        weight_low, result_rows, preferred_element_type=jnp.float32
    )
    combined = hidden.astype(jnp.float32) + routed
    return combined.astype(jnp.bfloat16)


def solution(mesh):
    return jax.shard_map(
        per_device,
        mesh=mesh,
        in_specs=(
            P(("group", "ctx"), None, "head"),
            P(("group", "ctx"), "head"),
            P(("group", "ctx"), "head"),
            P(("group", "ctx"), "head"),
            P(("group", "ctx"), "head"),
            P("group"),
            P(None, None, "head"),
            P(None, "head"),
            P(),
            P("head", None),
            P(("group", "ctx", "head"), None),
            P(),
            P(("group", "ctx", "head"), None),
            P(("group", "ctx", "head"), None),
            P(("ctx", "head"), None, None),
            P(("ctx", "head"), None, None),
        ),
        out_specs=P(("group", "ctx", "head"), None),
        check_vma=False,
    )
```

```python
import jax
import jax.numpy as jnp
from jax import lax
from jax.sharding import Mesh, PartitionSpec as P

D = 2048
DK = 128
DV = 128
BLOCK = 64
CTX = ("ctx_hi", "ctx_lo")


HIGHEST = lax.Precision.HIGHEST


def passed_along(block, axis, distance):
    devices = range(lax.axis_size(axis))
    route = [(i - distance, i) for i in devices if i - distance in devices]
    return lax.ppermute(block, axis, route)


def scanned_entry(whole_map, whole_shift, axis):
    peers, position = (lax.axis_size(axis), lax.axis_index(axis))
    distance = 1
    while distance < peers:
        last = 2 * distance >= peers
        shift_in = passed_along(whole_shift.astype(jnp.bfloat16), axis, distance).astype(jnp.float32)
        reached = position >= distance
        new_shift = batched(whole_map, shift_in) + whole_shift
        if not last:
            map_in = passed_along(whole_map.astype(jnp.bfloat16), axis, distance).astype(jnp.float32)
            whole_map = jnp.where(reached, batched(whole_map, map_in), whole_map)
        whole_shift = jnp.where(reached, new_shift, whole_shift)
        distance *= 2
    return passed_along(whole_shift.astype(jnp.bfloat16), axis, 1).astype(jnp.float32)


def precise_dot(left, right):
    return jnp.dot(left, right, precision=HIGHEST, preferred_element_type=jnp.float32)


def causal_filter(padded_raw, filter_taps, padded_ids, kernel):
    length = padded_raw.shape[0] - (kernel - 1)
    source = padded_raw.astype(jnp.float32)
    current_ids = padded_ids[kernel - 1 :]
    summed = jnp.zeros((length, padded_raw.shape[1]), jnp.float32)
    for lag_step in range(kernel):
        offset_start = kernel - 1 - lag_step
        shifted = source[offset_start : offset_start + length]
        matching = (padded_ids[offset_start : offset_start + length] == current_ids).astype(
            jnp.float32
        )
        summed = summed + filter_taps[lag_step] * shifted * matching[:, None]
    return jax.nn.silu(summed)


def unit_rows(values_in):
    return values_in / jnp.sqrt(jnp.sum(values_in * values_in, axis=-1, keepdims=True) + 1e-06)


def mixer_inputs(pair_padded, value_padded, pair_filter, value_filter, padded_ids, kernel):
    pair_act = causal_filter(pair_padded, pair_filter.reshape(kernel, -1), padded_ids, kernel)
    length = pair_act.shape[0]
    pair_heads = pair_act.reshape(length, 2, -1, DK)
    queries = unit_rows(pair_heads[:, 0]) * DK ** (-0.5)
    key_rows = unit_rows(pair_heads[:, 1])
    value_rows = causal_filter(value_padded, value_filter, padded_ids, kernel).reshape(
        length, -1, DV
    )
    repeat_factor = value_rows.shape[1] // key_rows.shape[1]
    return (
        jnp.repeat(queries, repeat_factor, axis=1),
        jnp.repeat(key_rows, repeat_factor, axis=1),
        value_rows,
    )


def unit_lower_inverse(system):
    size = system.shape[-1]
    lead = system.shape[:-2]
    blocks = jnp.ones(lead + (size, 1, 1), system.dtype)
    width = 1
    while width < size:
        count = size // (2 * width)
        grid = system.reshape(lead + (count, 2 * width, count, 2 * width))
        diagonal = jnp.moveaxis(jnp.diagonal(grid, axis1=-4, axis2=-2), -1, -3)
        lower_left = diagonal[..., width:, :width]
        upper = blocks[..., 0::2, :, :]
        lower = blocks[..., 1::2, :, :]
        linked = -jnp.einsum(
            "...jab,...jbc->...jac",
            lower,
            jnp.einsum("...jab,...jbc->...jac", lower_left, upper, precision=HIGHEST),
            precision=HIGHEST,
        )
        top = jnp.concatenate([upper, jnp.zeros_like(upper)], axis=-1)
        bottom = jnp.concatenate([linked, lower], axis=-1)
        blocks = jnp.concatenate([top, bottom], axis=-2)
        width *= 2
    return blocks.reshape(lead + (size, size))


def block_setup(queries, key_rows, value_rows, strength, decay_rows, segment_here, prior_id):
    cumulative = jnp.cumsum(decay_rows)
    row_index = lax.broadcasted_iota(jnp.int32, (BLOCK, BLOCK), 0)
    col_index = lax.broadcasted_iota(jnp.int32, (BLOCK, BLOCK), 1)
    same_segment = segment_here[:, None] == segment_here[None, :]
    causal = (row_index >= col_index) & same_segment
    strictly = (row_index > col_index) & same_segment
    decay_matrix = jnp.where(
        causal, jnp.exp(jnp.where(causal, cumulative[:, None] - cumulative[None, :], 0.0)), 0.0
    )
    carried_in = (segment_here == prior_id).astype(jnp.float32)
    keyed_beta = key_rows * strength[:, None]
    coupling = jnp.where(strictly, precise_dot(keyed_beta, key_rows.T) * decay_matrix, 0.0)
    system = jnp.eye(BLOCK, dtype=jnp.float32) + coupling
    stacked = jnp.concatenate(
        [value_rows * strength[:, None], keyed_beta * (jnp.exp(cumulative) * carried_in)[:, None]],
        axis=1,
    )
    solved = precise_dot(unit_lower_inverse(system), stacked)
    targets = solved[:, :DV]
    corrector = solved[:, DV:]
    within = jnp.where(causal, precise_dot(queries, key_rows.T) * decay_matrix, 0.0)
    query_decayed = queries * (jnp.exp(cumulative) * carried_in)[:, None]
    final_log = cumulative[BLOCK - 1]
    weighting = (segment_here == segment_here[BLOCK - 1]).astype(jnp.float32) * jnp.exp(
        final_log - cumulative
    )
    keys_weighted = key_rows * weighting[:, None]
    transition = jnp.exp(final_log) * carried_in[BLOCK - 1] * jnp.eye(
        DK, dtype=jnp.float32
    ) - precise_dot(keys_weighted.T, corrector)
    increment = precise_dot(keys_weighted.T, targets)
    return (within, query_decayed, targets, corrector, transition, increment)


def head_major(array_in, block_count):
    moved = jnp.moveaxis(array_in, 1, 0)
    return moved.reshape((array_in.shape[1], block_count, BLOCK) + array_in.shape[2:])


def block_tables(queries, key_rows, value_rows, strength, decay_rows, padded_ids, kernel):
    length = queries.shape[0]
    block_count = length // BLOCK
    current_ids = padded_ids[kernel - 1 :].reshape(block_count, BLOCK)
    prior_ids = padded_ids[kernel - 2 : kernel - 2 + length : BLOCK]
    per_block = jax.vmap(block_setup, in_axes=(0, 0, 0, 0, 0, 0, 0))
    per_head = jax.vmap(per_block, in_axes=(0, 0, 0, 0, 0, None, None))
    return per_head(
        head_major(queries, block_count),
        head_major(key_rows, block_count),
        head_major(value_rows, block_count),
        head_major(strength, block_count),
        head_major(decay_rows, block_count),
        current_ids,
        prior_ids,
    )


def batched(left, right):
    return jnp.einsum("hij,hjk->hik", left, right, precision=HIGHEST)


def sweep_blocks(block_terms, start_state):
    blocks_first = tuple((jnp.swapaxes(member, 0, 1) for member in block_terms))

    def advance(carry_state, pieces):
        within, query_decayed, targets, corrector, transition, increment = pieces
        fresh_values = targets - batched(corrector, carry_state)
        emitted = batched(query_decayed, carry_state) + batched(within, fresh_values)
        updated = batched(transition, carry_state) + increment
        return (updated, emitted)

    final_state, emitted = lax.scan(advance, start_state, blocks_first)
    return emitted


def tokens_first(emitted):
    heads_count = emitted.shape[1]
    return jnp.transpose(emitted, (0, 2, 1, 3)).reshape(-1, heads_count, emitted.shape[3])


def gate_output(mixed_heads, gate_raw, norm_gain):
    square_mean = jnp.mean(mixed_heads * mixed_heads, axis=-1, keepdims=True)
    gate_values = jax.nn.silu(gate_raw.reshape(mixed_heads.shape).astype(jnp.float32))
    normed = mixed_heads / jnp.sqrt(square_mean + 1e-06) * norm_gain * gate_values
    return normed.astype(jnp.bfloat16).reshape(mixed_heads.shape[0], -1)


def post_norm(hidden, post_gain):
    hidden_full = hidden.astype(jnp.float32)
    square_mean = jnp.mean(hidden_full * hidden_full, axis=-1, keepdims=True)
    return (hidden_full / jnp.sqrt(square_mean + 1e-06) * post_gain).astype(jnp.bfloat16)


def expert_apply_rows(rows_in, up_matrix, down_matrix):
    hidden_units = down_matrix.shape[0]
    gate_up = jnp.dot(rows_in, up_matrix, preferred_element_type=jnp.float32)
    activated = (jax.nn.silu(gate_up[:, :hidden_units]) * gate_up[:, hidden_units:]).astype(
        jnp.bfloat16
    )
    return jnp.dot(activated, down_matrix, preferred_element_type=jnp.float32).astype(jnp.bfloat16)


def expert_apply(arrived, expert_up, expert_down):
    member_rows = arrived[:, 0]
    flattened = member_rows.reshape(-1, member_rows.shape[-1])
    result = expert_apply_rows(flattened, expert_up[0], expert_down[0])
    outputs = [result.reshape(member_rows.shape)]
    return jnp.stack(outputs, axis=1)


def route_slots(routes, experts_all, capacity):
    assigned = routes.reshape(-1)
    expert_ids = jnp.arange(experts_all, dtype=jnp.int32)
    onehot = (assigned[:, None] == expert_ids[None, :]).astype(jnp.int32)
    slot_rank = jnp.sum((jnp.cumsum(onehot, axis=0) - 1) * onehot, axis=1)
    return assigned * capacity + slot_rank


def per_device(
    pair_raw,
    value_raw,
    gate_raw,
    write_strength,
    log_decay,
    segment_ids,
    pair_filter,
    value_filter,
    norm_gain,
    out_weight,
    residual,
    post_gain,
    routes,
    route_weights,
    expert_up,
    expert_down,
):
    local_tokens = pair_raw.shape[0]
    kernel = value_filter.shape[0]
    pair_flat = pair_raw.reshape(local_tokens, -1)
    pair_width = pair_flat.shape[1]
    rim_rows = jnp.concatenate(
        [pair_flat[local_tokens - (kernel - 1) :], value_raw[local_tokens - (kernel - 1) :]], axis=1
    )
    before = passed_along(rim_rows, CTX, 1)
    first_token = lax.axis_index(CTX) * local_tokens
    padded_ids = jnp.concatenate([jnp.full((kernel - 1,), -1, jnp.int32), segment_ids])
    window_ids = lax.dynamic_slice_in_dim(padded_ids, first_token, local_tokens + kernel - 1)
    pair_padded = jnp.concatenate([before[:, :pair_width], pair_flat])
    value_padded = jnp.concatenate([before[:, pair_width:], value_raw])
    queries, key_rows, value_rows = mixer_inputs(
        pair_padded, value_padded, pair_filter, value_filter, window_ids, kernel
    )
    block_terms = block_tables(
        queries, key_rows, value_rows, write_strength, log_decay, window_ids, kernel
    )
    heads_here = value_rows.shape[1]
    identity_maps = jnp.broadcast_to(jnp.eye(DK, dtype=jnp.float32), (heads_here, DK, DK))
    empty_state = jnp.zeros((heads_here, DK, DV), jnp.float32)

    def fold_block(totals, pieces):
        transition, increment = pieces
        return ((batched(transition, totals[0]), batched(transition, totals[1]) + increment), None)

    whole_pair, unused = lax.scan(
        fold_block,
        (identity_maps, empty_state),
        (jnp.swapaxes(block_terms[4], 0, 1), jnp.swapaxes(block_terms[5], 0, 1)),
    )
    whole_map, whole_shift = whole_pair

    entering = scanned_entry(whole_map, whole_shift, CTX)
    emitted = sweep_blocks(block_terms, entering)
    gated_out = gate_output(tokens_first(emitted), gate_raw, norm_gain)
    attention = lax.psum_scatter(
        jnp.dot(gated_out, out_weight, preferred_element_type=jnp.float32).astype(jnp.bfloat16),
        "head",
        scatter_dimension=0,
        tiled=True,
    ).astype(jnp.float32)
    hidden = (residual.astype(jnp.float32) + attention).astype(jnp.bfloat16)
    expert_in = post_norm(hidden, post_gain)
    levels = lax.axis_size("ctx_hi")
    level = lax.axis_index("ctx_hi")
    local_experts = expert_up.shape[0]
    per_level = lax.axis_size("ctx_lo") * lax.axis_size("head") * local_experts
    experts_all = levels * per_level
    local_rows = routes.shape[0]
    top_count = routes.shape[1]
    capacity = local_rows * top_count * 5 // (4 * experts_all)
    gathered_in = lax.all_gather(expert_in, "ctx_hi").reshape(levels * local_rows, D)
    gathered_routes = lax.all_gather(routes, "ctx_hi").reshape(levels, local_rows * top_count)
    gathered_weights = lax.all_gather(route_weights, "ctx_hi").reshape(levels * local_rows, top_count)
    expert_ids = jnp.arange(experts_all, dtype=jnp.int32)
    onehot = (gathered_routes[:, :, None] == expert_ids[None, None, :]).astype(jnp.int32)
    slot_rank = jnp.sum((jnp.cumsum(onehot, axis=1) - 1) * onehot, axis=2)
    source = lax.broadcasted_iota(jnp.int32, gathered_routes.shape, 0)
    within = gathered_routes % per_level
    slot_index = jnp.where(
        gathered_routes // per_level == level, (within * levels + source) * capacity + slot_rank, -1
    )
    slots_total = per_level * levels * capacity
    chosen_slots = slot_index.reshape(levels * local_rows, top_count)
    slot_ids = jnp.arange(slots_total, dtype=jnp.int32)
    hits = chosen_slots[:, :, None] == slot_ids[None, None, :]
    picker = jnp.any(hits, axis=1).astype(jnp.bfloat16)
    outgoing = lax.dot_general(
        picker, gathered_in, (((0,), (0,)), ((), ())), preferred_element_type=jnp.float32
    ).astype(jnp.bfloat16)
    level_axes = ("ctx_lo", "head")
    outgoing = outgoing.reshape(per_level // local_experts, local_experts * levels * capacity, D)
    arrived = lax.all_to_all(outgoing, level_axes, split_axis=0, concat_axis=0, tiled=True)
    arrived = arrived.reshape(per_level // local_experts, local_experts, levels * capacity, D)
    answered = jnp.stack(
        [
            expert_apply_rows(
                arrived[:, member].reshape(-1, D), expert_up[member], expert_down[member]
            ).reshape(arrived.shape[0], levels * capacity, D)
            for member in range(local_experts)
        ],
        axis=1,
    ).reshape(per_level // local_experts, local_experts * levels * capacity, D)
    returned = lax.all_to_all(answered, level_axes, split_axis=0, concat_axis=0, tiled=True)
    result_rows = returned.reshape(slots_total, D)
    weight_table = jnp.sum(jnp.where(hits, gathered_weights[:, :, None], 0.0), axis=1)
    weight_high = weight_table.astype(jnp.bfloat16)
    weight_low = (weight_table - weight_high.astype(jnp.float32)).astype(jnp.bfloat16)
    partial = jnp.dot(weight_high, result_rows, preferred_element_type=jnp.float32) + jnp.dot(
        weight_low, result_rows, preferred_element_type=jnp.float32
    )
    routed = lax.psum_scatter(
        partial.astype(jnp.bfloat16), "ctx_hi", scatter_dimension=0, tiled=True
    ).astype(jnp.float32)
    combined = hidden.astype(jnp.float32) + routed
    return combined.astype(jnp.bfloat16)


def split_mesh(mesh):
    groups, peers, pairs = (mesh.shape["group"], mesh.shape["ctx"], mesh.shape["head"])
    low = 4 if peers % 4 == 0 else 1
    devices = mesh.devices.reshape(groups, peers // low, low, pairs)
    return Mesh(devices, ("group", "ctx_hi", "ctx_lo", "head"))


def solution(mesh):
    return jax.shard_map(
        per_device,
        mesh=split_mesh(mesh),
        in_specs=(
            P(("group", "ctx_hi", "ctx_lo"), None, "head"),
            P(("group", "ctx_hi", "ctx_lo"), "head"),
            P(("group", "ctx_hi", "ctx_lo"), "head"),
            P(("group", "ctx_hi", "ctx_lo"), "head"),
            P(("group", "ctx_hi", "ctx_lo"), "head"),
            P("group"),
            P(None, None, "head"),
            P(None, "head"),
            P(),
            P("head", None),
            P(("group", "ctx_hi", "ctx_lo", "head"), None),
            P(),
            P(("group", "ctx_hi", "ctx_lo", "head"), None),
            P(("group", "ctx_hi", "ctx_lo", "head"), None),
            P(("ctx_hi", "ctx_lo", "head"), None, None),
            P(("ctx_hi", "ctx_lo", "head"), None, None),
        ),
        out_specs=P(("group", "ctx_hi", "ctx_lo", "head"), None),
        check_vma=False,
    )
```

```python
import jax
import jax.numpy as jnp
from jax import lax
from jax.sharding import Mesh, PartitionSpec as P

D = 2048
DK = 128
DV = 128
BLOCK = 64
CTX = ("ctx_hi", "ctx_lo")


HIGHEST = lax.Precision.HIGHEST


def passed_along(block, axis, distance):
    devices = range(lax.axis_size(axis))
    route = [(i - distance, i) for i in devices if i - distance in devices]
    return lax.ppermute(block, axis, route)


def scanned_entry(whole_map, whole_shift, axis):
    peers, position = (lax.axis_size(axis), lax.axis_index(axis))
    distance = 1
    while distance < peers:
        last = 2 * distance >= peers
        shift_in = passed_along(whole_shift.astype(jnp.bfloat16), axis, distance).astype(jnp.float32)
        reached = position >= distance
        new_shift = batched(whole_map, shift_in) + whole_shift
        if not last:
            map_in = passed_along(whole_map.astype(jnp.bfloat16), axis, distance).astype(jnp.float32)
            whole_map = jnp.where(reached, batched(whole_map, map_in), whole_map)
        whole_shift = jnp.where(reached, new_shift, whole_shift)
        distance *= 2
    return passed_along(whole_shift.astype(jnp.bfloat16), axis, 1).astype(jnp.float32)


def precise_dot(left, right):
    return jnp.dot(left, right, precision=HIGHEST, preferred_element_type=jnp.float32)


def causal_filter(padded_raw, filter_taps, padded_ids, kernel):
    length = padded_raw.shape[0] - (kernel - 1)
    source = padded_raw.astype(jnp.float32)
    current_ids = padded_ids[kernel - 1 :]
    summed = jnp.zeros((length, padded_raw.shape[1]), jnp.float32)
    for lag_step in range(kernel):
        offset_start = kernel - 1 - lag_step
        shifted = source[offset_start : offset_start + length]
        matching = (padded_ids[offset_start : offset_start + length] == current_ids).astype(
            jnp.float32
        )
        summed = summed + filter_taps[lag_step] * shifted * matching[:, None]
    return jax.nn.silu(summed)


def unit_rows(values_in):
    return values_in / jnp.sqrt(jnp.sum(values_in * values_in, axis=-1, keepdims=True) + 1e-06)


def mixer_inputs(pair_padded, value_padded, pair_filter, value_filter, padded_ids, kernel):
    pair_act = causal_filter(pair_padded, pair_filter.reshape(kernel, -1), padded_ids, kernel)
    length = pair_act.shape[0]
    pair_heads = pair_act.reshape(length, 2, -1, DK)
    queries = unit_rows(pair_heads[:, 0]) * DK ** (-0.5)
    key_rows = unit_rows(pair_heads[:, 1])
    value_rows = causal_filter(value_padded, value_filter, padded_ids, kernel).reshape(
        length, -1, DV
    )
    repeat_factor = value_rows.shape[1] // key_rows.shape[1]
    return (
        jnp.repeat(queries, repeat_factor, axis=1),
        jnp.repeat(key_rows, repeat_factor, axis=1),
        value_rows,
    )


def unit_lower_inverse(system):
    size = system.shape[-1]
    lead = system.shape[:-2]
    blocks = jnp.ones(lead + (size, 1, 1), system.dtype)
    width = 1
    while width < size:
        count = size // (2 * width)
        grid = system.reshape(lead + (count, 2 * width, count, 2 * width))
        diagonal = jnp.moveaxis(jnp.diagonal(grid, axis1=-4, axis2=-2), -1, -3)
        lower_left = diagonal[..., width:, :width]
        upper = blocks[..., 0::2, :, :]
        lower = blocks[..., 1::2, :, :]
        linked = -jnp.einsum(
            "...jab,...jbc->...jac",
            lower,
            jnp.einsum("...jab,...jbc->...jac", lower_left, upper, precision=HIGHEST),
            precision=HIGHEST,
        )
        top = jnp.concatenate([upper, jnp.zeros_like(upper)], axis=-1)
        bottom = jnp.concatenate([linked, lower], axis=-1)
        blocks = jnp.concatenate([top, bottom], axis=-2)
        width *= 2
    return blocks.reshape(lead + (size, size))


def block_setup(queries, key_rows, value_rows, strength, decay_rows, segment_here, prior_id):
    cumulative = jnp.cumsum(decay_rows)
    row_index = lax.broadcasted_iota(jnp.int32, (BLOCK, BLOCK), 0)
    col_index = lax.broadcasted_iota(jnp.int32, (BLOCK, BLOCK), 1)
    same_segment = segment_here[:, None] == segment_here[None, :]
    causal = (row_index >= col_index) & same_segment
    strictly = (row_index > col_index) & same_segment
    decay_matrix = jnp.where(
        causal, jnp.exp(jnp.where(causal, cumulative[:, None] - cumulative[None, :], 0.0)), 0.0
    )
    carried_in = (segment_here == prior_id).astype(jnp.float32)
    keyed_beta = key_rows * strength[:, None]
    coupling = jnp.where(strictly, precise_dot(keyed_beta, key_rows.T) * decay_matrix, 0.0)
    system = jnp.eye(BLOCK, dtype=jnp.float32) + coupling
    stacked = jnp.concatenate(
        [value_rows * strength[:, None], keyed_beta * (jnp.exp(cumulative) * carried_in)[:, None]],
        axis=1,
    )
    solved = precise_dot(unit_lower_inverse(system), stacked)
    targets = solved[:, :DV]
    corrector = solved[:, DV:]
    within = jnp.where(causal, precise_dot(queries, key_rows.T) * decay_matrix, 0.0)
    query_decayed = queries * (jnp.exp(cumulative) * carried_in)[:, None]
    final_log = cumulative[BLOCK - 1]
    weighting = (segment_here == segment_here[BLOCK - 1]).astype(jnp.float32) * jnp.exp(
        final_log - cumulative
    )
    keys_weighted = key_rows * weighting[:, None]
    transition = jnp.exp(final_log) * carried_in[BLOCK - 1] * jnp.eye(
        DK, dtype=jnp.float32
    ) - precise_dot(keys_weighted.T, corrector)
    increment = precise_dot(keys_weighted.T, targets)
    return (within, query_decayed, targets, corrector, transition, increment)


def head_major(array_in, block_count):
    moved = jnp.moveaxis(array_in, 1, 0)
    return moved.reshape((array_in.shape[1], block_count, BLOCK) + array_in.shape[2:])


def block_tables(queries, key_rows, value_rows, strength, decay_rows, padded_ids, kernel):
    length = queries.shape[0]
    block_count = length // BLOCK
    current_ids = padded_ids[kernel - 1 :].reshape(block_count, BLOCK)
    prior_ids = padded_ids[kernel - 2 : kernel - 2 + length : BLOCK]
    per_block = jax.vmap(block_setup, in_axes=(0, 0, 0, 0, 0, 0, 0))
    per_head = jax.vmap(per_block, in_axes=(0, 0, 0, 0, 0, None, None))
    return per_head(
        head_major(queries, block_count),
        head_major(key_rows, block_count),
        head_major(value_rows, block_count),
        head_major(strength, block_count),
        head_major(decay_rows, block_count),
        current_ids,
        prior_ids,
    )


def batched(left, right):
    return jnp.einsum("hij,hjk->hik", left, right, precision=HIGHEST)


def sweep_blocks(block_terms, start_state):
    blocks_first = tuple((jnp.swapaxes(member, 0, 1) for member in block_terms))

    def advance(carry_state, pieces):
        within, query_decayed, targets, corrector, transition, increment = pieces
        fresh_values = targets - batched(corrector, carry_state)
        emitted = batched(query_decayed, carry_state) + batched(within, fresh_values)
        updated = batched(transition, carry_state) + increment
        return (updated, emitted)

    final_state, emitted = lax.scan(advance, start_state, blocks_first)
    return emitted


def tokens_first(emitted):
    heads_count = emitted.shape[1]
    return jnp.transpose(emitted, (0, 2, 1, 3)).reshape(-1, heads_count, emitted.shape[3])


def gate_output(mixed_heads, gate_raw, norm_gain):
    square_mean = jnp.mean(mixed_heads * mixed_heads, axis=-1, keepdims=True)
    gate_values = jax.nn.silu(gate_raw.reshape(mixed_heads.shape).astype(jnp.float32))
    normed = mixed_heads / jnp.sqrt(square_mean + 1e-06) * norm_gain * gate_values
    return normed.astype(jnp.bfloat16).reshape(mixed_heads.shape[0], -1)


def post_norm(hidden, post_gain):
    hidden_full = hidden.astype(jnp.float32)
    square_mean = jnp.mean(hidden_full * hidden_full, axis=-1, keepdims=True)
    return (hidden_full / jnp.sqrt(square_mean + 1e-06) * post_gain).astype(jnp.bfloat16)


def expert_apply_rows(rows_in, up_matrix, down_matrix):
    hidden_units = down_matrix.shape[0]
    gate_up = jnp.dot(rows_in, up_matrix, preferred_element_type=jnp.float32)
    activated = (jax.nn.silu(gate_up[:, :hidden_units]) * gate_up[:, hidden_units:]).astype(
        jnp.bfloat16
    )
    return jnp.dot(activated, down_matrix, preferred_element_type=jnp.float32).astype(jnp.bfloat16)


def expert_apply(arrived, expert_up, expert_down):
    member_rows = arrived[:, 0]
    flattened = member_rows.reshape(-1, member_rows.shape[-1])
    result = expert_apply_rows(flattened, expert_up[0], expert_down[0])
    outputs = [result.reshape(member_rows.shape)]
    return jnp.stack(outputs, axis=1)


def route_slots(routes, experts_all, capacity):
    assigned = routes.reshape(-1)
    expert_ids = jnp.arange(experts_all, dtype=jnp.int32)
    onehot = (assigned[:, None] == expert_ids[None, :]).astype(jnp.int32)
    slot_rank = jnp.sum((jnp.cumsum(onehot, axis=0) - 1) * onehot, axis=1)
    return assigned * capacity + slot_rank


def per_device(
    pair_raw,
    value_raw,
    gate_raw,
    write_strength,
    log_decay,
    segment_ids,
    pair_filter,
    value_filter,
    norm_gain,
    out_weight,
    residual,
    post_gain,
    routes,
    route_weights,
    expert_up,
    expert_down,
):
    local_tokens = pair_raw.shape[0]
    kernel = value_filter.shape[0]
    pair_flat = pair_raw.reshape(local_tokens, -1)
    pair_width = pair_flat.shape[1]
    rim_rows = jnp.concatenate(
        [pair_flat[local_tokens - (kernel - 1) :], value_raw[local_tokens - (kernel - 1) :]], axis=1
    )
    before = passed_along(rim_rows, CTX, 1)
    first_token = lax.axis_index(CTX) * local_tokens
    padded_ids = jnp.concatenate([jnp.full((kernel - 1,), -1, jnp.int32), segment_ids])
    window_ids = lax.dynamic_slice_in_dim(padded_ids, first_token, local_tokens + kernel - 1)
    pair_padded = jnp.concatenate([before[:, :pair_width], pair_flat])
    value_padded = jnp.concatenate([before[:, pair_width:], value_raw])
    queries, key_rows, value_rows = mixer_inputs(
        pair_padded, value_padded, pair_filter, value_filter, window_ids, kernel
    )
    block_terms = block_tables(
        queries, key_rows, value_rows, write_strength, log_decay, window_ids, kernel
    )
    heads_here = value_rows.shape[1]
    identity_maps = jnp.broadcast_to(jnp.eye(DK, dtype=jnp.float32), (heads_here, DK, DK))
    empty_state = jnp.zeros((heads_here, DK, DV), jnp.float32)

    def fold_block(totals, pieces):
        transition, increment = pieces
        return ((batched(transition, totals[0]), batched(transition, totals[1]) + increment), None)

    whole_pair, unused = lax.scan(
        fold_block,
        (identity_maps, empty_state),
        (jnp.swapaxes(block_terms[4], 0, 1), jnp.swapaxes(block_terms[5], 0, 1)),
    )
    whole_map, whole_shift = whole_pair

    entering = scanned_entry(whole_map, whole_shift, CTX)
    emitted = sweep_blocks(block_terms, entering)
    gated_out = gate_output(tokens_first(emitted), gate_raw, norm_gain)
    attention = lax.psum_scatter(
        jnp.dot(gated_out, out_weight, preferred_element_type=jnp.float32).astype(jnp.bfloat16),
        "head",
        scatter_dimension=0,
        tiled=True,
    ).astype(jnp.float32)
    hidden = (residual.astype(jnp.float32) + attention).astype(jnp.bfloat16)
    expert_in = post_norm(hidden, post_gain)
    levels = lax.axis_size("ctx_hi")
    level = lax.axis_index("ctx_hi")
    local_experts = expert_up.shape[0]
    per_level = lax.axis_size("ctx_lo") * lax.axis_size("head") * local_experts
    experts_all = levels * per_level
    local_rows = routes.shape[0]
    top_count = routes.shape[1]
    capacity = local_rows * top_count * 5 // (4 * experts_all)
    own_high = route_weights.astype(jnp.bfloat16)
    own_low = (route_weights - own_high.astype(jnp.float32)).astype(jnp.bfloat16)
    spare = -(-(3 * top_count) // 128) * 128 - 3 * top_count
    packed = jnp.concatenate(
        [
            expert_in,
            routes.astype(jnp.bfloat16),
            own_high,
            own_low,
            jnp.zeros((local_rows, spare), jnp.bfloat16),
        ],
        axis=1,
    )
    gathered = lax.all_gather(packed, "ctx_hi").reshape(levels * local_rows, -1)
    gathered_in = gathered[:, :D]
    gathered_routes = gathered[:, D : D + top_count].astype(jnp.int32)
    gathered_high = gathered[:, D + top_count : D + 2 * top_count]
    gathered_low = gathered[:, D + 2 * top_count : D + 3 * top_count]
    expert_ids = jnp.arange(experts_all, dtype=jnp.int32)
    row_hot = jnp.any(gathered_routes[:, :, None] == expert_ids[None, None, :], axis=1)
    row_hot = row_hot.reshape(levels, local_rows, experts_all).astype(jnp.bfloat16)
    earlier_rows = (
        lax.broadcasted_iota(jnp.int32, (local_rows, local_rows), 0)
        > lax.broadcasted_iota(jnp.int32, (local_rows, local_rows), 1)
    ).astype(jnp.bfloat16)
    earlier = jnp.einsum(
        "ij,sje->sie", earlier_rows, row_hot, preferred_element_type=jnp.float32
    ).reshape(levels * local_rows, 1, experts_all)
    slot_rank = jnp.sum(
        jnp.where(gathered_routes[:, :, None] == expert_ids[None, None, :], earlier, 0.0), axis=2
    ).astype(jnp.int32)
    gathered_routes = gathered_routes.reshape(levels, local_rows * top_count)
    slot_rank = slot_rank.reshape(levels, local_rows * top_count)
    source = lax.broadcasted_iota(jnp.int32, gathered_routes.shape, 0)
    within = gathered_routes % per_level
    slot_index = jnp.where(
        gathered_routes // per_level == level, (within * levels + source) * capacity + slot_rank, -1
    )
    slots_total = per_level * levels * capacity
    chosen_slots = slot_index.reshape(levels * local_rows, top_count)
    slot_ids = jnp.arange(slots_total, dtype=jnp.int32)
    hits = chosen_slots[:, :, None] == slot_ids[None, None, :]
    picker = jnp.any(hits, axis=1).astype(jnp.bfloat16)
    outgoing = lax.dot_general(
        picker, gathered_in, (((0,), (0,)), ((), ())), preferred_element_type=jnp.float32
    ).astype(jnp.bfloat16)
    level_axes = ("ctx_lo", "head")
    outgoing = outgoing.reshape(per_level // local_experts, local_experts * levels * capacity, D)
    arrived = lax.all_to_all(outgoing, level_axes, split_axis=0, concat_axis=0, tiled=True)
    arrived = arrived.reshape(per_level // local_experts, local_experts, levels * capacity, D)
    answered = jnp.stack(
        [
            expert_apply_rows(
                arrived[:, member].reshape(-1, D), expert_up[member], expert_down[member]
            ).reshape(arrived.shape[0], levels * capacity, D)
            for member in range(local_experts)
        ],
        axis=1,
    ).reshape(per_level // local_experts, local_experts * levels * capacity, D)
    returned = lax.all_to_all(answered, level_axes, split_axis=0, concat_axis=0, tiled=True)
    result_rows = returned.reshape(slots_total, D)
    weight_high = jnp.sum(jnp.where(hits, gathered_high[:, :, None], 0.0), axis=1).astype(
        jnp.bfloat16
    )
    weight_low = jnp.sum(jnp.where(hits, gathered_low[:, :, None], 0.0), axis=1).astype(
        jnp.bfloat16
    )
    partial = jnp.dot(weight_high, result_rows, preferred_element_type=jnp.float32) + jnp.dot(
        weight_low, result_rows, preferred_element_type=jnp.float32
    )
    routed = lax.psum_scatter(
        partial.astype(jnp.bfloat16), "ctx_hi", scatter_dimension=0, tiled=True
    ).astype(jnp.float32)
    combined = hidden.astype(jnp.float32) + routed
    return combined.astype(jnp.bfloat16)


def split_mesh(mesh):
    groups, peers, pairs = (mesh.shape["group"], mesh.shape["ctx"], mesh.shape["head"])
    low = 4 if peers % 4 == 0 else 1
    devices = mesh.devices.reshape(groups, peers // low, low, pairs)
    return Mesh(devices, ("group", "ctx_hi", "ctx_lo", "head"))


def solution(mesh):
    return jax.shard_map(
        per_device,
        mesh=split_mesh(mesh),
        in_specs=(
            P(("group", "ctx_hi", "ctx_lo"), None, "head"),
            P(("group", "ctx_hi", "ctx_lo"), "head"),
            P(("group", "ctx_hi", "ctx_lo"), "head"),
            P(("group", "ctx_hi", "ctx_lo"), "head"),
            P(("group", "ctx_hi", "ctx_lo"), "head"),
            P("group"),
            P(None, None, "head"),
            P(None, "head"),
            P(),
            P("head", None),
            P(("group", "ctx_hi", "ctx_lo", "head"), None),
            P(),
            P(("group", "ctx_hi", "ctx_lo", "head"), None),
            P(("group", "ctx_hi", "ctx_lo", "head"), None),
            P(("ctx_hi", "ctx_lo", "head"), None, None),
            P(("ctx_hi", "ctx_lo", "head"), None, None),
        ),
        out_specs=P(("group", "ctx_hi", "ctx_lo", "head"), None),
        check_vma=False,
    )
```

```python
import jax
import jax.numpy as jnp
from jax import lax
from jax.sharding import Mesh, PartitionSpec as P

D = 2048
DK = 128
DV = 128
BLOCK = 64
CTX = ("ctx_hi", "ctx_lo")


HIGHEST = lax.Precision.HIGHEST


def passed_along(block, axis, distance):
    devices = range(lax.axis_size(axis))
    route = [(i - distance, i) for i in devices if i - distance in devices]
    return lax.ppermute(block, axis, route)


def scanned_entry(whole_map, whole_shift, axis):
    peers, position = (lax.axis_size(axis), lax.axis_index(axis))
    distance = 1
    while distance < peers:
        last = 2 * distance >= peers
        shift_in = passed_along(whole_shift.astype(jnp.bfloat16), axis, distance).astype(jnp.float32)
        reached = position >= distance
        new_shift = batched(whole_map, shift_in) + whole_shift
        if not last:
            map_in = passed_along(whole_map.astype(jnp.bfloat16), axis, distance).astype(jnp.float32)
            whole_map = jnp.where(reached, batched(whole_map, map_in), whole_map)
        whole_shift = jnp.where(reached, new_shift, whole_shift)
        distance *= 2
    return passed_along(whole_shift.astype(jnp.bfloat16), axis, 1).astype(jnp.float32)


def precise_dot(left, right):
    return jnp.dot(left, right, precision=HIGHEST, preferred_element_type=jnp.float32)


def causal_filter(padded_raw, filter_taps, padded_ids, kernel):
    length = padded_raw.shape[0] - (kernel - 1)
    source = padded_raw.astype(jnp.float32)
    current_ids = padded_ids[kernel - 1 :]
    summed = jnp.zeros((length, padded_raw.shape[1]), jnp.float32)
    for lag_step in range(kernel):
        offset_start = kernel - 1 - lag_step
        shifted = source[offset_start : offset_start + length]
        matching = (padded_ids[offset_start : offset_start + length] == current_ids).astype(
            jnp.float32
        )
        summed = summed + filter_taps[lag_step] * shifted * matching[:, None]
    return jax.nn.silu(summed)


def unit_rows(values_in):
    return values_in / jnp.sqrt(jnp.sum(values_in * values_in, axis=-1, keepdims=True) + 1e-06)


def mixer_inputs(pair_padded, value_padded, pair_filter, value_filter, padded_ids, kernel):
    pair_act = causal_filter(pair_padded, pair_filter.reshape(kernel, -1), padded_ids, kernel)
    length = pair_act.shape[0]
    pair_heads = pair_act.reshape(length, 2, -1, DK)
    queries = unit_rows(pair_heads[:, 0]) * DK ** (-0.5)
    key_rows = unit_rows(pair_heads[:, 1])
    value_rows = causal_filter(value_padded, value_filter, padded_ids, kernel).reshape(
        length, -1, DV
    )
    repeat_factor = value_rows.shape[1] // key_rows.shape[1]
    return (
        jnp.repeat(queries, repeat_factor, axis=1),
        jnp.repeat(key_rows, repeat_factor, axis=1),
        value_rows,
    )


def unit_lower_inverse(system):
    size = system.shape[-1]
    row_index = lax.broadcasted_iota(jnp.int32, (size, size), 0)
    col_index = lax.broadcasted_iota(jnp.int32, (size, size), 1)
    inverse = jnp.broadcast_to(jnp.eye(size, dtype=system.dtype), system.shape)
    width = 1
    while width < size:
        linking = (
            (row_index // (2 * width) == col_index // (2 * width))
            & ((row_index // width) % 2 == 1)
            & ((col_index // width) % 2 == 0)
        )
        lower_left = jnp.where(linking, system, 0.0)
        inverse = inverse - precise_dot(inverse, precise_dot(lower_left, inverse))
        width *= 2
    return inverse


def block_setup(queries, key_rows, value_rows, strength, decay_rows, segment_here, prior_id):
    cumulative = jnp.cumsum(decay_rows)
    row_index = lax.broadcasted_iota(jnp.int32, (BLOCK, BLOCK), 0)
    col_index = lax.broadcasted_iota(jnp.int32, (BLOCK, BLOCK), 1)
    same_segment = segment_here[:, None] == segment_here[None, :]
    causal = (row_index >= col_index) & same_segment
    strictly = (row_index > col_index) & same_segment
    decay_matrix = jnp.where(
        causal, jnp.exp(jnp.where(causal, cumulative[:, None] - cumulative[None, :], 0.0)), 0.0
    )
    carried_in = (segment_here == prior_id).astype(jnp.float32)
    keyed_beta = key_rows * strength[:, None]
    coupling = jnp.where(strictly, precise_dot(keyed_beta, key_rows.T) * decay_matrix, 0.0)
    system = jnp.eye(BLOCK, dtype=jnp.float32) + coupling
    stacked = jnp.concatenate(
        [value_rows * strength[:, None], keyed_beta * (jnp.exp(cumulative) * carried_in)[:, None]],
        axis=1,
    )
    solved = precise_dot(unit_lower_inverse(system), stacked)
    targets = solved[:, :DV]
    corrector = solved[:, DV:]
    within = jnp.where(causal, precise_dot(queries, key_rows.T) * decay_matrix, 0.0)
    query_decayed = queries * (jnp.exp(cumulative) * carried_in)[:, None]
    final_log = cumulative[BLOCK - 1]
    weighting = (segment_here == segment_here[BLOCK - 1]).astype(jnp.float32) * jnp.exp(
        final_log - cumulative
    )
    keys_weighted = key_rows * weighting[:, None]
    transition = jnp.exp(final_log) * carried_in[BLOCK - 1] * jnp.eye(
        DK, dtype=jnp.float32
    ) - precise_dot(keys_weighted.T, corrector)
    increment = precise_dot(keys_weighted.T, targets)
    return (within, query_decayed, targets, corrector, transition, increment)


def head_major(array_in, block_count):
    moved = jnp.moveaxis(array_in, 1, 0)
    return moved.reshape((array_in.shape[1], block_count, BLOCK) + array_in.shape[2:])


def block_tables(queries, key_rows, value_rows, strength, decay_rows, padded_ids, kernel):
    length = queries.shape[0]
    block_count = length // BLOCK
    current_ids = padded_ids[kernel - 1 :].reshape(block_count, BLOCK)
    prior_ids = padded_ids[kernel - 2 : kernel - 2 + length : BLOCK]
    per_block = jax.vmap(block_setup, in_axes=(0, 0, 0, 0, 0, 0, 0))
    per_head = jax.vmap(per_block, in_axes=(0, 0, 0, 0, 0, None, None))
    return per_head(
        head_major(queries, block_count),
        head_major(key_rows, block_count),
        head_major(value_rows, block_count),
        head_major(strength, block_count),
        head_major(decay_rows, block_count),
        current_ids,
        prior_ids,
    )


def batched(left, right):
    return jnp.einsum("hij,hjk->hik", left, right, precision=HIGHEST)


def sweep_blocks(block_terms, start_state):
    blocks_first = tuple((jnp.swapaxes(member, 0, 1) for member in block_terms))

    def advance(carry_state, pieces):
        within, query_decayed, targets, corrector, transition, increment = pieces
        fresh_values = targets - batched(corrector, carry_state)
        emitted = batched(query_decayed, carry_state) + batched(within, fresh_values)
        updated = batched(transition, carry_state) + increment
        return (updated, emitted)

    final_state, emitted = lax.scan(advance, start_state, blocks_first)
    return emitted


def tokens_first(emitted):
    heads_count = emitted.shape[1]
    return jnp.transpose(emitted, (0, 2, 1, 3)).reshape(-1, heads_count, emitted.shape[3])


def gate_output(mixed_heads, gate_raw, norm_gain):
    square_mean = jnp.mean(mixed_heads * mixed_heads, axis=-1, keepdims=True)
    gate_values = jax.nn.silu(gate_raw.reshape(mixed_heads.shape).astype(jnp.float32))
    normed = mixed_heads / jnp.sqrt(square_mean + 1e-06) * norm_gain * gate_values
    return normed.astype(jnp.bfloat16).reshape(mixed_heads.shape[0], -1)


def post_norm(hidden, post_gain):
    hidden_full = hidden.astype(jnp.float32)
    square_mean = jnp.mean(hidden_full * hidden_full, axis=-1, keepdims=True)
    return (hidden_full / jnp.sqrt(square_mean + 1e-06) * post_gain).astype(jnp.bfloat16)


def expert_apply_rows(rows_in, up_matrix, down_matrix):
    hidden_units = down_matrix.shape[0]
    gate_up = jnp.dot(rows_in, up_matrix, preferred_element_type=jnp.float32)
    activated = (jax.nn.silu(gate_up[:, :hidden_units]) * gate_up[:, hidden_units:]).astype(
        jnp.bfloat16
    )
    return jnp.dot(activated, down_matrix, preferred_element_type=jnp.float32).astype(jnp.bfloat16)


def expert_apply(arrived, expert_up, expert_down):
    member_rows = arrived[:, 0]
    flattened = member_rows.reshape(-1, member_rows.shape[-1])
    result = expert_apply_rows(flattened, expert_up[0], expert_down[0])
    outputs = [result.reshape(member_rows.shape)]
    return jnp.stack(outputs, axis=1)


def route_slots(routes, experts_all, capacity):
    assigned = routes.reshape(-1)
    expert_ids = jnp.arange(experts_all, dtype=jnp.int32)
    onehot = (assigned[:, None] == expert_ids[None, :]).astype(jnp.int32)
    slot_rank = jnp.sum((jnp.cumsum(onehot, axis=0) - 1) * onehot, axis=1)
    return assigned * capacity + slot_rank


def per_device(
    pair_raw,
    value_raw,
    gate_raw,
    write_strength,
    log_decay,
    segment_ids,
    pair_filter,
    value_filter,
    norm_gain,
    out_weight,
    residual,
    post_gain,
    routes,
    route_weights,
    expert_up,
    expert_down,
):
    local_tokens = pair_raw.shape[0]
    kernel = value_filter.shape[0]
    pair_flat = pair_raw.reshape(local_tokens, -1)
    pair_width = pair_flat.shape[1]
    rim_rows = jnp.concatenate(
        [pair_flat[local_tokens - (kernel - 1) :], value_raw[local_tokens - (kernel - 1) :]], axis=1
    )
    before = passed_along(rim_rows, CTX, 1)
    first_token = lax.axis_index(CTX) * local_tokens
    padded_ids = jnp.concatenate([jnp.full((kernel - 1,), -1, jnp.int32), segment_ids])
    window_ids = lax.dynamic_slice_in_dim(padded_ids, first_token, local_tokens + kernel - 1)
    pair_padded = jnp.concatenate([before[:, :pair_width], pair_flat])
    value_padded = jnp.concatenate([before[:, pair_width:], value_raw])
    queries, key_rows, value_rows = mixer_inputs(
        pair_padded, value_padded, pair_filter, value_filter, window_ids, kernel
    )
    block_terms = block_tables(
        queries, key_rows, value_rows, write_strength, log_decay, window_ids, kernel
    )
    heads_here = value_rows.shape[1]
    identity_maps = jnp.broadcast_to(jnp.eye(DK, dtype=jnp.float32), (heads_here, DK, DK))
    empty_state = jnp.zeros((heads_here, DK, DV), jnp.float32)

    def fold_block(totals, pieces):
        transition, increment = pieces
        return ((batched(transition, totals[0]), batched(transition, totals[1]) + increment), None)

    whole_pair, unused = lax.scan(
        fold_block,
        (identity_maps, empty_state),
        (jnp.swapaxes(block_terms[4], 0, 1), jnp.swapaxes(block_terms[5], 0, 1)),
    )
    whole_map, whole_shift = whole_pair

    entering = scanned_entry(whole_map, whole_shift, CTX)
    emitted = sweep_blocks(block_terms, entering)
    gated_out = gate_output(tokens_first(emitted), gate_raw, norm_gain)
    attention = lax.psum_scatter(
        jnp.dot(gated_out, out_weight, preferred_element_type=jnp.float32).astype(jnp.bfloat16),
        "head",
        scatter_dimension=0,
        tiled=True,
    ).astype(jnp.float32)
    hidden = (residual.astype(jnp.float32) + attention).astype(jnp.bfloat16)
    expert_in = post_norm(hidden, post_gain)
    levels = lax.axis_size("ctx_hi")
    level = lax.axis_index("ctx_hi")
    local_experts = expert_up.shape[0]
    per_level = lax.axis_size("ctx_lo") * lax.axis_size("head") * local_experts
    experts_all = levels * per_level
    local_rows = routes.shape[0]
    top_count = routes.shape[1]
    capacity = local_rows * top_count * 5 // (4 * experts_all)
    own_high = route_weights.astype(jnp.bfloat16)
    own_low = (route_weights - own_high.astype(jnp.float32)).astype(jnp.bfloat16)
    spare = -(-(3 * top_count) // 128) * 128 - 3 * top_count
    packed = jnp.concatenate(
        [
            expert_in,
            routes.astype(jnp.bfloat16),
            own_high,
            own_low,
            jnp.zeros((local_rows, spare), jnp.bfloat16),
        ],
        axis=1,
    )
    gathered = lax.all_gather(packed, "ctx_hi").reshape(levels * local_rows, -1)
    gathered_in = gathered[:, :D]
    gathered_routes = gathered[:, D : D + top_count].astype(jnp.int32)
    gathered_high = gathered[:, D + top_count : D + 2 * top_count]
    gathered_low = gathered[:, D + 2 * top_count : D + 3 * top_count]
    expert_ids = jnp.arange(experts_all, dtype=jnp.int32)
    row_hot = jnp.any(gathered_routes[:, :, None] == expert_ids[None, None, :], axis=1)
    row_hot = row_hot.reshape(levels, local_rows, experts_all).astype(jnp.bfloat16)
    earlier_rows = (
        lax.broadcasted_iota(jnp.int32, (local_rows, local_rows), 0)
        > lax.broadcasted_iota(jnp.int32, (local_rows, local_rows), 1)
    ).astype(jnp.bfloat16)
    earlier = jnp.einsum(
        "ij,sje->sie", earlier_rows, row_hot, preferred_element_type=jnp.float32
    ).reshape(levels * local_rows, 1, experts_all)
    slot_rank = jnp.sum(
        jnp.where(gathered_routes[:, :, None] == expert_ids[None, None, :], earlier, 0.0), axis=2
    ).astype(jnp.int32)
    gathered_routes = gathered_routes.reshape(levels, local_rows * top_count)
    slot_rank = slot_rank.reshape(levels, local_rows * top_count)
    source = lax.broadcasted_iota(jnp.int32, gathered_routes.shape, 0)
    within = gathered_routes % per_level
    slot_index = jnp.where(
        gathered_routes // per_level == level, (within * levels + source) * capacity + slot_rank, -1
    )
    slots_total = per_level * levels * capacity
    chosen_slots = slot_index.reshape(levels * local_rows, top_count)
    slot_ids = jnp.arange(slots_total, dtype=jnp.int32)
    hits = chosen_slots[:, :, None] == slot_ids[None, None, :]
    picker = jnp.any(hits, axis=1).astype(jnp.bfloat16)
    outgoing = lax.dot_general(
        picker, gathered_in, (((0,), (0,)), ((), ())), preferred_element_type=jnp.float32
    ).astype(jnp.bfloat16)
    level_axes = ("ctx_lo", "head")
    outgoing = outgoing.reshape(per_level // local_experts, local_experts * levels * capacity, D)
    arrived = lax.all_to_all(outgoing, level_axes, split_axis=0, concat_axis=0, tiled=True)
    arrived = arrived.reshape(per_level // local_experts, local_experts, levels * capacity, D)
    answered = jnp.stack(
        [
            expert_apply_rows(
                arrived[:, member].reshape(-1, D), expert_up[member], expert_down[member]
            ).reshape(arrived.shape[0], levels * capacity, D)
            for member in range(local_experts)
        ],
        axis=1,
    ).reshape(per_level // local_experts, local_experts * levels * capacity, D)
    returned = lax.all_to_all(answered, level_axes, split_axis=0, concat_axis=0, tiled=True)
    result_rows = returned.reshape(slots_total, D)
    weight_high = jnp.sum(jnp.where(hits, gathered_high[:, :, None], 0.0), axis=1).astype(
        jnp.bfloat16
    )
    weight_low = jnp.sum(jnp.where(hits, gathered_low[:, :, None], 0.0), axis=1).astype(
        jnp.bfloat16
    )
    partial = jnp.dot(weight_high, result_rows, preferred_element_type=jnp.float32) + jnp.dot(
        weight_low, result_rows, preferred_element_type=jnp.float32
    )
    routed = lax.psum_scatter(
        partial.astype(jnp.bfloat16), "ctx_hi", scatter_dimension=0, tiled=True
    ).astype(jnp.float32)
    combined = hidden.astype(jnp.float32) + routed
    return combined.astype(jnp.bfloat16)


def split_mesh(mesh):
    groups, peers, pairs = (mesh.shape["group"], mesh.shape["ctx"], mesh.shape["head"])
    low = 4 if peers % 4 == 0 else 1
    devices = mesh.devices.reshape(groups, peers // low, low, pairs)
    return Mesh(devices, ("group", "ctx_hi", "ctx_lo", "head"))


def solution(mesh):
    return jax.shard_map(
        per_device,
        mesh=split_mesh(mesh),
        in_specs=(
            P(("group", "ctx_hi", "ctx_lo"), None, "head"),
            P(("group", "ctx_hi", "ctx_lo"), "head"),
            P(("group", "ctx_hi", "ctx_lo"), "head"),
            P(("group", "ctx_hi", "ctx_lo"), "head"),
            P(("group", "ctx_hi", "ctx_lo"), "head"),
            P("group"),
            P(None, None, "head"),
            P(None, "head"),
            P(),
            P("head", None),
            P(("group", "ctx_hi", "ctx_lo", "head"), None),
            P(),
            P(("group", "ctx_hi", "ctx_lo", "head"), None),
            P(("group", "ctx_hi", "ctx_lo", "head"), None),
            P(("ctx_hi", "ctx_lo", "head"), None, None),
            P(("ctx_hi", "ctx_lo", "head"), None, None),
        ),
        out_specs=P(("group", "ctx_hi", "ctx_lo", "head"), None),
        check_vma=False,
    )
```

```python
import jax
import jax.numpy as jnp
from jax import lax
from jax.sharding import Mesh, PartitionSpec as P

D = 2048
DK = 128
DV = 128
BLOCK = 64
CTX = ("ctx_hi", "ctx_lo")


HIGHEST = lax.Precision.HIGHEST


def passed_along(block, axis, distance):
    devices = range(lax.axis_size(axis))
    route = [(i - distance, i) for i in devices if i - distance in devices]
    return lax.ppermute(block, axis, route)


def scanned_entry(whole_map, whole_shift, axis):
    peers, position = (lax.axis_size(axis), lax.axis_index(axis))
    distance = 1
    while distance < peers:
        last = 2 * distance >= peers
        shift_in = passed_along(whole_shift.astype(jnp.bfloat16), axis, distance).astype(jnp.float32)
        reached = position >= distance
        new_shift = batched(whole_map, shift_in) + whole_shift
        if not last:
            map_in = passed_along(whole_map.astype(jnp.bfloat16), axis, distance).astype(jnp.float32)
            whole_map = jnp.where(reached, batched(whole_map, map_in), whole_map)
        whole_shift = jnp.where(reached, new_shift, whole_shift)
        distance *= 2
    return passed_along(whole_shift.astype(jnp.bfloat16), axis, 1).astype(jnp.float32)


def precise_dot(left, right):
    return jnp.dot(left, right, precision=HIGHEST, preferred_element_type=jnp.float32)


def causal_filter(padded_raw, filter_taps, padded_ids, kernel):
    length = padded_raw.shape[0] - (kernel - 1)
    source = padded_raw.astype(jnp.float32)
    current_ids = padded_ids[kernel - 1 :]
    summed = jnp.zeros((length, padded_raw.shape[1]), jnp.float32)
    for lag_step in range(kernel):
        offset_start = kernel - 1 - lag_step
        shifted = source[offset_start : offset_start + length]
        matching = (padded_ids[offset_start : offset_start + length] == current_ids).astype(
            jnp.float32
        )
        summed = summed + filter_taps[lag_step] * shifted * matching[:, None]
    return jax.nn.silu(summed)


def unit_rows(values_in):
    return values_in / jnp.sqrt(jnp.sum(values_in * values_in, axis=-1, keepdims=True) + 1e-06)


def mixer_inputs(pair_padded, value_padded, pair_filter, value_filter, padded_ids, kernel):
    pair_act = causal_filter(pair_padded, pair_filter.reshape(kernel, -1), padded_ids, kernel)
    length = pair_act.shape[0]
    pair_heads = pair_act.reshape(length, 2, -1, DK)
    queries = unit_rows(pair_heads[:, 0]) * DK ** (-0.5)
    key_rows = unit_rows(pair_heads[:, 1])
    value_rows = causal_filter(value_padded, value_filter, padded_ids, kernel).reshape(
        length, -1, DV
    )
    repeat_factor = value_rows.shape[1] // key_rows.shape[1]
    return (
        jnp.repeat(queries, repeat_factor, axis=1),
        jnp.repeat(key_rows, repeat_factor, axis=1),
        value_rows,
    )


def unit_lower_inverse(system):
    size = system.shape[-1]
    row_index = lax.broadcasted_iota(jnp.int32, (size, size), 0)
    col_index = lax.broadcasted_iota(jnp.int32, (size, size), 1)
    inverse = jnp.broadcast_to(jnp.eye(size, dtype=system.dtype), system.shape)
    width = 1
    while width < size:
        linking = (
            (row_index // (2 * width) == col_index // (2 * width))
            & ((row_index // width) % 2 == 1)
            & ((col_index // width) % 2 == 0)
        )
        lower_left = jnp.where(linking, system, 0.0)
        inverse = inverse - precise_dot(inverse, precise_dot(lower_left, inverse))
        width *= 2
    return inverse


def block_setup(queries, key_rows, value_rows, strength, decay_rows, segment_here, prior_id):
    cumulative = jnp.cumsum(decay_rows)
    row_index = lax.broadcasted_iota(jnp.int32, (BLOCK, BLOCK), 0)
    col_index = lax.broadcasted_iota(jnp.int32, (BLOCK, BLOCK), 1)
    same_segment = segment_here[:, None] == segment_here[None, :]
    causal = (row_index >= col_index) & same_segment
    strictly = (row_index > col_index) & same_segment
    decay_matrix = jnp.where(
        causal, jnp.exp(jnp.where(causal, cumulative[:, None] - cumulative[None, :], 0.0)), 0.0
    )
    carried_in = (segment_here == prior_id).astype(jnp.float32)
    keyed_beta = key_rows * strength[:, None]
    coupling = jnp.where(strictly, precise_dot(keyed_beta, key_rows.T) * decay_matrix, 0.0)
    system = jnp.eye(BLOCK, dtype=jnp.float32) + coupling
    stacked = jnp.concatenate(
        [value_rows * strength[:, None], keyed_beta * (jnp.exp(cumulative) * carried_in)[:, None]],
        axis=1,
    )
    solved = precise_dot(unit_lower_inverse(system), stacked)
    targets = solved[:, :DV]
    corrector = solved[:, DV:]
    within = jnp.where(causal, precise_dot(queries, key_rows.T) * decay_matrix, 0.0)
    query_decayed = queries * (jnp.exp(cumulative) * carried_in)[:, None]
    final_log = cumulative[BLOCK - 1]
    weighting = (segment_here == segment_here[BLOCK - 1]).astype(jnp.float32) * jnp.exp(
        final_log - cumulative
    )
    keys_weighted = key_rows * weighting[:, None]
    transition = jnp.exp(final_log) * carried_in[BLOCK - 1] * jnp.eye(
        DK, dtype=jnp.float32
    ) - precise_dot(keys_weighted.T, corrector)
    increment = precise_dot(keys_weighted.T, targets)
    return (within, query_decayed, targets, corrector, transition, increment)


def head_major(array_in, block_count):
    moved = jnp.moveaxis(array_in, 1, 0)
    return moved.reshape((array_in.shape[1], block_count, BLOCK) + array_in.shape[2:])


def block_tables(queries, key_rows, value_rows, strength, decay_rows, padded_ids, kernel):
    length = queries.shape[0]
    block_count = length // BLOCK
    current_ids = padded_ids[kernel - 1 :].reshape(block_count, BLOCK)
    prior_ids = padded_ids[kernel - 2 : kernel - 2 + length : BLOCK]
    per_block = jax.vmap(block_setup, in_axes=(0, 0, 0, 0, 0, 0, 0))
    per_head = jax.vmap(per_block, in_axes=(0, 0, 0, 0, 0, None, None))
    return per_head(
        head_major(queries, block_count),
        head_major(key_rows, block_count),
        head_major(value_rows, block_count),
        head_major(strength, block_count),
        head_major(decay_rows, block_count),
        current_ids,
        prior_ids,
    )


def blockwise(left, right):
    return jnp.einsum("hbij,hbjk->hbik", left, right, precision=HIGHEST)


def batched(left, right):
    return jnp.einsum("hij,hjk->hik", left, right, precision=HIGHEST)


def sweep_blocks(block_terms, start_state):
    blocks_first = tuple((jnp.swapaxes(member, 0, 1) for member in block_terms))

    def advance(carry_state, pieces):
        within, query_decayed, targets, corrector, transition, increment = pieces
        fresh_values = targets - batched(corrector, carry_state)
        emitted = batched(query_decayed, carry_state) + batched(within, fresh_values)
        updated = batched(transition, carry_state) + increment
        return (updated, emitted)

    final_state, emitted = lax.scan(advance, start_state, blocks_first)
    return emitted


def tokens_first(emitted):
    heads_count = emitted.shape[1]
    return jnp.transpose(emitted, (0, 2, 1, 3)).reshape(-1, heads_count, emitted.shape[3])


def gate_output(mixed_heads, gate_raw, norm_gain):
    square_mean = jnp.mean(mixed_heads * mixed_heads, axis=-1, keepdims=True)
    gate_values = jax.nn.silu(gate_raw.reshape(mixed_heads.shape).astype(jnp.float32))
    normed = mixed_heads / jnp.sqrt(square_mean + 1e-06) * norm_gain * gate_values
    return normed.astype(jnp.bfloat16).reshape(mixed_heads.shape[0], -1)


def post_norm(hidden, post_gain):
    hidden_full = hidden.astype(jnp.float32)
    square_mean = jnp.mean(hidden_full * hidden_full, axis=-1, keepdims=True)
    return (hidden_full / jnp.sqrt(square_mean + 1e-06) * post_gain).astype(jnp.bfloat16)


def expert_apply_rows(rows_in, up_matrix, down_matrix):
    hidden_units = down_matrix.shape[0]
    gate_up = jnp.dot(rows_in, up_matrix, preferred_element_type=jnp.float32)
    activated = (jax.nn.silu(gate_up[:, :hidden_units]) * gate_up[:, hidden_units:]).astype(
        jnp.bfloat16
    )
    return jnp.dot(activated, down_matrix, preferred_element_type=jnp.float32).astype(jnp.bfloat16)


def expert_apply(arrived, expert_up, expert_down):
    member_rows = arrived[:, 0]
    flattened = member_rows.reshape(-1, member_rows.shape[-1])
    result = expert_apply_rows(flattened, expert_up[0], expert_down[0])
    outputs = [result.reshape(member_rows.shape)]
    return jnp.stack(outputs, axis=1)


def route_slots(routes, experts_all, capacity):
    assigned = routes.reshape(-1)
    expert_ids = jnp.arange(experts_all, dtype=jnp.int32)
    onehot = (assigned[:, None] == expert_ids[None, :]).astype(jnp.int32)
    slot_rank = jnp.sum((jnp.cumsum(onehot, axis=0) - 1) * onehot, axis=1)
    return assigned * capacity + slot_rank


def per_device(
    pair_raw,
    value_raw,
    gate_raw,
    write_strength,
    log_decay,
    segment_ids,
    pair_filter,
    value_filter,
    norm_gain,
    out_weight,
    residual,
    post_gain,
    routes,
    route_weights,
    expert_up,
    expert_down,
):
    local_tokens = pair_raw.shape[0]
    kernel = value_filter.shape[0]
    pair_flat = pair_raw.reshape(local_tokens, -1)
    pair_width = pair_flat.shape[1]
    rim_rows = jnp.concatenate(
        [pair_flat[local_tokens - (kernel - 1) :], value_raw[local_tokens - (kernel - 1) :]], axis=1
    )
    before = passed_along(rim_rows, CTX, 1)
    first_token = lax.axis_index(CTX) * local_tokens
    padded_ids = jnp.concatenate([jnp.full((kernel - 1,), -1, jnp.int32), segment_ids])
    window_ids = lax.dynamic_slice_in_dim(padded_ids, first_token, local_tokens + kernel - 1)
    pair_padded = jnp.concatenate([before[:, :pair_width], pair_flat])
    value_padded = jnp.concatenate([before[:, pair_width:], value_raw])
    queries, key_rows, value_rows = mixer_inputs(
        pair_padded, value_padded, pair_filter, value_filter, window_ids, kernel
    )
    block_terms = block_tables(
        queries, key_rows, value_rows, write_strength, log_decay, window_ids, kernel
    )
    within, query_decayed, targets, corrector, transition, increment = block_terms
    heads_here, block_count = transition.shape[:2]
    prefix_map = jnp.broadcast_to(jnp.eye(DK, dtype=jnp.float32), (heads_here, DK, DK))
    prefix_shift = jnp.zeros((heads_here, DK, DV), jnp.float32)
    prefix_maps, prefix_shifts = ([], [])
    for block in range(block_count):
        prefix_maps.append(prefix_map)
        prefix_shifts.append(prefix_shift)
        prefix_map = batched(transition[:, block], prefix_map)
        prefix_shift = batched(transition[:, block], prefix_shift) + increment[:, block]
    stacked_maps = jnp.stack(prefix_maps, axis=1)
    stacked_shifts = jnp.stack(prefix_shifts, axis=1)
    query_effective = query_decayed - blockwise(within, corrector)
    through_entry = blockwise(query_effective, stacked_maps)
    fixed_part = blockwise(query_effective, stacked_shifts) + blockwise(within, targets)
    entering = scanned_entry(prefix_map, prefix_shift, CTX)
    emitted = (
        jnp.einsum("hbtk,hkv->hbtv", through_entry, entering, precision=HIGHEST) + fixed_part
    )
    mixed_heads = jnp.transpose(emitted, (1, 2, 0, 3)).reshape(-1, heads_here, DV)
    gated_out = gate_output(mixed_heads, gate_raw, norm_gain)
    partial_out = jnp.dot(gated_out, out_weight, preferred_element_type=jnp.float32)
    pairs = lax.axis_size("head")
    if pairs == 2:
        side = lax.axis_index("head")
        halves = partial_out.reshape(2, -1, partial_out.shape[1])
        kept = lax.dynamic_index_in_dim(halves, side, keepdims=False)
        given = lax.dynamic_index_in_dim(halves, 1 - side, keepdims=False)
        attention = kept + lax.ppermute(
            given.astype(jnp.bfloat16), "head", [(0, 1), (1, 0)]
        ).astype(jnp.float32)
    else:
        attention = lax.psum_scatter(
            partial_out.astype(jnp.bfloat16), "head", scatter_dimension=0, tiled=True
        ).astype(jnp.float32)
    hidden = (residual.astype(jnp.float32) + attention).astype(jnp.bfloat16)
    expert_in = post_norm(hidden, post_gain)
    levels = lax.axis_size("ctx_hi")
    level = lax.axis_index("ctx_hi")
    local_experts = expert_up.shape[0]
    per_level = lax.axis_size("ctx_lo") * lax.axis_size("head") * local_experts
    experts_all = levels * per_level
    local_rows = routes.shape[0]
    top_count = routes.shape[1]
    capacity = local_rows * top_count * 5 // (4 * experts_all)
    own_high = route_weights.astype(jnp.bfloat16)
    own_low = (route_weights - own_high.astype(jnp.float32)).astype(jnp.bfloat16)
    spare = -(-(3 * top_count) // 128) * 128 - 3 * top_count
    packed = jnp.concatenate(
        [
            expert_in,
            routes.astype(jnp.bfloat16),
            own_high,
            own_low,
            jnp.zeros((local_rows, spare), jnp.bfloat16),
        ],
        axis=1,
    )
    gathered = lax.all_gather(packed, "ctx_hi").reshape(levels * local_rows, -1)
    gathered_in = gathered[:, :D]
    gathered_routes = gathered[:, D : D + top_count].astype(jnp.int32)
    gathered_high = gathered[:, D + top_count : D + 2 * top_count]
    gathered_low = gathered[:, D + 2 * top_count : D + 3 * top_count]
    expert_ids = jnp.arange(experts_all, dtype=jnp.int32)
    row_hot = jnp.any(gathered_routes[:, :, None] == expert_ids[None, None, :], axis=1)
    row_hot = row_hot.reshape(levels, local_rows, experts_all).astype(jnp.bfloat16)
    earlier_rows = (
        lax.broadcasted_iota(jnp.int32, (local_rows, local_rows), 0)
        > lax.broadcasted_iota(jnp.int32, (local_rows, local_rows), 1)
    ).astype(jnp.bfloat16)
    earlier = jnp.einsum(
        "ij,sje->sie", earlier_rows, row_hot, preferred_element_type=jnp.float32
    ).reshape(levels * local_rows, 1, experts_all)
    slot_rank = jnp.sum(
        jnp.where(gathered_routes[:, :, None] == expert_ids[None, None, :], earlier, 0.0), axis=2
    ).astype(jnp.int32)
    gathered_routes = gathered_routes.reshape(levels, local_rows * top_count)
    slot_rank = slot_rank.reshape(levels, local_rows * top_count)
    source = lax.broadcasted_iota(jnp.int32, gathered_routes.shape, 0)
    within = gathered_routes % per_level
    slot_index = jnp.where(
        gathered_routes // per_level == level, (within * levels + source) * capacity + slot_rank, -1
    )
    slots_total = per_level * levels * capacity
    chosen_slots = slot_index.reshape(levels * local_rows, top_count)
    slot_ids = jnp.arange(slots_total, dtype=jnp.int32)
    hits = chosen_slots[:, :, None] == slot_ids[None, None, :]
    picker = jnp.any(hits, axis=1).astype(jnp.bfloat16)
    outgoing = lax.dot_general(
        picker, gathered_in, (((0,), (0,)), ((), ())), preferred_element_type=jnp.float32
    ).astype(jnp.bfloat16)
    level_axes = ("ctx_lo", "head")
    outgoing = outgoing.reshape(per_level // local_experts, local_experts * levels * capacity, D)
    arrived = lax.all_to_all(outgoing, level_axes, split_axis=0, concat_axis=0, tiled=True)
    arrived = arrived.reshape(per_level // local_experts, local_experts, levels * capacity, D)
    answered = jnp.stack(
        [
            expert_apply_rows(
                arrived[:, member].reshape(-1, D), expert_up[member], expert_down[member]
            ).reshape(arrived.shape[0], levels * capacity, D)
            for member in range(local_experts)
        ],
        axis=1,
    ).reshape(per_level // local_experts, local_experts * levels * capacity, D)
    returned = lax.all_to_all(answered, level_axes, split_axis=0, concat_axis=0, tiled=True)
    result_rows = returned.reshape(slots_total, D)
    weight_high = jnp.sum(jnp.where(hits, gathered_high[:, :, None], 0.0), axis=1).astype(
        jnp.bfloat16
    )
    weight_low = jnp.sum(jnp.where(hits, gathered_low[:, :, None], 0.0), axis=1).astype(
        jnp.bfloat16
    )
    partial = jnp.dot(weight_high, result_rows, preferred_element_type=jnp.float32) + jnp.dot(
        weight_low, result_rows, preferred_element_type=jnp.float32
    )
    routed = lax.psum_scatter(
        partial.astype(jnp.bfloat16), "ctx_hi", scatter_dimension=0, tiled=True
    ).astype(jnp.float32)
    combined = hidden.astype(jnp.float32) + routed
    return combined.astype(jnp.bfloat16)


def split_mesh(mesh):
    groups, peers, pairs = (mesh.shape["group"], mesh.shape["ctx"], mesh.shape["head"])
    low = 4 if peers % 4 == 0 else 1
    devices = mesh.devices.reshape(groups, peers // low, low, pairs)
    return Mesh(devices, ("group", "ctx_hi", "ctx_lo", "head"))


def solution(mesh):
    return jax.shard_map(
        per_device,
        mesh=split_mesh(mesh),
        in_specs=(
            P(("group", "ctx_hi", "ctx_lo"), None, "head"),
            P(("group", "ctx_hi", "ctx_lo"), "head"),
            P(("group", "ctx_hi", "ctx_lo"), "head"),
            P(("group", "ctx_hi", "ctx_lo"), "head"),
            P(("group", "ctx_hi", "ctx_lo"), "head"),
            P("group"),
            P(None, None, "head"),
            P(None, "head"),
            P(),
            P("head", None),
            P(("group", "ctx_hi", "ctx_lo", "head"), None),
            P(),
            P(("group", "ctx_hi", "ctx_lo", "head"), None),
            P(("group", "ctx_hi", "ctx_lo", "head"), None),
            P(("ctx_hi", "ctx_lo", "head"), None, None),
            P(("ctx_hi", "ctx_lo", "head"), None, None),
        ),
        out_specs=P(("group", "ctx_hi", "ctx_lo", "head"), None),
        check_vma=False,
    )
```

```python
import jax
import jax.numpy as jnp
from jax import lax
from jax.sharding import Mesh, PartitionSpec as P

D = 2048
DK = 128
DV = 128
BLOCK = 64
CTX = ("ctx_hi", "ctx_lo")


HIGHEST = lax.Precision.HIGHEST


def passed_along(block, axis, distance):
    devices = range(lax.axis_size(axis))
    route = [(i - distance, i) for i in devices if i - distance in devices]
    return lax.ppermute(block, axis, route)


def scanned_entry(whole_map, whole_shift, axis):
    peers, position = (lax.axis_size(axis), lax.axis_index(axis))
    distance = 1
    while distance < peers:
        last = 2 * distance >= peers
        shift_in = passed_along(whole_shift.astype(jnp.bfloat16), axis, distance).astype(jnp.float32)
        reached = position >= distance
        new_shift = batched(whole_map, shift_in) + whole_shift
        if not last:
            map_in = passed_along(whole_map.astype(jnp.bfloat16), axis, distance).astype(jnp.float32)
            whole_map = jnp.where(reached, batched(whole_map, map_in), whole_map)
        whole_shift = jnp.where(reached, new_shift, whole_shift)
        distance *= 2
    return passed_along(whole_shift.astype(jnp.bfloat16), axis, 1).astype(jnp.float32)


def precise_dot(left, right):
    return jnp.dot(left, right, precision=HIGHEST, preferred_element_type=jnp.float32)


def causal_filter(padded_raw, filter_taps, padded_ids, kernel):
    length = padded_raw.shape[0] - (kernel - 1)
    source = padded_raw.astype(jnp.float32)
    current_ids = padded_ids[kernel - 1 :]
    summed = jnp.zeros((length, padded_raw.shape[1]), jnp.float32)
    for lag_step in range(kernel):
        offset_start = kernel - 1 - lag_step
        shifted = source[offset_start : offset_start + length]
        matching = (padded_ids[offset_start : offset_start + length] == current_ids).astype(
            jnp.float32
        )
        summed = summed + filter_taps[lag_step] * shifted * matching[:, None]
    return jax.nn.silu(summed)


def unit_rows(values_in):
    return values_in / jnp.sqrt(jnp.sum(values_in * values_in, axis=-1, keepdims=True) + 1e-06)


def mixer_inputs(pair_padded, value_padded, pair_filter, value_filter, padded_ids, kernel):
    pair_act = causal_filter(pair_padded, pair_filter.reshape(kernel, -1), padded_ids, kernel)
    length = pair_act.shape[0]
    pair_heads = pair_act.reshape(length, 2, -1, DK)
    queries = unit_rows(pair_heads[:, 0]) * DK ** (-0.5)
    key_rows = unit_rows(pair_heads[:, 1])
    value_rows = causal_filter(value_padded, value_filter, padded_ids, kernel).reshape(
        length, -1, DV
    )
    repeat_factor = value_rows.shape[1] // key_rows.shape[1]
    return (
        jnp.repeat(queries, repeat_factor, axis=1),
        jnp.repeat(key_rows, repeat_factor, axis=1),
        value_rows,
    )


def unit_lower_inverse(system):
    size = system.shape[-1]
    row_index = lax.broadcasted_iota(jnp.int32, (size, size), 0)
    col_index = lax.broadcasted_iota(jnp.int32, (size, size), 1)
    inverse = jnp.broadcast_to(jnp.eye(size, dtype=system.dtype), system.shape)
    width = 1
    while width < size:
        linking = (
            (row_index // (2 * width) == col_index // (2 * width))
            & ((row_index // width) % 2 == 1)
            & ((col_index // width) % 2 == 0)
        )
        lower_left = jnp.where(linking, system, 0.0)
        inverse = inverse - precise_dot(inverse, precise_dot(lower_left, inverse))
        width *= 2
    return inverse


def block_setup(queries, key_rows, value_rows, strength, decay_rows, segment_here, prior_id):
    cumulative = jnp.cumsum(decay_rows)
    row_index = lax.broadcasted_iota(jnp.int32, (BLOCK, BLOCK), 0)
    col_index = lax.broadcasted_iota(jnp.int32, (BLOCK, BLOCK), 1)
    same_segment = segment_here[:, None] == segment_here[None, :]
    causal = (row_index >= col_index) & same_segment
    strictly = (row_index > col_index) & same_segment
    decay_matrix = jnp.where(
        causal, jnp.exp(jnp.where(causal, cumulative[:, None] - cumulative[None, :], 0.0)), 0.0
    )
    carried_in = (segment_here == prior_id).astype(jnp.float32)
    keyed_beta = key_rows * strength[:, None]
    coupling = jnp.where(strictly, precise_dot(keyed_beta, key_rows.T) * decay_matrix, 0.0)
    system = jnp.eye(BLOCK, dtype=jnp.float32) + coupling
    stacked = jnp.concatenate(
        [value_rows * strength[:, None], keyed_beta * (jnp.exp(cumulative) * carried_in)[:, None]],
        axis=1,
    )
    solved = precise_dot(unit_lower_inverse(system), stacked)
    targets = solved[:, :DV]
    corrector = solved[:, DV:]
    within = jnp.where(causal, precise_dot(queries, key_rows.T) * decay_matrix, 0.0)
    query_decayed = queries * (jnp.exp(cumulative) * carried_in)[:, None]
    final_log = cumulative[BLOCK - 1]
    weighting = (segment_here == segment_here[BLOCK - 1]).astype(jnp.float32) * jnp.exp(
        final_log - cumulative
    )
    keys_weighted = key_rows * weighting[:, None]
    transition = jnp.exp(final_log) * carried_in[BLOCK - 1] * jnp.eye(
        DK, dtype=jnp.float32
    ) - precise_dot(keys_weighted.T, corrector)
    increment = precise_dot(keys_weighted.T, targets)
    return (within, query_decayed, targets, corrector, transition, increment)


def head_major(array_in, block_count):
    moved = jnp.moveaxis(array_in, 1, 0)
    return moved.reshape((array_in.shape[1], block_count, BLOCK) + array_in.shape[2:])


def block_tables(queries, key_rows, value_rows, strength, decay_rows, padded_ids, kernel):
    length = queries.shape[0]
    block_count = length // BLOCK
    current_ids = padded_ids[kernel - 1 :].reshape(block_count, BLOCK)
    prior_ids = padded_ids[kernel - 2 : kernel - 2 + length : BLOCK]
    per_block = jax.vmap(block_setup, in_axes=(0, 0, 0, 0, 0, 0, 0))
    per_head = jax.vmap(per_block, in_axes=(0, 0, 0, 0, 0, None, None))
    return per_head(
        head_major(queries, block_count),
        head_major(key_rows, block_count),
        head_major(value_rows, block_count),
        head_major(strength, block_count),
        head_major(decay_rows, block_count),
        current_ids,
        prior_ids,
    )


def blockwise(left, right):
    return jnp.einsum("hbij,hbjk->hbik", left, right, precision=HIGHEST)


def batched(left, right):
    return jnp.einsum("hij,hjk->hik", left, right, precision=HIGHEST)


def sweep_blocks(block_terms, start_state):
    blocks_first = tuple((jnp.swapaxes(member, 0, 1) for member in block_terms))

    def advance(carry_state, pieces):
        within, query_decayed, targets, corrector, transition, increment = pieces
        fresh_values = targets - batched(corrector, carry_state)
        emitted = batched(query_decayed, carry_state) + batched(within, fresh_values)
        updated = batched(transition, carry_state) + increment
        return (updated, emitted)

    final_state, emitted = lax.scan(advance, start_state, blocks_first)
    return emitted


def tokens_first(emitted):
    heads_count = emitted.shape[1]
    return jnp.transpose(emitted, (0, 2, 1, 3)).reshape(-1, heads_count, emitted.shape[3])


def gate_output(mixed_heads, gate_raw, norm_gain):
    square_mean = jnp.mean(mixed_heads * mixed_heads, axis=-1, keepdims=True)
    gate_values = jax.nn.silu(gate_raw.reshape(mixed_heads.shape).astype(jnp.float32))
    normed = mixed_heads / jnp.sqrt(square_mean + 1e-06) * norm_gain * gate_values
    return normed.astype(jnp.bfloat16).reshape(mixed_heads.shape[0], -1)


def post_norm(hidden, post_gain):
    hidden_full = hidden.astype(jnp.float32)
    square_mean = jnp.mean(hidden_full * hidden_full, axis=-1, keepdims=True)
    return (hidden_full / jnp.sqrt(square_mean + 1e-06) * post_gain).astype(jnp.bfloat16)


def expert_apply_rows(rows_in, up_matrix, down_matrix):
    hidden_units = down_matrix.shape[0]
    gate_up = jnp.dot(rows_in, up_matrix, preferred_element_type=jnp.float32)
    activated = (jax.nn.silu(gate_up[:, :hidden_units]) * gate_up[:, hidden_units:]).astype(
        jnp.bfloat16
    )
    return jnp.dot(activated, down_matrix, preferred_element_type=jnp.float32).astype(jnp.bfloat16)


def expert_apply(arrived, expert_up, expert_down):
    member_rows = arrived[:, 0]
    flattened = member_rows.reshape(-1, member_rows.shape[-1])
    result = expert_apply_rows(flattened, expert_up[0], expert_down[0])
    outputs = [result.reshape(member_rows.shape)]
    return jnp.stack(outputs, axis=1)


def route_slots(routes, experts_all, capacity):
    assigned = routes.reshape(-1)
    expert_ids = jnp.arange(experts_all, dtype=jnp.int32)
    onehot = (assigned[:, None] == expert_ids[None, :]).astype(jnp.int32)
    slot_rank = jnp.sum((jnp.cumsum(onehot, axis=0) - 1) * onehot, axis=1)
    return assigned * capacity + slot_rank


def per_device(
    pair_raw,
    value_raw,
    gate_raw,
    write_strength,
    log_decay,
    segment_ids,
    pair_filter,
    value_filter,
    norm_gain,
    out_weight,
    residual,
    post_gain,
    routes,
    route_weights,
    expert_up,
    expert_down,
):
    local_tokens = pair_raw.shape[0]
    kernel = value_filter.shape[0]
    pair_flat = pair_raw.reshape(local_tokens, -1)
    pair_width = pair_flat.shape[1]
    rim_rows = jnp.concatenate(
        [pair_flat[local_tokens - (kernel - 1) :], value_raw[local_tokens - (kernel - 1) :]], axis=1
    )
    before = passed_along(rim_rows, CTX, 1)
    first_token = lax.axis_index(CTX) * local_tokens
    padded_ids = jnp.concatenate([jnp.full((kernel - 1,), -1, jnp.int32), segment_ids])
    window_ids = lax.dynamic_slice_in_dim(padded_ids, first_token, local_tokens + kernel - 1)
    pair_padded = jnp.concatenate([before[:, :pair_width], pair_flat])
    value_padded = jnp.concatenate([before[:, pair_width:], value_raw])
    queries, key_rows, value_rows = mixer_inputs(
        pair_padded, value_padded, pair_filter, value_filter, window_ids, kernel
    )
    block_terms = block_tables(
        queries, key_rows, value_rows, write_strength, log_decay, window_ids, kernel
    )
    within, query_decayed, targets, corrector, transition, increment = block_terms
    heads_here, block_count = transition.shape[:2]
    prefix_map = jnp.broadcast_to(jnp.eye(DK, dtype=jnp.float32), (heads_here, DK, DK))
    prefix_shift = jnp.zeros((heads_here, DK, DV), jnp.float32)
    prefix_maps, prefix_shifts = ([], [])
    for block in range(block_count):
        prefix_maps.append(prefix_map)
        prefix_shifts.append(prefix_shift)
        prefix_map = batched(transition[:, block], prefix_map)
        prefix_shift = batched(transition[:, block], prefix_shift) + increment[:, block]
    stacked_maps = jnp.stack(prefix_maps, axis=1)
    stacked_shifts = jnp.stack(prefix_shifts, axis=1)
    query_effective = query_decayed - blockwise(within, corrector)
    through_entry = blockwise(query_effective, stacked_maps)
    fixed_part = blockwise(query_effective, stacked_shifts) + blockwise(within, targets)
    entering = scanned_entry(prefix_map, prefix_shift, CTX)
    emitted = (
        jnp.einsum("hbtk,hkv->hbtv", through_entry, entering, precision=HIGHEST) + fixed_part
    )
    mixed_heads = jnp.transpose(emitted, (1, 2, 0, 3)).reshape(-1, heads_here, DV)
    gated_out = gate_output(mixed_heads, gate_raw, norm_gain)
    partial_out = jnp.dot(gated_out, out_weight, preferred_element_type=jnp.float32)
    pairs = lax.axis_size("head")
    if pairs == 2:
        side = lax.axis_index("head")
        halves = partial_out.reshape(2, -1, partial_out.shape[1])
        kept = lax.dynamic_index_in_dim(halves, side, keepdims=False)
        given = lax.dynamic_index_in_dim(halves, 1 - side, keepdims=False)
        attention = kept + lax.ppermute(
            given.astype(jnp.bfloat16), "head", [(0, 1), (1, 0)]
        ).astype(jnp.float32)
    else:
        attention = lax.psum_scatter(
            partial_out.astype(jnp.bfloat16), "head", scatter_dimension=0, tiled=True
        ).astype(jnp.float32)
    hidden = (residual.astype(jnp.float32) + attention).astype(jnp.bfloat16)
    expert_in = post_norm(hidden, post_gain)
    levels = lax.axis_size("ctx_hi")
    level = lax.axis_index("ctx_hi")
    local_experts = expert_up.shape[0]
    per_level = lax.axis_size("ctx_lo") * lax.axis_size("head") * local_experts
    experts_all = levels * per_level
    local_rows = routes.shape[0]
    top_count = routes.shape[1]
    capacity = local_rows * top_count * 5 // (4 * experts_all)
    own_high = route_weights.astype(jnp.bfloat16)
    own_low = (route_weights - own_high.astype(jnp.float32)).astype(jnp.bfloat16)
    spare = -(-(3 * top_count) // 128) * 128 - 3 * top_count
    packed = jnp.concatenate(
        [
            expert_in,
            routes.astype(jnp.bfloat16),
            own_high,
            own_low,
            jnp.zeros((local_rows, spare), jnp.bfloat16),
        ],
        axis=1,
    )
    expert_ids = jnp.arange(experts_all, dtype=jnp.int32)
    earlier_rows = (
        lax.broadcasted_iota(jnp.int32, (local_rows, local_rows), 0)
        > lax.broadcasted_iota(jnp.int32, (local_rows, local_rows), 1)
    ).astype(jnp.bfloat16)
    slots_total = per_level * capacity
    slot_ids = jnp.arange(slots_total, dtype=jnp.int32)
    level_axes = ("ctx_lo", "head")
    routed = None
    for turn in range(levels):
        if turn == 0:
            chunk = packed
        else:
            chunk = lax.ppermute(
                packed, "ctx_hi", [(i, (i - turn) % levels) for i in range(levels)]
            )
        chunk_in = chunk[:, :D]
        chunk_routes = chunk[:, D : D + top_count].astype(jnp.int32)
        chunk_high = chunk[:, D + top_count : D + 2 * top_count]
        chunk_low = chunk[:, D + 2 * top_count : D + 3 * top_count]
        route_hot = chunk_routes[:, :, None] == expert_ids[None, None, :]
        row_hot = jnp.any(route_hot, axis=1).astype(jnp.bfloat16)
        earlier = jnp.dot(earlier_rows, row_hot, preferred_element_type=jnp.float32)
        slot_rank = jnp.sum(jnp.where(route_hot, earlier[:, None, :], 0.0), axis=2).astype(
            jnp.int32
        )
        slot_index = jnp.where(
            chunk_routes // per_level == level,
            (chunk_routes % per_level) * capacity + slot_rank,
            -1,
        )
        hits = slot_index[:, :, None] == slot_ids[None, None, :]
        picker = jnp.any(hits, axis=1).astype(jnp.bfloat16)
        outgoing = lax.dot_general(
            picker, chunk_in, (((0,), (0,)), ((), ())), preferred_element_type=jnp.float32
        ).astype(jnp.bfloat16)
        outgoing = outgoing.reshape(per_level // local_experts, local_experts * capacity, D)
        arrived = lax.all_to_all(outgoing, level_axes, split_axis=0, concat_axis=0, tiled=True)
        arrived = arrived.reshape(per_level // local_experts, local_experts, capacity, D)
        answered = jnp.stack(
            [
                expert_apply_rows(
                    arrived[:, member].reshape(-1, D), expert_up[member], expert_down[member]
                ).reshape(arrived.shape[0], capacity, D)
                for member in range(local_experts)
            ],
            axis=1,
        ).reshape(per_level // local_experts, local_experts * capacity, D)
        returned = lax.all_to_all(answered, level_axes, split_axis=0, concat_axis=0, tiled=True)
        result_rows = returned.reshape(slots_total, D)
        weight_high = jnp.sum(jnp.where(hits, chunk_high[:, :, None], 0.0), axis=1).astype(
            jnp.bfloat16
        )
        weight_low = jnp.sum(jnp.where(hits, chunk_low[:, :, None], 0.0), axis=1).astype(
            jnp.bfloat16
        )
        partial = jnp.dot(weight_high, result_rows, preferred_element_type=jnp.float32) + jnp.dot(
            weight_low, result_rows, preferred_element_type=jnp.float32
        )
        if turn == 0:
            routed = partial
        else:
            routed = routed + lax.ppermute(
                partial.astype(jnp.bfloat16),
                "ctx_hi",
                [(i, (i + turn) % levels) for i in range(levels)],
            ).astype(jnp.float32)
    combined = hidden.astype(jnp.float32) + routed
    return combined.astype(jnp.bfloat16)


def split_mesh(mesh):
    groups, peers, pairs = (mesh.shape["group"], mesh.shape["ctx"], mesh.shape["head"])
    low = 4 if peers % 4 == 0 else 1
    devices = mesh.devices.reshape(groups, peers // low, low, pairs)
    return Mesh(devices, ("group", "ctx_hi", "ctx_lo", "head"))


def solution(mesh):
    return jax.shard_map(
        per_device,
        mesh=split_mesh(mesh),
        in_specs=(
            P(("group", "ctx_hi", "ctx_lo"), None, "head"),
            P(("group", "ctx_hi", "ctx_lo"), "head"),
            P(("group", "ctx_hi", "ctx_lo"), "head"),
            P(("group", "ctx_hi", "ctx_lo"), "head"),
            P(("group", "ctx_hi", "ctx_lo"), "head"),
            P("group"),
            P(None, None, "head"),
            P(None, "head"),
            P(),
            P("head", None),
            P(("group", "ctx_hi", "ctx_lo", "head"), None),
            P(),
            P(("group", "ctx_hi", "ctx_lo", "head"), None),
            P(("group", "ctx_hi", "ctx_lo", "head"), None),
            P(("ctx_hi", "ctx_lo", "head"), None, None),
            P(("ctx_hi", "ctx_lo", "head"), None, None),
        ),
        out_specs=P(("group", "ctx_hi", "ctx_lo", "head"), None),
        check_vma=False,
    )
```

```python
import jax
import jax.numpy as jnp
from jax import lax
from jax.sharding import Mesh, PartitionSpec as P

D = 2048
DK = 128
DV = 128
BLOCK = 64
CTX = ("ctx_hi", "ctx_lo")


HIGHEST = lax.Precision.HIGHEST


def passed_along(block, axis, distance):
    devices = range(lax.axis_size(axis))
    route = [(i - distance, i) for i in devices if i - distance in devices]
    return lax.ppermute(block, axis, route)


def scanned_entry(whole_map, whole_shift, axis):
    peers, position = (lax.axis_size(axis), lax.axis_index(axis))
    distance = 1
    while distance < peers:
        last = 2 * distance >= peers
        shift_in = passed_along(whole_shift.astype(jnp.bfloat16), axis, distance).astype(jnp.float32)
        reached = position >= distance
        new_shift = batched(whole_map, shift_in) + whole_shift
        if not last:
            map_in = passed_along(whole_map.astype(jnp.bfloat16), axis, distance).astype(jnp.float32)
            whole_map = jnp.where(reached, batched(whole_map, map_in), whole_map)
        whole_shift = jnp.where(reached, new_shift, whole_shift)
        distance *= 2
    return passed_along(whole_shift.astype(jnp.bfloat16), axis, 1).astype(jnp.float32)


def precise_dot(left, right):
    return jnp.dot(left, right, precision=HIGHEST, preferred_element_type=jnp.float32)


def causal_filter(padded_raw, filter_taps, padded_ids, kernel):
    length = padded_raw.shape[0] - (kernel - 1)
    source = padded_raw.astype(jnp.float32)
    current_ids = padded_ids[kernel - 1 :]
    summed = jnp.zeros((length, padded_raw.shape[1]), jnp.float32)
    for lag_step in range(kernel):
        offset_start = kernel - 1 - lag_step
        shifted = source[offset_start : offset_start + length]
        matching = (padded_ids[offset_start : offset_start + length] == current_ids).astype(
            jnp.float32
        )
        summed = summed + filter_taps[lag_step] * shifted * matching[:, None]
    return jax.nn.silu(summed)


def unit_rows(values_in):
    return values_in / jnp.sqrt(jnp.sum(values_in * values_in, axis=-1, keepdims=True) + 1e-06)


def mixer_inputs(pair_padded, value_padded, pair_filter, value_filter, padded_ids, kernel):
    pair_act = causal_filter(pair_padded, pair_filter.reshape(kernel, -1), padded_ids, kernel)
    length = pair_act.shape[0]
    pair_heads = pair_act.reshape(length, 2, -1, DK)
    queries = unit_rows(pair_heads[:, 0]) * DK ** (-0.5)
    key_rows = unit_rows(pair_heads[:, 1])
    value_rows = causal_filter(value_padded, value_filter, padded_ids, kernel).reshape(
        length, -1, DV
    )
    repeat_factor = value_rows.shape[1] // key_rows.shape[1]
    return (
        jnp.repeat(queries, repeat_factor, axis=1),
        jnp.repeat(key_rows, repeat_factor, axis=1),
        value_rows,
    )


def unit_lower_inverse(system):
    size = system.shape[-1]
    row_index = lax.broadcasted_iota(jnp.int32, (size, size), 0)
    col_index = lax.broadcasted_iota(jnp.int32, (size, size), 1)
    inverse = jnp.broadcast_to(jnp.eye(size, dtype=system.dtype), system.shape)
    width = 1
    while width < size:
        linking = (
            (row_index // (2 * width) == col_index // (2 * width))
            & ((row_index // width) % 2 == 1)
            & ((col_index // width) % 2 == 0)
        )
        lower_left = jnp.where(linking, system, 0.0)
        inverse = inverse - precise_dot(inverse, precise_dot(lower_left, inverse))
        width *= 2
    return inverse


def block_setup(queries, key_rows, value_rows, strength, decay_rows, segment_here, prior_id):
    cumulative = jnp.cumsum(decay_rows)
    row_index = lax.broadcasted_iota(jnp.int32, (BLOCK, BLOCK), 0)
    col_index = lax.broadcasted_iota(jnp.int32, (BLOCK, BLOCK), 1)
    same_segment = segment_here[:, None] == segment_here[None, :]
    causal = (row_index >= col_index) & same_segment
    strictly = (row_index > col_index) & same_segment
    decay_matrix = jnp.where(
        causal, jnp.exp(jnp.where(causal, cumulative[:, None] - cumulative[None, :], 0.0)), 0.0
    )
    carried_in = (segment_here == prior_id).astype(jnp.float32)
    keyed_beta = key_rows * strength[:, None]
    coupling = jnp.where(strictly, precise_dot(keyed_beta, key_rows.T) * decay_matrix, 0.0)
    system = jnp.eye(BLOCK, dtype=jnp.float32) + coupling
    stacked = jnp.concatenate(
        [value_rows * strength[:, None], keyed_beta * (jnp.exp(cumulative) * carried_in)[:, None]],
        axis=1,
    )
    solved = precise_dot(unit_lower_inverse(system), stacked)
    targets = solved[:, :DV]
    corrector = solved[:, DV:]
    within = jnp.where(causal, precise_dot(queries, key_rows.T) * decay_matrix, 0.0)
    query_decayed = queries * (jnp.exp(cumulative) * carried_in)[:, None]
    final_log = cumulative[BLOCK - 1]
    weighting = (segment_here == segment_here[BLOCK - 1]).astype(jnp.float32) * jnp.exp(
        final_log - cumulative
    )
    keys_weighted = key_rows * weighting[:, None]
    transition = jnp.exp(final_log) * carried_in[BLOCK - 1] * jnp.eye(
        DK, dtype=jnp.float32
    ) - precise_dot(keys_weighted.T, corrector)
    increment = precise_dot(keys_weighted.T, targets)
    return (within, query_decayed, targets, corrector, transition, increment)


def head_major(array_in, block_count):
    moved = jnp.moveaxis(array_in, 1, 0)
    return moved.reshape((array_in.shape[1], block_count, BLOCK) + array_in.shape[2:])


def block_tables(queries, key_rows, value_rows, strength, decay_rows, padded_ids, kernel):
    length = queries.shape[0]
    block_count = length // BLOCK
    current_ids = padded_ids[kernel - 1 :].reshape(block_count, BLOCK)
    prior_ids = padded_ids[kernel - 2 : kernel - 2 + length : BLOCK]
    per_block = jax.vmap(block_setup, in_axes=(0, 0, 0, 0, 0, 0, 0))
    per_head = jax.vmap(per_block, in_axes=(0, 0, 0, 0, 0, None, None))
    return per_head(
        head_major(queries, block_count),
        head_major(key_rows, block_count),
        head_major(value_rows, block_count),
        head_major(strength, block_count),
        head_major(decay_rows, block_count),
        current_ids,
        prior_ids,
    )


def blockwise(left, right):
    return jnp.einsum("hbij,hbjk->hbik", left, right, precision=HIGHEST)


def batched(left, right):
    return jnp.einsum("hij,hjk->hik", left, right, precision=HIGHEST)


def sweep_blocks(block_terms, start_state):
    blocks_first = tuple((jnp.swapaxes(member, 0, 1) for member in block_terms))

    def advance(carry_state, pieces):
        within, query_decayed, targets, corrector, transition, increment = pieces
        fresh_values = targets - batched(corrector, carry_state)
        emitted = batched(query_decayed, carry_state) + batched(within, fresh_values)
        updated = batched(transition, carry_state) + increment
        return (updated, emitted)

    final_state, emitted = lax.scan(advance, start_state, blocks_first)
    return emitted


def tokens_first(emitted):
    heads_count = emitted.shape[1]
    return jnp.transpose(emitted, (0, 2, 1, 3)).reshape(-1, heads_count, emitted.shape[3])


def gate_output(mixed_heads, gate_raw, norm_gain):
    square_mean = jnp.mean(mixed_heads * mixed_heads, axis=-1, keepdims=True)
    gate_values = jax.nn.silu(gate_raw.reshape(mixed_heads.shape).astype(jnp.float32))
    normed = mixed_heads / jnp.sqrt(square_mean + 1e-06) * norm_gain * gate_values
    return normed.astype(jnp.bfloat16).reshape(mixed_heads.shape[0], -1)


def post_norm(hidden, post_gain):
    hidden_full = hidden.astype(jnp.float32)
    square_mean = jnp.mean(hidden_full * hidden_full, axis=-1, keepdims=True)
    return (hidden_full / jnp.sqrt(square_mean + 1e-06) * post_gain).astype(jnp.bfloat16)


def expert_apply_rows(rows_in, up_matrix, down_matrix):
    hidden_units = down_matrix.shape[0]
    gate_up = jnp.dot(rows_in, up_matrix, preferred_element_type=jnp.float32)
    activated = (jax.nn.silu(gate_up[:, :hidden_units]) * gate_up[:, hidden_units:]).astype(
        jnp.bfloat16
    )
    return jnp.dot(activated, down_matrix, preferred_element_type=jnp.float32).astype(jnp.bfloat16)


def expert_apply(arrived, expert_up, expert_down):
    member_rows = arrived[:, 0]
    flattened = member_rows.reshape(-1, member_rows.shape[-1])
    result = expert_apply_rows(flattened, expert_up[0], expert_down[0])
    outputs = [result.reshape(member_rows.shape)]
    return jnp.stack(outputs, axis=1)


def level_pairs(levels, turn, back):
    if levels & (levels - 1) == 0:
        return [(i, i ^ turn) for i in range(levels)]
    if back:
        return [(i, (i + turn) % levels) for i in range(levels)]
    return [(i, (i - turn) % levels) for i in range(levels)]


def route_slots(routes, experts_all, capacity):
    assigned = routes.reshape(-1)
    expert_ids = jnp.arange(experts_all, dtype=jnp.int32)
    onehot = (assigned[:, None] == expert_ids[None, :]).astype(jnp.int32)
    slot_rank = jnp.sum((jnp.cumsum(onehot, axis=0) - 1) * onehot, axis=1)
    return assigned * capacity + slot_rank


def per_device(
    pair_raw,
    value_raw,
    gate_raw,
    write_strength,
    log_decay,
    segment_ids,
    pair_filter,
    value_filter,
    norm_gain,
    out_weight,
    residual,
    post_gain,
    routes,
    route_weights,
    expert_up,
    expert_down,
):
    local_tokens = pair_raw.shape[0]
    kernel = value_filter.shape[0]
    pair_flat = pair_raw.reshape(local_tokens, -1)
    pair_width = pair_flat.shape[1]
    rim_rows = jnp.concatenate(
        [pair_flat[local_tokens - (kernel - 1) :], value_raw[local_tokens - (kernel - 1) :]], axis=1
    )
    before = passed_along(rim_rows, CTX, 1)
    first_token = lax.axis_index(CTX) * local_tokens
    padded_ids = jnp.concatenate([jnp.full((kernel - 1,), -1, jnp.int32), segment_ids])
    window_ids = lax.dynamic_slice_in_dim(padded_ids, first_token, local_tokens + kernel - 1)
    pair_padded = jnp.concatenate([before[:, :pair_width], pair_flat])
    value_padded = jnp.concatenate([before[:, pair_width:], value_raw])
    queries, key_rows, value_rows = mixer_inputs(
        pair_padded, value_padded, pair_filter, value_filter, window_ids, kernel
    )
    block_terms = block_tables(
        queries, key_rows, value_rows, write_strength, log_decay, window_ids, kernel
    )
    within, query_decayed, targets, corrector, transition, increment = block_terms
    heads_here, block_count = transition.shape[:2]
    prefix_map = jnp.broadcast_to(jnp.eye(DK, dtype=jnp.float32), (heads_here, DK, DK))
    prefix_shift = jnp.zeros((heads_here, DK, DV), jnp.float32)
    prefix_maps, prefix_shifts = ([], [])
    for block in range(block_count):
        prefix_maps.append(prefix_map)
        prefix_shifts.append(prefix_shift)
        prefix_map = batched(transition[:, block], prefix_map)
        prefix_shift = batched(transition[:, block], prefix_shift) + increment[:, block]
    stacked_maps = jnp.stack(prefix_maps, axis=1)
    stacked_shifts = jnp.stack(prefix_shifts, axis=1)
    query_effective = query_decayed - blockwise(within, corrector)
    through_entry = blockwise(query_effective, stacked_maps)
    fixed_part = blockwise(query_effective, stacked_shifts) + blockwise(within, targets)
    entering = scanned_entry(prefix_map, prefix_shift, CTX)
    emitted = (
        jnp.einsum("hbtk,hkv->hbtv", through_entry, entering, precision=HIGHEST) + fixed_part
    )
    mixed_heads = jnp.transpose(emitted, (1, 2, 0, 3)).reshape(-1, heads_here, DV)
    gated_out = gate_output(mixed_heads, gate_raw, norm_gain)
    partial_out = jnp.dot(gated_out, out_weight, preferred_element_type=jnp.float32)
    pairs = lax.axis_size("head")
    if pairs == 2:
        side = lax.axis_index("head")
        halves = partial_out.reshape(2, -1, partial_out.shape[1])
        kept = lax.dynamic_index_in_dim(halves, side, keepdims=False)
        given = lax.dynamic_index_in_dim(halves, 1 - side, keepdims=False)
        attention = kept + lax.ppermute(
            given.astype(jnp.bfloat16), "head", [(0, 1), (1, 0)]
        ).astype(jnp.float32)
    else:
        attention = lax.psum_scatter(
            partial_out.astype(jnp.bfloat16), "head", scatter_dimension=0, tiled=True
        ).astype(jnp.float32)
    hidden = (residual.astype(jnp.float32) + attention).astype(jnp.bfloat16)
    expert_in = post_norm(hidden, post_gain)
    levels = lax.axis_size("ctx_hi")
    level = lax.axis_index("ctx_hi")
    local_experts = expert_up.shape[0]
    per_level = lax.axis_size("ctx_lo") * lax.axis_size("head") * local_experts
    experts_all = levels * per_level
    local_rows = routes.shape[0]
    top_count = routes.shape[1]
    capacity = local_rows * top_count * 5 // (4 * experts_all)
    own_high = route_weights.astype(jnp.bfloat16)
    own_low = (route_weights - own_high.astype(jnp.float32)).astype(jnp.bfloat16)
    spare = -(-(3 * top_count) // 128) * 128 - 3 * top_count
    packed = jnp.concatenate(
        [
            expert_in,
            routes.astype(jnp.bfloat16),
            own_high,
            own_low,
            jnp.zeros((local_rows, spare), jnp.bfloat16),
        ],
        axis=1,
    )
    expert_ids = jnp.arange(experts_all, dtype=jnp.int32)
    earlier_rows = (
        lax.broadcasted_iota(jnp.int32, (local_rows, local_rows), 0)
        > lax.broadcasted_iota(jnp.int32, (local_rows, local_rows), 1)
    ).astype(jnp.bfloat16)
    slots_total = per_level * capacity
    slot_ids = jnp.arange(slots_total, dtype=jnp.int32)
    level_axes = ("ctx_lo", "head")
    routed = None
    for turn in range(levels):
        if turn == 0:
            chunk = packed
        else:
            chunk = lax.ppermute(packed, "ctx_hi", level_pairs(levels, turn, False))
        chunk_in = chunk[:, :D]
        chunk_routes = chunk[:, D : D + top_count].astype(jnp.int32)
        chunk_high = chunk[:, D + top_count : D + 2 * top_count]
        chunk_low = chunk[:, D + 2 * top_count : D + 3 * top_count]
        route_hot = chunk_routes[:, :, None] == expert_ids[None, None, :]
        row_hot = jnp.any(route_hot, axis=1).astype(jnp.bfloat16)
        earlier = jnp.dot(earlier_rows, row_hot, preferred_element_type=jnp.float32)
        slot_rank = jnp.sum(jnp.where(route_hot, earlier[:, None, :], 0.0), axis=2).astype(
            jnp.int32
        )
        slot_index = jnp.where(
            chunk_routes // per_level == level,
            (chunk_routes % per_level) * capacity + slot_rank,
            -1,
        )
        hits = slot_index[:, :, None] == slot_ids[None, None, :]
        picker = jnp.any(hits, axis=1).astype(jnp.bfloat16)
        outgoing = lax.dot_general(
            picker, chunk_in, (((0,), (0,)), ((), ())), preferred_element_type=jnp.float32
        ).astype(jnp.bfloat16)
        outgoing = outgoing.reshape(per_level // local_experts, local_experts * capacity, D)
        arrived = lax.all_to_all(outgoing, level_axes, split_axis=0, concat_axis=0, tiled=True)
        arrived = arrived.reshape(per_level // local_experts, local_experts, capacity, D)
        answered = jnp.stack(
            [
                expert_apply_rows(
                    arrived[:, member].reshape(-1, D), expert_up[member], expert_down[member]
                ).reshape(arrived.shape[0], capacity, D)
                for member in range(local_experts)
            ],
            axis=1,
        ).reshape(per_level // local_experts, local_experts * capacity, D)
        returned = lax.all_to_all(answered, level_axes, split_axis=0, concat_axis=0, tiled=True)
        result_rows = returned.reshape(slots_total, D)
        weight_high = jnp.sum(jnp.where(hits, chunk_high[:, :, None], 0.0), axis=1).astype(
            jnp.bfloat16
        )
        weight_low = jnp.sum(jnp.where(hits, chunk_low[:, :, None], 0.0), axis=1).astype(
            jnp.bfloat16
        )
        partial = jnp.dot(weight_high, result_rows, preferred_element_type=jnp.float32) + jnp.dot(
            weight_low, result_rows, preferred_element_type=jnp.float32
        )
        if turn == 0:
            routed = partial
        else:
            routed = routed + lax.ppermute(
                partial.astype(jnp.bfloat16),
                "ctx_hi",
                level_pairs(levels, turn, True),
            ).astype(jnp.float32)
    combined = hidden.astype(jnp.float32) + routed
    return combined.astype(jnp.bfloat16)


def split_mesh(mesh):
    groups, peers, pairs = (mesh.shape["group"], mesh.shape["ctx"], mesh.shape["head"])
    low = 4 if peers % 4 == 0 else 1
    devices = mesh.devices.reshape(groups, peers // low, low, pairs)
    return Mesh(devices, ("group", "ctx_hi", "ctx_lo", "head"))


def solution(mesh):
    return jax.shard_map(
        per_device,
        mesh=split_mesh(mesh),
        in_specs=(
            P(("group", "ctx_hi", "ctx_lo"), None, "head"),
            P(("group", "ctx_hi", "ctx_lo"), "head"),
            P(("group", "ctx_hi", "ctx_lo"), "head"),
            P(("group", "ctx_hi", "ctx_lo"), "head"),
            P(("group", "ctx_hi", "ctx_lo"), "head"),
            P("group"),
            P(None, None, "head"),
            P(None, "head"),
            P(),
            P("head", None),
            P(("group", "ctx_hi", "ctx_lo", "head"), None),
            P(),
            P(("group", "ctx_hi", "ctx_lo", "head"), None),
            P(("group", "ctx_hi", "ctx_lo", "head"), None),
            P(("ctx_hi", "ctx_lo", "head"), None, None),
            P(("ctx_hi", "ctx_lo", "head"), None, None),
        ),
        out_specs=P(("group", "ctx_hi", "ctx_lo", "head"), None),
        check_vma=False,
    )
```

```python
import jax
import jax.numpy as jnp
from jax import lax
from jax.sharding import Mesh, PartitionSpec as P

D = 2048
DK = 128
DV = 128
BLOCK = 64
CTX = ("ctx_hi", "ctx_lo")


HIGHEST = lax.Precision.HIGHEST


def passed_along(block, axis, distance):
    devices = range(lax.axis_size(axis))
    route = [(i - distance, i) for i in devices if i - distance in devices]
    return lax.ppermute(block, axis, route)


def scanned_entry(whole_map, whole_shift, axis):
    peers, position = (lax.axis_size(axis), lax.axis_index(axis))
    distance = 1
    while distance < peers:
        last = 2 * distance >= peers
        reached = position >= distance
        if last:
            shift_in = passed_along(whole_shift.astype(jnp.bfloat16), axis, distance)
            shift_in = shift_in.astype(jnp.float32)
        else:
            both = jnp.stack([whole_map, whole_shift]).astype(jnp.bfloat16)
            both_in = passed_along(both, axis, distance).astype(jnp.float32)
            map_in, shift_in = (both_in[0], both_in[1])
        new_shift = batched(whole_map, shift_in) + whole_shift
        if not last:
            whole_map = jnp.where(reached, batched(whole_map, map_in), whole_map)
        whole_shift = jnp.where(reached, new_shift, whole_shift)
        distance *= 2
    return passed_along(whole_shift.astype(jnp.bfloat16), axis, 1).astype(jnp.float32)


def precise_dot(left, right):
    return jnp.dot(left, right, precision=HIGHEST, preferred_element_type=jnp.float32)


def causal_filter(padded_raw, filter_taps, padded_ids, kernel):
    length = padded_raw.shape[0] - (kernel - 1)
    source = padded_raw.astype(jnp.float32)
    current_ids = padded_ids[kernel - 1 :]
    summed = jnp.zeros((length, padded_raw.shape[1]), jnp.float32)
    for lag_step in range(kernel):
        offset_start = kernel - 1 - lag_step
        shifted = source[offset_start : offset_start + length]
        matching = (padded_ids[offset_start : offset_start + length] == current_ids).astype(
            jnp.float32
        )
        summed = summed + filter_taps[lag_step] * shifted * matching[:, None]
    return jax.nn.silu(summed)


def unit_rows(values_in):
    return values_in / jnp.sqrt(jnp.sum(values_in * values_in, axis=-1, keepdims=True) + 1e-06)


def mixer_inputs(pair_padded, value_padded, pair_filter, value_filter, padded_ids, kernel):
    pair_act = causal_filter(pair_padded, pair_filter.reshape(kernel, -1), padded_ids, kernel)
    length = pair_act.shape[0]
    pair_heads = pair_act.reshape(length, 2, -1, DK)
    queries = unit_rows(pair_heads[:, 0]) * DK ** (-0.5)
    key_rows = unit_rows(pair_heads[:, 1])
    value_rows = causal_filter(value_padded, value_filter, padded_ids, kernel).reshape(
        length, -1, DV
    )
    repeat_factor = value_rows.shape[1] // key_rows.shape[1]
    return (
        jnp.repeat(queries, repeat_factor, axis=1),
        jnp.repeat(key_rows, repeat_factor, axis=1),
        value_rows,
    )


def unit_lower_inverse(system):
    size = system.shape[-1]
    row_index = lax.broadcasted_iota(jnp.int32, (size, size), 0)
    col_index = lax.broadcasted_iota(jnp.int32, (size, size), 1)
    inverse = jnp.broadcast_to(jnp.eye(size, dtype=system.dtype), system.shape)
    width = 1
    while width < size:
        linking = (
            (row_index // (2 * width) == col_index // (2 * width))
            & ((row_index // width) % 2 == 1)
            & ((col_index // width) % 2 == 0)
        )
        lower_left = jnp.where(linking, system, 0.0)
        inverse = inverse - precise_dot(inverse, precise_dot(lower_left, inverse))
        width *= 2
    return inverse


def block_setup(queries, key_rows, value_rows, strength, decay_rows, segment_here, prior_id):
    cumulative = jnp.cumsum(decay_rows)
    row_index = lax.broadcasted_iota(jnp.int32, (BLOCK, BLOCK), 0)
    col_index = lax.broadcasted_iota(jnp.int32, (BLOCK, BLOCK), 1)
    same_segment = segment_here[:, None] == segment_here[None, :]
    causal = (row_index >= col_index) & same_segment
    strictly = (row_index > col_index) & same_segment
    decay_matrix = jnp.where(
        causal, jnp.exp(jnp.where(causal, cumulative[:, None] - cumulative[None, :], 0.0)), 0.0
    )
    carried_in = (segment_here == prior_id).astype(jnp.float32)
    keyed_beta = key_rows * strength[:, None]
    coupling = jnp.where(strictly, precise_dot(keyed_beta, key_rows.T) * decay_matrix, 0.0)
    system = jnp.eye(BLOCK, dtype=jnp.float32) + coupling
    stacked = jnp.concatenate(
        [value_rows * strength[:, None], keyed_beta * (jnp.exp(cumulative) * carried_in)[:, None]],
        axis=1,
    )
    solved = precise_dot(unit_lower_inverse(system), stacked)
    targets = solved[:, :DV]
    corrector = solved[:, DV:]
    within = jnp.where(causal, precise_dot(queries, key_rows.T) * decay_matrix, 0.0)
    query_decayed = queries * (jnp.exp(cumulative) * carried_in)[:, None]
    final_log = cumulative[BLOCK - 1]
    weighting = (segment_here == segment_here[BLOCK - 1]).astype(jnp.float32) * jnp.exp(
        final_log - cumulative
    )
    keys_weighted = key_rows * weighting[:, None]
    transition = jnp.exp(final_log) * carried_in[BLOCK - 1] * jnp.eye(
        DK, dtype=jnp.float32
    ) - precise_dot(keys_weighted.T, corrector)
    increment = precise_dot(keys_weighted.T, targets)
    return (within, query_decayed, targets, corrector, transition, increment)


def head_major(array_in, block_count):
    moved = jnp.moveaxis(array_in, 1, 0)
    return moved.reshape((array_in.shape[1], block_count, BLOCK) + array_in.shape[2:])


def block_tables(queries, key_rows, value_rows, strength, decay_rows, padded_ids, kernel):
    length = queries.shape[0]
    block_count = length // BLOCK
    current_ids = padded_ids[kernel - 1 :].reshape(block_count, BLOCK)
    prior_ids = padded_ids[kernel - 2 : kernel - 2 + length : BLOCK]
    per_block = jax.vmap(block_setup, in_axes=(0, 0, 0, 0, 0, 0, 0))
    per_head = jax.vmap(per_block, in_axes=(0, 0, 0, 0, 0, None, None))
    return per_head(
        head_major(queries, block_count),
        head_major(key_rows, block_count),
        head_major(value_rows, block_count),
        head_major(strength, block_count),
        head_major(decay_rows, block_count),
        current_ids,
        prior_ids,
    )


def blockwise(left, right):
    return jnp.einsum("hbij,hbjk->hbik", left, right, precision=HIGHEST)


def batched(left, right):
    return jnp.einsum("hij,hjk->hik", left, right, precision=HIGHEST)


def sweep_blocks(block_terms, start_state):
    blocks_first = tuple((jnp.swapaxes(member, 0, 1) for member in block_terms))

    def advance(carry_state, pieces):
        within, query_decayed, targets, corrector, transition, increment = pieces
        fresh_values = targets - batched(corrector, carry_state)
        emitted = batched(query_decayed, carry_state) + batched(within, fresh_values)
        updated = batched(transition, carry_state) + increment
        return (updated, emitted)

    final_state, emitted = lax.scan(advance, start_state, blocks_first)
    return emitted


def tokens_first(emitted):
    heads_count = emitted.shape[1]
    return jnp.transpose(emitted, (0, 2, 1, 3)).reshape(-1, heads_count, emitted.shape[3])


def gate_output(mixed_heads, gate_raw, norm_gain):
    square_mean = jnp.mean(mixed_heads * mixed_heads, axis=-1, keepdims=True)
    gate_values = jax.nn.silu(gate_raw.reshape(mixed_heads.shape).astype(jnp.float32))
    normed = mixed_heads / jnp.sqrt(square_mean + 1e-06) * norm_gain * gate_values
    return normed.astype(jnp.bfloat16).reshape(mixed_heads.shape[0], -1)


def post_norm(hidden, post_gain):
    hidden_full = hidden.astype(jnp.float32)
    square_mean = jnp.mean(hidden_full * hidden_full, axis=-1, keepdims=True)
    return (hidden_full / jnp.sqrt(square_mean + 1e-06) * post_gain).astype(jnp.bfloat16)


def expert_apply_rows(rows_in, up_matrix, down_matrix):
    hidden_units = down_matrix.shape[0]
    gate_up = jnp.dot(rows_in, up_matrix, preferred_element_type=jnp.float32)
    activated = (jax.nn.silu(gate_up[:, :hidden_units]) * gate_up[:, hidden_units:]).astype(
        jnp.bfloat16
    )
    return jnp.dot(activated, down_matrix, preferred_element_type=jnp.float32).astype(jnp.bfloat16)


def expert_apply(arrived, expert_up, expert_down):
    member_rows = arrived[:, 0]
    flattened = member_rows.reshape(-1, member_rows.shape[-1])
    result = expert_apply_rows(flattened, expert_up[0], expert_down[0])
    outputs = [result.reshape(member_rows.shape)]
    return jnp.stack(outputs, axis=1)


def route_slots(routes, experts_all, capacity):
    assigned = routes.reshape(-1)
    expert_ids = jnp.arange(experts_all, dtype=jnp.int32)
    onehot = (assigned[:, None] == expert_ids[None, :]).astype(jnp.int32)
    slot_rank = jnp.sum((jnp.cumsum(onehot, axis=0) - 1) * onehot, axis=1)
    return assigned * capacity + slot_rank


def per_device(
    pair_raw,
    value_raw,
    gate_raw,
    write_strength,
    log_decay,
    segment_ids,
    pair_filter,
    value_filter,
    norm_gain,
    out_weight,
    residual,
    post_gain,
    routes,
    route_weights,
    expert_up,
    expert_down,
):
    local_tokens = pair_raw.shape[0]
    kernel = value_filter.shape[0]
    pair_flat = pair_raw.reshape(local_tokens, -1)
    pair_width = pair_flat.shape[1]
    rim_rows = jnp.concatenate(
        [pair_flat[local_tokens - (kernel - 1) :], value_raw[local_tokens - (kernel - 1) :]], axis=1
    )
    before = passed_along(rim_rows, CTX, 1)
    first_token = lax.axis_index(CTX) * local_tokens
    padded_ids = jnp.concatenate([jnp.full((kernel - 1,), -1, jnp.int32), segment_ids])
    window_ids = lax.dynamic_slice_in_dim(padded_ids, first_token, local_tokens + kernel - 1)
    pair_padded = jnp.concatenate([before[:, :pair_width], pair_flat])
    value_padded = jnp.concatenate([before[:, pair_width:], value_raw])
    queries, key_rows, value_rows = mixer_inputs(
        pair_padded, value_padded, pair_filter, value_filter, window_ids, kernel
    )
    block_terms = block_tables(
        queries, key_rows, value_rows, write_strength, log_decay, window_ids, kernel
    )
    within, query_decayed, targets, corrector, transition, increment = block_terms
    heads_here, block_count = transition.shape[:2]
    prefix_map = jnp.broadcast_to(jnp.eye(DK, dtype=jnp.float32), (heads_here, DK, DK))
    prefix_shift = jnp.zeros((heads_here, DK, DV), jnp.float32)
    prefix_maps, prefix_shifts = ([], [])
    for block in range(block_count):
        prefix_maps.append(prefix_map)
        prefix_shifts.append(prefix_shift)
        prefix_map = batched(transition[:, block], prefix_map)
        prefix_shift = batched(transition[:, block], prefix_shift) + increment[:, block]
    stacked_maps = jnp.stack(prefix_maps, axis=1)
    stacked_shifts = jnp.stack(prefix_shifts, axis=1)
    query_effective = query_decayed - blockwise(within, corrector)
    through_entry = blockwise(query_effective, stacked_maps)
    fixed_part = blockwise(query_effective, stacked_shifts) + blockwise(within, targets)
    entering = scanned_entry(prefix_map, prefix_shift, CTX)
    emitted = (
        jnp.einsum("hbtk,hkv->hbtv", through_entry, entering, precision=HIGHEST) + fixed_part
    )
    mixed_heads = jnp.transpose(emitted, (1, 2, 0, 3)).reshape(-1, heads_here, DV)
    gated_out = gate_output(mixed_heads, gate_raw, norm_gain)
    partial_out = jnp.dot(gated_out, out_weight, preferred_element_type=jnp.float32)
    pairs = lax.axis_size("head")
    if pairs == 2:
        side = lax.axis_index("head")
        halves = partial_out.reshape(2, -1, partial_out.shape[1])
        kept = lax.dynamic_index_in_dim(halves, side, keepdims=False)
        given = lax.dynamic_index_in_dim(halves, 1 - side, keepdims=False)
        attention = kept + lax.ppermute(
            given.astype(jnp.bfloat16), "head", [(0, 1), (1, 0)]
        ).astype(jnp.float32)
    else:
        attention = lax.psum_scatter(
            partial_out.astype(jnp.bfloat16), "head", scatter_dimension=0, tiled=True
        ).astype(jnp.float32)
    hidden = (residual.astype(jnp.float32) + attention).astype(jnp.bfloat16)
    expert_in = post_norm(hidden, post_gain)
    levels = lax.axis_size("ctx_hi")
    level = lax.axis_index("ctx_hi")
    local_experts = expert_up.shape[0]
    per_level = lax.axis_size("ctx_lo") * lax.axis_size("head") * local_experts
    experts_all = levels * per_level
    local_rows = routes.shape[0]
    top_count = routes.shape[1]
    capacity = local_rows * top_count * 5 // (4 * experts_all)
    own_high = route_weights.astype(jnp.bfloat16)
    own_low = (route_weights - own_high.astype(jnp.float32)).astype(jnp.bfloat16)
    spare = -(-(3 * top_count) // 128) * 128 - 3 * top_count
    packed = jnp.concatenate(
        [
            expert_in,
            routes.astype(jnp.bfloat16),
            own_high,
            own_low,
            jnp.zeros((local_rows, spare), jnp.bfloat16),
        ],
        axis=1,
    )
    expert_ids = jnp.arange(experts_all, dtype=jnp.int32)
    earlier_rows = (
        lax.broadcasted_iota(jnp.int32, (local_rows, local_rows), 0)
        > lax.broadcasted_iota(jnp.int32, (local_rows, local_rows), 1)
    ).astype(jnp.bfloat16)
    slots_total = per_level * capacity
    slot_ids = jnp.arange(slots_total, dtype=jnp.int32)
    level_axes = ("ctx_lo", "head")
    routed = None
    for turn in range(levels):
        if turn == 0:
            chunk = packed
        else:
            chunk = lax.ppermute(
                packed, "ctx_hi", [(i, (i - turn) % levels) for i in range(levels)]
            )
        chunk_in = chunk[:, :D]
        chunk_routes = chunk[:, D : D + top_count].astype(jnp.int32)
        chunk_high = chunk[:, D + top_count : D + 2 * top_count]
        chunk_low = chunk[:, D + 2 * top_count : D + 3 * top_count]
        route_hot = chunk_routes[:, :, None] == expert_ids[None, None, :]
        row_hot = jnp.any(route_hot, axis=1).astype(jnp.bfloat16)
        earlier = jnp.dot(earlier_rows, row_hot, preferred_element_type=jnp.float32)
        slot_rank = jnp.sum(jnp.where(route_hot, earlier[:, None, :], 0.0), axis=2).astype(
            jnp.int32
        )
        slot_index = jnp.where(
            chunk_routes // per_level == level,
            (chunk_routes % per_level) * capacity + slot_rank,
            -1,
        )
        hits = slot_index[:, :, None] == slot_ids[None, None, :]
        picker = jnp.any(hits, axis=1).astype(jnp.bfloat16)
        outgoing = lax.dot_general(
            picker, chunk_in, (((0,), (0,)), ((), ())), preferred_element_type=jnp.float32
        ).astype(jnp.bfloat16)
        outgoing = outgoing.reshape(per_level // local_experts, local_experts * capacity, D)
        arrived = lax.all_to_all(outgoing, level_axes, split_axis=0, concat_axis=0, tiled=True)
        arrived = arrived.reshape(per_level // local_experts, local_experts, capacity, D)
        answered = jnp.stack(
            [
                expert_apply_rows(
                    arrived[:, member].reshape(-1, D), expert_up[member], expert_down[member]
                ).reshape(arrived.shape[0], capacity, D)
                for member in range(local_experts)
            ],
            axis=1,
        ).reshape(per_level // local_experts, local_experts * capacity, D)
        returned = lax.all_to_all(answered, level_axes, split_axis=0, concat_axis=0, tiled=True)
        result_rows = returned.reshape(slots_total, D)
        weight_high = jnp.sum(jnp.where(hits, chunk_high[:, :, None], 0.0), axis=1).astype(
            jnp.bfloat16
        )
        weight_low = jnp.sum(jnp.where(hits, chunk_low[:, :, None], 0.0), axis=1).astype(
            jnp.bfloat16
        )
        partial = jnp.dot(weight_high, result_rows, preferred_element_type=jnp.float32) + jnp.dot(
            weight_low, result_rows, preferred_element_type=jnp.float32
        )
        if turn == 0:
            routed = partial
        else:
            routed = routed + lax.ppermute(
                partial.astype(jnp.bfloat16),
                "ctx_hi",
                [(i, (i + turn) % levels) for i in range(levels)],
            ).astype(jnp.float32)
    combined = hidden.astype(jnp.float32) + routed
    return combined.astype(jnp.bfloat16)


def split_mesh(mesh):
    groups, peers, pairs = (mesh.shape["group"], mesh.shape["ctx"], mesh.shape["head"])
    low = 4 if peers % 4 == 0 else 1
    devices = mesh.devices.reshape(groups, peers // low, low, pairs)
    return Mesh(devices, ("group", "ctx_hi", "ctx_lo", "head"))


def solution(mesh):
    return jax.shard_map(
        per_device,
        mesh=split_mesh(mesh),
        in_specs=(
            P(("group", "ctx_hi", "ctx_lo"), None, "head"),
            P(("group", "ctx_hi", "ctx_lo"), "head"),
            P(("group", "ctx_hi", "ctx_lo"), "head"),
            P(("group", "ctx_hi", "ctx_lo"), "head"),
            P(("group", "ctx_hi", "ctx_lo"), "head"),
            P("group"),
            P(None, None, "head"),
            P(None, "head"),
            P(),
            P("head", None),
            P(("group", "ctx_hi", "ctx_lo", "head"), None),
            P(),
            P(("group", "ctx_hi", "ctx_lo", "head"), None),
            P(("group", "ctx_hi", "ctx_lo", "head"), None),
            P(("ctx_hi", "ctx_lo", "head"), None, None),
            P(("ctx_hi", "ctx_lo", "head"), None, None),
        ),
        out_specs=P(("group", "ctx_hi", "ctx_lo", "head"), None),
        check_vma=False,
    )
```

```python
import jax
import jax.numpy as jnp
from jax import lax
from jax.sharding import Mesh, PartitionSpec as P

D = 2048
DK = 128
DV = 128
BLOCK = 64
CTX = ("ctx_hi", "ctx_lo")


HIGHEST = lax.Precision.HIGHEST


def passed_along(block, axis, distance):
    devices = range(lax.axis_size(axis))
    route = [(i - distance, i) for i in devices if i - distance in devices]
    return lax.ppermute(block, axis, route)


def scanned_entry(whole_map, whole_shift, axis):
    peers, position = (lax.axis_size(axis), lax.axis_index(axis))
    window = 1
    while 2 * window < peers - 1:
        reached = position >= window
        both = jnp.stack([whole_map, whole_shift]).astype(jnp.bfloat16)
        both_in = passed_along(both, axis, window).astype(jnp.float32)
        new_map = batched(whole_map, both_in[0])
        new_shift = batched(whole_map, both_in[1]) + whole_shift
        whole_map = jnp.where(reached, new_map, whole_map)
        whole_shift = jnp.where(reached, new_shift, whole_shift)
        window *= 2
    both = jnp.stack([whole_map, whole_shift]).astype(jnp.bfloat16)
    nearest = passed_along(both, axis, 1).astype(jnp.float32)
    farther = passed_along(whole_shift.astype(jnp.bfloat16), axis, window + 1)
    return batched(nearest[0], farther.astype(jnp.float32)) + nearest[1]


def precise_dot(left, right):
    return jnp.dot(left, right, precision=HIGHEST, preferred_element_type=jnp.float32)


def causal_filter(padded_raw, filter_taps, padded_ids, kernel):
    length = padded_raw.shape[0] - (kernel - 1)
    source = padded_raw.astype(jnp.float32)
    current_ids = padded_ids[kernel - 1 :]
    summed = jnp.zeros((length, padded_raw.shape[1]), jnp.float32)
    for lag_step in range(kernel):
        offset_start = kernel - 1 - lag_step
        shifted = source[offset_start : offset_start + length]
        matching = (padded_ids[offset_start : offset_start + length] == current_ids).astype(
            jnp.float32
        )
        summed = summed + filter_taps[lag_step] * shifted * matching[:, None]
    return jax.nn.silu(summed)


def unit_rows(values_in):
    return values_in / jnp.sqrt(jnp.sum(values_in * values_in, axis=-1, keepdims=True) + 1e-06)


def mixer_inputs(pair_padded, value_padded, pair_filter, value_filter, padded_ids, kernel):
    pair_act = causal_filter(pair_padded, pair_filter.reshape(kernel, -1), padded_ids, kernel)
    length = pair_act.shape[0]
    pair_heads = pair_act.reshape(length, 2, -1, DK)
    queries = unit_rows(pair_heads[:, 0]) * DK ** (-0.5)
    key_rows = unit_rows(pair_heads[:, 1])
    value_rows = causal_filter(value_padded, value_filter, padded_ids, kernel).reshape(
        length, -1, DV
    )
    repeat_factor = value_rows.shape[1] // key_rows.shape[1]
    return (
        jnp.repeat(queries, repeat_factor, axis=1),
        jnp.repeat(key_rows, repeat_factor, axis=1),
        value_rows,
    )


def unit_lower_inverse(system):
    size = system.shape[-1]
    row_index = lax.broadcasted_iota(jnp.int32, (size, size), 0)
    col_index = lax.broadcasted_iota(jnp.int32, (size, size), 1)
    inverse = jnp.broadcast_to(jnp.eye(size, dtype=system.dtype), system.shape)
    width = 1
    while width < size:
        linking = (
            (row_index // (2 * width) == col_index // (2 * width))
            & ((row_index // width) % 2 == 1)
            & ((col_index // width) % 2 == 0)
        )
        lower_left = jnp.where(linking, system, 0.0)
        inverse = inverse - precise_dot(inverse, precise_dot(lower_left, inverse))
        width *= 2
    return inverse


def block_setup(queries, key_rows, value_rows, strength, decay_rows, segment_here, prior_id):
    cumulative = jnp.cumsum(decay_rows)
    row_index = lax.broadcasted_iota(jnp.int32, (BLOCK, BLOCK), 0)
    col_index = lax.broadcasted_iota(jnp.int32, (BLOCK, BLOCK), 1)
    same_segment = segment_here[:, None] == segment_here[None, :]
    causal = (row_index >= col_index) & same_segment
    strictly = (row_index > col_index) & same_segment
    decay_matrix = jnp.where(
        causal, jnp.exp(jnp.where(causal, cumulative[:, None] - cumulative[None, :], 0.0)), 0.0
    )
    carried_in = (segment_here == prior_id).astype(jnp.float32)
    keyed_beta = key_rows * strength[:, None]
    coupling = jnp.where(strictly, precise_dot(keyed_beta, key_rows.T) * decay_matrix, 0.0)
    system = jnp.eye(BLOCK, dtype=jnp.float32) + coupling
    stacked = jnp.concatenate(
        [value_rows * strength[:, None], keyed_beta * (jnp.exp(cumulative) * carried_in)[:, None]],
        axis=1,
    )
    solved = precise_dot(unit_lower_inverse(system), stacked)
    targets = solved[:, :DV]
    corrector = solved[:, DV:]
    within = jnp.where(causal, precise_dot(queries, key_rows.T) * decay_matrix, 0.0)
    query_decayed = queries * (jnp.exp(cumulative) * carried_in)[:, None]
    final_log = cumulative[BLOCK - 1]
    weighting = (segment_here == segment_here[BLOCK - 1]).astype(jnp.float32) * jnp.exp(
        final_log - cumulative
    )
    keys_weighted = key_rows * weighting[:, None]
    transition = jnp.exp(final_log) * carried_in[BLOCK - 1] * jnp.eye(
        DK, dtype=jnp.float32
    ) - precise_dot(keys_weighted.T, corrector)
    increment = precise_dot(keys_weighted.T, targets)
    return (within, query_decayed, targets, corrector, transition, increment)


def head_major(array_in, block_count):
    moved = jnp.moveaxis(array_in, 1, 0)
    return moved.reshape((array_in.shape[1], block_count, BLOCK) + array_in.shape[2:])


def block_tables(queries, key_rows, value_rows, strength, decay_rows, padded_ids, kernel):
    length = queries.shape[0]
    block_count = length // BLOCK
    current_ids = padded_ids[kernel - 1 :].reshape(block_count, BLOCK)
    prior_ids = padded_ids[kernel - 2 : kernel - 2 + length : BLOCK]
    per_block = jax.vmap(block_setup, in_axes=(0, 0, 0, 0, 0, 0, 0))
    per_head = jax.vmap(per_block, in_axes=(0, 0, 0, 0, 0, None, None))
    return per_head(
        head_major(queries, block_count),
        head_major(key_rows, block_count),
        head_major(value_rows, block_count),
        head_major(strength, block_count),
        head_major(decay_rows, block_count),
        current_ids,
        prior_ids,
    )


def blockwise(left, right):
    return jnp.einsum("hbij,hbjk->hbik", left, right, precision=HIGHEST)


def batched(left, right):
    return jnp.einsum("hij,hjk->hik", left, right, precision=HIGHEST)


def sweep_blocks(block_terms, start_state):
    blocks_first = tuple((jnp.swapaxes(member, 0, 1) for member in block_terms))

    def advance(carry_state, pieces):
        within, query_decayed, targets, corrector, transition, increment = pieces
        fresh_values = targets - batched(corrector, carry_state)
        emitted = batched(query_decayed, carry_state) + batched(within, fresh_values)
        updated = batched(transition, carry_state) + increment
        return (updated, emitted)

    final_state, emitted = lax.scan(advance, start_state, blocks_first)
    return emitted


def tokens_first(emitted):
    heads_count = emitted.shape[1]
    return jnp.transpose(emitted, (0, 2, 1, 3)).reshape(-1, heads_count, emitted.shape[3])


def gate_output(mixed_heads, gate_raw, norm_gain):
    square_mean = jnp.mean(mixed_heads * mixed_heads, axis=-1, keepdims=True)
    gate_values = jax.nn.silu(gate_raw.reshape(mixed_heads.shape).astype(jnp.float32))
    normed = mixed_heads / jnp.sqrt(square_mean + 1e-06) * norm_gain * gate_values
    return normed.astype(jnp.bfloat16).reshape(mixed_heads.shape[0], -1)


def post_norm(hidden, post_gain):
    hidden_full = hidden.astype(jnp.float32)
    square_mean = jnp.mean(hidden_full * hidden_full, axis=-1, keepdims=True)
    return (hidden_full / jnp.sqrt(square_mean + 1e-06) * post_gain).astype(jnp.bfloat16)


def expert_apply_rows(rows_in, up_matrix, down_matrix):
    hidden_units = down_matrix.shape[0]
    gate_up = jnp.dot(rows_in, up_matrix, preferred_element_type=jnp.float32)
    activated = (jax.nn.silu(gate_up[:, :hidden_units]) * gate_up[:, hidden_units:]).astype(
        jnp.bfloat16
    )
    return jnp.dot(activated, down_matrix, preferred_element_type=jnp.float32).astype(jnp.bfloat16)


def expert_apply(arrived, expert_up, expert_down):
    member_rows = arrived[:, 0]
    flattened = member_rows.reshape(-1, member_rows.shape[-1])
    result = expert_apply_rows(flattened, expert_up[0], expert_down[0])
    outputs = [result.reshape(member_rows.shape)]
    return jnp.stack(outputs, axis=1)


def route_slots(routes, experts_all, capacity):
    assigned = routes.reshape(-1)
    expert_ids = jnp.arange(experts_all, dtype=jnp.int32)
    onehot = (assigned[:, None] == expert_ids[None, :]).astype(jnp.int32)
    slot_rank = jnp.sum((jnp.cumsum(onehot, axis=0) - 1) * onehot, axis=1)
    return assigned * capacity + slot_rank


def per_device(
    pair_raw,
    value_raw,
    gate_raw,
    write_strength,
    log_decay,
    segment_ids,
    pair_filter,
    value_filter,
    norm_gain,
    out_weight,
    residual,
    post_gain,
    routes,
    route_weights,
    expert_up,
    expert_down,
):
    local_tokens = pair_raw.shape[0]
    kernel = value_filter.shape[0]
    pair_flat = pair_raw.reshape(local_tokens, -1)
    pair_width = pair_flat.shape[1]
    rim_rows = jnp.concatenate(
        [pair_flat[local_tokens - (kernel - 1) :], value_raw[local_tokens - (kernel - 1) :]], axis=1
    )
    before = passed_along(rim_rows, CTX, 1)
    first_token = lax.axis_index(CTX) * local_tokens
    padded_ids = jnp.concatenate([jnp.full((kernel - 1,), -1, jnp.int32), segment_ids])
    window_ids = lax.dynamic_slice_in_dim(padded_ids, first_token, local_tokens + kernel - 1)
    pair_padded = jnp.concatenate([before[:, :pair_width], pair_flat])
    value_padded = jnp.concatenate([before[:, pair_width:], value_raw])
    queries, key_rows, value_rows = mixer_inputs(
        pair_padded, value_padded, pair_filter, value_filter, window_ids, kernel
    )
    block_terms = block_tables(
        queries, key_rows, value_rows, write_strength, log_decay, window_ids, kernel
    )
    within, query_decayed, targets, corrector, transition, increment = block_terms
    heads_here, block_count = transition.shape[:2]
    prefix_map = jnp.broadcast_to(jnp.eye(DK, dtype=jnp.float32), (heads_here, DK, DK))
    prefix_shift = jnp.zeros((heads_here, DK, DV), jnp.float32)
    prefix_maps, prefix_shifts = ([], [])
    for block in range(block_count):
        prefix_maps.append(prefix_map)
        prefix_shifts.append(prefix_shift)
        prefix_map = batched(transition[:, block], prefix_map)
        prefix_shift = batched(transition[:, block], prefix_shift) + increment[:, block]
    stacked_maps = jnp.stack(prefix_maps, axis=1)
    stacked_shifts = jnp.stack(prefix_shifts, axis=1)
    query_effective = query_decayed - blockwise(within, corrector)
    through_entry = blockwise(query_effective, stacked_maps)
    fixed_part = blockwise(query_effective, stacked_shifts) + blockwise(within, targets)
    entering = scanned_entry(prefix_map, prefix_shift, CTX)
    emitted = (
        jnp.einsum("hbtk,hkv->hbtv", through_entry, entering, precision=HIGHEST) + fixed_part
    )
    mixed_heads = jnp.transpose(emitted, (1, 2, 0, 3)).reshape(-1, heads_here, DV)
    gated_out = gate_output(mixed_heads, gate_raw, norm_gain)
    partial_out = jnp.dot(gated_out, out_weight, preferred_element_type=jnp.float32)
    pairs = lax.axis_size("head")
    if pairs == 2:
        side = lax.axis_index("head")
        halves = partial_out.reshape(2, -1, partial_out.shape[1])
        kept = lax.dynamic_index_in_dim(halves, side, keepdims=False)
        given = lax.dynamic_index_in_dim(halves, 1 - side, keepdims=False)
        attention = kept + lax.ppermute(
            given.astype(jnp.bfloat16), "head", [(0, 1), (1, 0)]
        ).astype(jnp.float32)
    else:
        attention = lax.psum_scatter(
            partial_out.astype(jnp.bfloat16), "head", scatter_dimension=0, tiled=True
        ).astype(jnp.float32)
    hidden = (residual.astype(jnp.float32) + attention).astype(jnp.bfloat16)
    expert_in = post_norm(hidden, post_gain)
    levels = lax.axis_size("ctx_hi")
    level = lax.axis_index("ctx_hi")
    local_experts = expert_up.shape[0]
    per_level = lax.axis_size("ctx_lo") * lax.axis_size("head") * local_experts
    experts_all = levels * per_level
    local_rows = routes.shape[0]
    top_count = routes.shape[1]
    capacity = local_rows * top_count * 5 // (4 * experts_all)
    own_high = route_weights.astype(jnp.bfloat16)
    own_low = (route_weights - own_high.astype(jnp.float32)).astype(jnp.bfloat16)
    spare = -(-(3 * top_count) // 128) * 128 - 3 * top_count
    packed = jnp.concatenate(
        [
            expert_in,
            routes.astype(jnp.bfloat16),
            own_high,
            own_low,
            jnp.zeros((local_rows, spare), jnp.bfloat16),
        ],
        axis=1,
    )
    expert_ids = jnp.arange(experts_all, dtype=jnp.int32)
    earlier_rows = (
        lax.broadcasted_iota(jnp.int32, (local_rows, local_rows), 0)
        > lax.broadcasted_iota(jnp.int32, (local_rows, local_rows), 1)
    ).astype(jnp.bfloat16)
    slots_total = per_level * capacity
    slot_ids = jnp.arange(slots_total, dtype=jnp.int32)
    level_axes = ("ctx_lo", "head")
    routed = None
    for turn in range(levels):
        if turn == 0:
            chunk = packed
        else:
            chunk = lax.ppermute(
                packed, "ctx_hi", [(i, (i - turn) % levels) for i in range(levels)]
            )
        chunk_in = chunk[:, :D]
        chunk_routes = chunk[:, D : D + top_count].astype(jnp.int32)
        chunk_high = chunk[:, D + top_count : D + 2 * top_count]
        chunk_low = chunk[:, D + 2 * top_count : D + 3 * top_count]
        route_hot = chunk_routes[:, :, None] == expert_ids[None, None, :]
        row_hot = jnp.any(route_hot, axis=1).astype(jnp.bfloat16)
        earlier = jnp.dot(earlier_rows, row_hot, preferred_element_type=jnp.float32)
        slot_rank = jnp.sum(jnp.where(route_hot, earlier[:, None, :], 0.0), axis=2).astype(
            jnp.int32
        )
        slot_index = jnp.where(
            chunk_routes // per_level == level,
            (chunk_routes % per_level) * capacity + slot_rank,
            -1,
        )
        hits = slot_index[:, :, None] == slot_ids[None, None, :]
        picker = jnp.any(hits, axis=1).astype(jnp.bfloat16)
        outgoing = lax.dot_general(
            picker, chunk_in, (((0,), (0,)), ((), ())), preferred_element_type=jnp.float32
        ).astype(jnp.bfloat16)
        outgoing = outgoing.reshape(per_level // local_experts, local_experts * capacity, D)
        arrived = lax.all_to_all(outgoing, level_axes, split_axis=0, concat_axis=0, tiled=True)
        arrived = arrived.reshape(per_level // local_experts, local_experts, capacity, D)
        answered = jnp.stack(
            [
                expert_apply_rows(
                    arrived[:, member].reshape(-1, D), expert_up[member], expert_down[member]
                ).reshape(arrived.shape[0], capacity, D)
                for member in range(local_experts)
            ],
            axis=1,
        ).reshape(per_level // local_experts, local_experts * capacity, D)
        returned = lax.all_to_all(answered, level_axes, split_axis=0, concat_axis=0, tiled=True)
        result_rows = returned.reshape(slots_total, D)
        weight_high = jnp.sum(jnp.where(hits, chunk_high[:, :, None], 0.0), axis=1).astype(
            jnp.bfloat16
        )
        weight_low = jnp.sum(jnp.where(hits, chunk_low[:, :, None], 0.0), axis=1).astype(
            jnp.bfloat16
        )
        partial = jnp.dot(weight_high, result_rows, preferred_element_type=jnp.float32) + jnp.dot(
            weight_low, result_rows, preferred_element_type=jnp.float32
        )
        if turn == 0:
            routed = partial
        else:
            routed = routed + lax.ppermute(
                partial.astype(jnp.bfloat16),
                "ctx_hi",
                [(i, (i + turn) % levels) for i in range(levels)],
            ).astype(jnp.float32)
    combined = hidden.astype(jnp.float32) + routed
    return combined.astype(jnp.bfloat16)


def split_mesh(mesh):
    groups, peers, pairs = (mesh.shape["group"], mesh.shape["ctx"], mesh.shape["head"])
    low = 4 if peers % 4 == 0 else 1
    devices = mesh.devices.reshape(groups, peers // low, low, pairs)
    return Mesh(devices, ("group", "ctx_hi", "ctx_lo", "head"))


def solution(mesh):
    return jax.shard_map(
        per_device,
        mesh=split_mesh(mesh),
        in_specs=(
            P(("group", "ctx_hi", "ctx_lo"), None, "head"),
            P(("group", "ctx_hi", "ctx_lo"), "head"),
            P(("group", "ctx_hi", "ctx_lo"), "head"),
            P(("group", "ctx_hi", "ctx_lo"), "head"),
            P(("group", "ctx_hi", "ctx_lo"), "head"),
            P("group"),
            P(None, None, "head"),
            P(None, "head"),
            P(),
            P("head", None),
            P(("group", "ctx_hi", "ctx_lo", "head"), None),
            P(),
            P(("group", "ctx_hi", "ctx_lo", "head"), None),
            P(("group", "ctx_hi", "ctx_lo", "head"), None),
            P(("ctx_hi", "ctx_lo", "head"), None, None),
            P(("ctx_hi", "ctx_lo", "head"), None, None),
        ),
        out_specs=P(("group", "ctx_hi", "ctx_lo", "head"), None),
        check_vma=False,
    )
```

```python
import jax
import jax.numpy as jnp
from jax import lax
from jax.sharding import Mesh, PartitionSpec as P

D = 2048
DK = 128
DV = 128
BLOCK = 64
CTX = ("ctx_hi", "ctx_lo")


HIGHEST = lax.Precision.HIGHEST


def passed_along(block, axis, distance):
    devices = range(lax.axis_size(axis))
    route = [(i - distance, i) for i in devices if i - distance in devices]
    return lax.ppermute(block, axis, route)


def scanned_entry(whole_map, whole_shift, axis):
    peers, position = (lax.axis_size(axis), lax.axis_index(axis))
    distance = 1
    while distance < peers:
        last = 2 * distance >= peers
        reached = position >= distance
        if last:
            shift_in = passed_along(whole_shift.astype(jnp.bfloat16), axis, distance)
            shift_in = shift_in.astype(jnp.float32)
        else:
            both = jnp.stack([whole_map, whole_shift]).astype(jnp.bfloat16)
            both_in = passed_along(both, axis, distance).astype(jnp.float32)
            map_in, shift_in = (both_in[0], both_in[1])
        new_shift = batched(whole_map, shift_in) + whole_shift
        if not last:
            whole_map = jnp.where(reached, batched(whole_map, map_in), whole_map)
        whole_shift = jnp.where(reached, new_shift, whole_shift)
        distance *= 2
    return passed_along(whole_shift.astype(jnp.bfloat16), axis, 1).astype(jnp.float32)


def precise_dot(left, right):
    return jnp.dot(left, right, precision=HIGHEST, preferred_element_type=jnp.float32)


def causal_filter(padded_raw, filter_taps, padded_ids, kernel):
    length = padded_raw.shape[0] - (kernel - 1)
    source = padded_raw.astype(jnp.float32)
    current_ids = padded_ids[kernel - 1 :]
    summed = jnp.zeros((length, padded_raw.shape[1]), jnp.float32)
    for lag_step in range(kernel):
        offset_start = kernel - 1 - lag_step
        shifted = source[offset_start : offset_start + length]
        matching = (padded_ids[offset_start : offset_start + length] == current_ids).astype(
            jnp.float32
        )
        summed = summed + filter_taps[lag_step] * shifted * matching[:, None]
    return jax.nn.silu(summed)


def unit_rows(values_in):
    return values_in / jnp.sqrt(jnp.sum(values_in * values_in, axis=-1, keepdims=True) + 1e-06)


def mixer_inputs(pair_padded, value_padded, pair_filter, value_filter, padded_ids, kernel):
    pair_act = causal_filter(pair_padded, pair_filter.reshape(kernel, -1), padded_ids, kernel)
    length = pair_act.shape[0]
    pair_heads = pair_act.reshape(length, 2, -1, DK)
    queries = unit_rows(pair_heads[:, 0]) * DK ** (-0.5)
    key_rows = unit_rows(pair_heads[:, 1])
    value_rows = causal_filter(value_padded, value_filter, padded_ids, kernel).reshape(
        length, -1, DV
    )
    repeat_factor = value_rows.shape[1] // key_rows.shape[1]
    return (
        jnp.repeat(queries, repeat_factor, axis=1),
        jnp.repeat(key_rows, repeat_factor, axis=1),
        value_rows,
    )


def unit_lower_inverse(system):
    size = system.shape[-1]
    row_index = lax.broadcasted_iota(jnp.int32, (size, size), 0)
    col_index = lax.broadcasted_iota(jnp.int32, (size, size), 1)
    inverse = jnp.broadcast_to(jnp.eye(size, dtype=system.dtype), system.shape)
    width = 1
    while width < size:
        linking = (
            (row_index // (2 * width) == col_index // (2 * width))
            & ((row_index // width) % 2 == 1)
            & ((col_index // width) % 2 == 0)
        )
        lower_left = jnp.where(linking, system, 0.0)
        inverse = inverse - precise_dot(inverse, precise_dot(lower_left, inverse))
        width *= 2
    return inverse


def block_setup(queries, key_rows, value_rows, strength, decay_rows, segment_here, prior_id):
    cumulative = jnp.cumsum(decay_rows)
    row_index = lax.broadcasted_iota(jnp.int32, (BLOCK, BLOCK), 0)
    col_index = lax.broadcasted_iota(jnp.int32, (BLOCK, BLOCK), 1)
    same_segment = segment_here[:, None] == segment_here[None, :]
    causal = (row_index >= col_index) & same_segment
    strictly = (row_index > col_index) & same_segment
    decay_matrix = jnp.where(
        causal, jnp.exp(jnp.where(causal, cumulative[:, None] - cumulative[None, :], 0.0)), 0.0
    )
    carried_in = (segment_here == prior_id).astype(jnp.float32)
    keyed_beta = key_rows * strength[:, None]
    coupling = jnp.where(strictly, precise_dot(keyed_beta, key_rows.T) * decay_matrix, 0.0)
    system = jnp.eye(BLOCK, dtype=jnp.float32) + coupling
    stacked = jnp.concatenate(
        [value_rows * strength[:, None], keyed_beta * (jnp.exp(cumulative) * carried_in)[:, None]],
        axis=1,
    )
    solved = precise_dot(unit_lower_inverse(system), stacked)
    targets = solved[:, :DV]
    corrector = solved[:, DV:]
    within = jnp.where(causal, precise_dot(queries, key_rows.T) * decay_matrix, 0.0)
    query_decayed = queries * (jnp.exp(cumulative) * carried_in)[:, None]
    final_log = cumulative[BLOCK - 1]
    weighting = (segment_here == segment_here[BLOCK - 1]).astype(jnp.float32) * jnp.exp(
        final_log - cumulative
    )
    keys_weighted = key_rows * weighting[:, None]
    transition = jnp.exp(final_log) * carried_in[BLOCK - 1] * jnp.eye(
        DK, dtype=jnp.float32
    ) - precise_dot(keys_weighted.T, corrector)
    increment = precise_dot(keys_weighted.T, targets)
    return (within, query_decayed, targets, corrector, transition, increment)


def head_major(array_in, block_count):
    moved = jnp.moveaxis(array_in, 1, 0)
    return moved.reshape((array_in.shape[1], block_count, BLOCK) + array_in.shape[2:])


def block_tables(queries, key_rows, value_rows, strength, decay_rows, padded_ids, kernel):
    length = queries.shape[0]
    block_count = length // BLOCK
    current_ids = padded_ids[kernel - 1 :].reshape(block_count, BLOCK)
    prior_ids = padded_ids[kernel - 2 : kernel - 2 + length : BLOCK]
    per_block = jax.vmap(block_setup, in_axes=(0, 0, 0, 0, 0, 0, 0))
    per_head = jax.vmap(per_block, in_axes=(0, 0, 0, 0, 0, None, None))
    return per_head(
        head_major(queries, block_count),
        head_major(key_rows, block_count),
        head_major(value_rows, block_count),
        head_major(strength, block_count),
        head_major(decay_rows, block_count),
        current_ids,
        prior_ids,
    )


def blockwise(left, right):
    return jnp.einsum("hbij,hbjk->hbik", left, right, precision=HIGHEST)


def batched(left, right):
    return jnp.einsum("hij,hjk->hik", left, right, precision=HIGHEST)


def sweep_blocks(block_terms, start_state):
    blocks_first = tuple((jnp.swapaxes(member, 0, 1) for member in block_terms))

    def advance(carry_state, pieces):
        within, query_decayed, targets, corrector, transition, increment = pieces
        fresh_values = targets - batched(corrector, carry_state)
        emitted = batched(query_decayed, carry_state) + batched(within, fresh_values)
        updated = batched(transition, carry_state) + increment
        return (updated, emitted)

    final_state, emitted = lax.scan(advance, start_state, blocks_first)
    return emitted


def tokens_first(emitted):
    heads_count = emitted.shape[1]
    return jnp.transpose(emitted, (0, 2, 1, 3)).reshape(-1, heads_count, emitted.shape[3])


def gate_output(mixed_heads, gate_raw, norm_gain):
    square_mean = jnp.mean(mixed_heads * mixed_heads, axis=-1, keepdims=True)
    gate_values = jax.nn.silu(gate_raw.reshape(mixed_heads.shape).astype(jnp.float32))
    normed = mixed_heads / jnp.sqrt(square_mean + 1e-06) * norm_gain * gate_values
    return normed.astype(jnp.bfloat16).reshape(mixed_heads.shape[0], -1)


def post_norm(hidden, post_gain):
    hidden_full = hidden.astype(jnp.float32)
    square_mean = jnp.mean(hidden_full * hidden_full, axis=-1, keepdims=True)
    return (hidden_full / jnp.sqrt(square_mean + 1e-06) * post_gain).astype(jnp.bfloat16)


def expert_apply_rows(rows_in, up_matrix, down_matrix):
    hidden_units = down_matrix.shape[0]
    gate_up = jnp.dot(rows_in, up_matrix, preferred_element_type=jnp.float32)
    activated = (jax.nn.silu(gate_up[:, :hidden_units]) * gate_up[:, hidden_units:]).astype(
        jnp.bfloat16
    )
    return jnp.dot(activated, down_matrix, preferred_element_type=jnp.float32).astype(jnp.bfloat16)


def expert_apply(arrived, expert_up, expert_down):
    member_rows = arrived[:, 0]
    flattened = member_rows.reshape(-1, member_rows.shape[-1])
    result = expert_apply_rows(flattened, expert_up[0], expert_down[0])
    outputs = [result.reshape(member_rows.shape)]
    return jnp.stack(outputs, axis=1)


def route_slots(routes, experts_all, capacity):
    assigned = routes.reshape(-1)
    expert_ids = jnp.arange(experts_all, dtype=jnp.int32)
    onehot = (assigned[:, None] == expert_ids[None, :]).astype(jnp.int32)
    slot_rank = jnp.sum((jnp.cumsum(onehot, axis=0) - 1) * onehot, axis=1)
    return assigned * capacity + slot_rank


def per_device(
    pair_raw,
    value_raw,
    gate_raw,
    write_strength,
    log_decay,
    segment_ids,
    pair_filter,
    value_filter,
    norm_gain,
    out_weight,
    residual,
    post_gain,
    routes,
    route_weights,
    expert_up,
    expert_down,
):
    local_tokens = pair_raw.shape[0]
    kernel = value_filter.shape[0]
    pair_flat = pair_raw.reshape(local_tokens, -1)
    pair_width = pair_flat.shape[1]
    rim_rows = jnp.concatenate(
        [pair_flat[local_tokens - (kernel - 1) :], value_raw[local_tokens - (kernel - 1) :]], axis=1
    )
    before = passed_along(rim_rows, CTX, 1)
    first_token = lax.axis_index(CTX) * local_tokens
    padded_ids = jnp.concatenate([jnp.full((kernel - 1,), -1, jnp.int32), segment_ids])
    window_ids = lax.dynamic_slice_in_dim(padded_ids, first_token, local_tokens + kernel - 1)
    pair_padded = jnp.concatenate([before[:, :pair_width], pair_flat])
    value_padded = jnp.concatenate([before[:, pair_width:], value_raw])
    queries, key_rows, value_rows = mixer_inputs(
        pair_padded, value_padded, pair_filter, value_filter, window_ids, kernel
    )
    block_terms = block_tables(
        queries, key_rows, value_rows, write_strength, log_decay, window_ids, kernel
    )
    within, query_decayed, targets, corrector, transition, increment = block_terms
    heads_here, block_count = transition.shape[:2]
    prefix_map = jnp.broadcast_to(jnp.eye(DK, dtype=jnp.float32), (heads_here, DK, DK))
    prefix_shift = jnp.zeros((heads_here, DK, DV), jnp.float32)
    prefix_maps, prefix_shifts = ([], [])
    for block in range(block_count):
        prefix_maps.append(prefix_map)
        prefix_shifts.append(prefix_shift)
        prefix_map = batched(transition[:, block], prefix_map)
        prefix_shift = batched(transition[:, block], prefix_shift) + increment[:, block]
    stacked_maps = jnp.stack(prefix_maps, axis=1)
    stacked_shifts = jnp.stack(prefix_shifts, axis=1)
    query_effective = query_decayed - blockwise(within, corrector)
    through_entry = blockwise(query_effective, stacked_maps)
    fixed_part = blockwise(query_effective, stacked_shifts) + blockwise(within, targets)
    entering = scanned_entry(prefix_map, prefix_shift, CTX)
    emitted = (
        jnp.einsum("hbtk,hkv->hbtv", through_entry, entering, precision=HIGHEST) + fixed_part
    )
    mixed_heads = jnp.transpose(emitted, (1, 2, 0, 3)).reshape(-1, heads_here, DV)
    gated_out = gate_output(mixed_heads, gate_raw, norm_gain)
    partial_out = jnp.dot(gated_out, out_weight, preferred_element_type=jnp.float32)
    pairs = lax.axis_size("head")
    if pairs == 2:
        side = lax.axis_index("head")
        halves = partial_out.reshape(2, -1, partial_out.shape[1])
        kept = lax.dynamic_index_in_dim(halves, side, keepdims=False)
        given = lax.dynamic_index_in_dim(halves, 1 - side, keepdims=False)
        attention = kept + lax.ppermute(
            given.astype(jnp.bfloat16), "head", [(0, 1), (1, 0)]
        ).astype(jnp.float32)
    else:
        attention = lax.psum_scatter(
            partial_out.astype(jnp.bfloat16), "head", scatter_dimension=0, tiled=True
        ).astype(jnp.float32)
    hidden = (residual.astype(jnp.float32) + attention).astype(jnp.bfloat16)
    expert_in = post_norm(hidden, post_gain)
    levels = lax.axis_size("ctx_hi")
    level = lax.axis_index("ctx_hi")
    local_experts = expert_up.shape[0]
    per_level = lax.axis_size("ctx_lo") * lax.axis_size("head") * local_experts
    experts_all = levels * per_level
    local_rows = routes.shape[0]
    top_count = routes.shape[1]
    capacity = local_rows * top_count * 5 // (4 * experts_all)
    own_high = route_weights.astype(jnp.bfloat16)
    own_low = (route_weights - own_high.astype(jnp.float32)).astype(jnp.bfloat16)
    spare = -(-(3 * top_count) // 128) * 128 - 3 * top_count
    packed = jnp.concatenate(
        [
            expert_in,
            routes.astype(jnp.bfloat16),
            own_high,
            own_low,
            jnp.zeros((local_rows, spare), jnp.bfloat16),
        ],
        axis=1,
    )
    expert_ids = jnp.arange(experts_all, dtype=jnp.int32)
    earlier_rows = (
        lax.broadcasted_iota(jnp.int32, (local_rows, local_rows), 0)
        > lax.broadcasted_iota(jnp.int32, (local_rows, local_rows), 1)
    ).astype(jnp.bfloat16)
    slots_total = per_level * capacity
    slot_ids = jnp.arange(slots_total, dtype=jnp.int32)
    level_axes = ("ctx_lo", "head")
    received = [packed] + [
        lax.ppermute(packed, "ctx_hi", [(i, (i - turn) % levels) for i in range(levels)])
        for turn in range(1, levels)
    ]
    turn_groups = [[0]] + ([list(range(1, levels))] if levels > 1 else [])
    routed = None
    for group_turns in turn_groups:
        members = len(group_turns)
        chunk = jnp.concatenate([received[turn] for turn in group_turns], axis=0)
        chunk_in = chunk[:, :D]
        chunk_routes = chunk[:, D : D + top_count].astype(jnp.int32)
        chunk_high = chunk[:, D + top_count : D + 2 * top_count]
        chunk_low = chunk[:, D + 2 * top_count : D + 3 * top_count]
        route_hot = chunk_routes[:, :, None] == expert_ids[None, None, :]
        row_hot = jnp.any(route_hot, axis=1).astype(jnp.bfloat16)
        earlier = jnp.einsum(
            "ij,sje->sie",
            earlier_rows,
            row_hot.reshape(members, local_rows, experts_all),
            preferred_element_type=jnp.float32,
        ).reshape(members * local_rows, experts_all)
        slot_rank = jnp.sum(jnp.where(route_hot, earlier[:, None, :], 0.0), axis=2).astype(
            jnp.int32
        )
        member_of = lax.broadcasted_iota(jnp.int32, chunk_routes.shape, 0) // local_rows
        group_capacity = members * capacity
        slot_index = jnp.where(
            chunk_routes // per_level == level,
            (chunk_routes % per_level) * group_capacity + member_of * capacity + slot_rank,
            -1,
        )
        slot_ids = jnp.arange(per_level * group_capacity, dtype=jnp.int32)
        hits = slot_index[:, :, None] == slot_ids[None, None, :]
        picker = jnp.any(hits, axis=1).astype(jnp.bfloat16)
        outgoing = lax.dot_general(
            picker, chunk_in, (((0,), (0,)), ((), ())), preferred_element_type=jnp.float32
        ).astype(jnp.bfloat16)
        outgoing = outgoing.reshape(per_level // local_experts, local_experts * group_capacity, D)
        arrived = lax.all_to_all(outgoing, level_axes, split_axis=0, concat_axis=0, tiled=True)
        arrived = arrived.reshape(per_level // local_experts, local_experts, group_capacity, D)
        answered = jnp.stack(
            [
                expert_apply_rows(
                    arrived[:, member].reshape(-1, D), expert_up[member], expert_down[member]
                ).reshape(arrived.shape[0], group_capacity, D)
                for member in range(local_experts)
            ],
            axis=1,
        ).reshape(per_level // local_experts, local_experts * group_capacity, D)
        returned = lax.all_to_all(answered, level_axes, split_axis=0, concat_axis=0, tiled=True)
        result_rows = returned.reshape(per_level * group_capacity, D)
        weight_high = jnp.sum(jnp.where(hits, chunk_high[:, :, None], 0.0), axis=1).astype(
            jnp.bfloat16
        )
        weight_low = jnp.sum(jnp.where(hits, chunk_low[:, :, None], 0.0), axis=1).astype(
            jnp.bfloat16
        )
        partial = jnp.dot(weight_high, result_rows, preferred_element_type=jnp.float32) + jnp.dot(
            weight_low, result_rows, preferred_element_type=jnp.float32
        )
        for index, turn in enumerate(group_turns):
            piece = partial[index * local_rows : (index + 1) * local_rows]
            if turn == 0:
                routed = piece
            else:
                routed = routed + lax.ppermute(
                    piece.astype(jnp.bfloat16),
                    "ctx_hi",
                    [(i, (i + turn) % levels) for i in range(levels)],
                ).astype(jnp.float32)
    combined = hidden.astype(jnp.float32) + routed
    return combined.astype(jnp.bfloat16)


def split_mesh(mesh):
    groups, peers, pairs = (mesh.shape["group"], mesh.shape["ctx"], mesh.shape["head"])
    low = 4 if peers % 4 == 0 else 1
    devices = mesh.devices.reshape(groups, peers // low, low, pairs)
    return Mesh(devices, ("group", "ctx_hi", "ctx_lo", "head"))


def solution(mesh):
    return jax.shard_map(
        per_device,
        mesh=split_mesh(mesh),
        in_specs=(
            P(("group", "ctx_hi", "ctx_lo"), None, "head"),
            P(("group", "ctx_hi", "ctx_lo"), "head"),
            P(("group", "ctx_hi", "ctx_lo"), "head"),
            P(("group", "ctx_hi", "ctx_lo"), "head"),
            P(("group", "ctx_hi", "ctx_lo"), "head"),
            P("group"),
            P(None, None, "head"),
            P(None, "head"),
            P(),
            P("head", None),
            P(("group", "ctx_hi", "ctx_lo", "head"), None),
            P(),
            P(("group", "ctx_hi", "ctx_lo", "head"), None),
            P(("group", "ctx_hi", "ctx_lo", "head"), None),
            P(("ctx_hi", "ctx_lo", "head"), None, None),
            P(("ctx_hi", "ctx_lo", "head"), None, None),
        ),
        out_specs=P(("group", "ctx_hi", "ctx_lo", "head"), None),
        check_vma=False,
    )
```

```python
import jax
import jax.numpy as jnp
from jax import lax
from jax.sharding import Mesh, PartitionSpec as P

D = 2048
DK = 128
DV = 128
BLOCK = 64
CTX = ("ctx_hi", "ctx_lo")


HIGHEST = lax.Precision.HIGH


def passed_along(block, axis, distance):
    devices = range(lax.axis_size(axis))
    route = [(i - distance, i) for i in devices if i - distance in devices]
    return lax.ppermute(block, axis, route)


def scanned_entry(whole_map, whole_shift, axis):
    peers, position = (lax.axis_size(axis), lax.axis_index(axis))
    distance = 1
    while distance < peers:
        last = 2 * distance >= peers
        reached = position >= distance
        if last:
            shift_in = passed_along(whole_shift.astype(jnp.bfloat16), axis, distance)
            shift_in = shift_in.astype(jnp.float32)
        else:
            both = jnp.stack([whole_map, whole_shift]).astype(jnp.bfloat16)
            both_in = passed_along(both, axis, distance).astype(jnp.float32)
            map_in, shift_in = (both_in[0], both_in[1])
        new_shift = batched(whole_map, shift_in) + whole_shift
        if not last:
            whole_map = jnp.where(reached, batched(whole_map, map_in), whole_map)
        whole_shift = jnp.where(reached, new_shift, whole_shift)
        distance *= 2
    return passed_along(whole_shift.astype(jnp.bfloat16), axis, 1).astype(jnp.float32)


def precise_dot(left, right):
    return jnp.dot(left, right, precision=HIGHEST, preferred_element_type=jnp.float32)


def causal_filter(padded_raw, filter_taps, padded_ids, kernel):
    length = padded_raw.shape[0] - (kernel - 1)
    source = padded_raw.astype(jnp.float32)
    current_ids = padded_ids[kernel - 1 :]
    summed = jnp.zeros((length, padded_raw.shape[1]), jnp.float32)
    for lag_step in range(kernel):
        offset_start = kernel - 1 - lag_step
        shifted = source[offset_start : offset_start + length]
        matching = (padded_ids[offset_start : offset_start + length] == current_ids).astype(
            jnp.float32
        )
        summed = summed + filter_taps[lag_step] * shifted * matching[:, None]
    return jax.nn.silu(summed)


def unit_rows(values_in):
    return values_in / jnp.sqrt(jnp.sum(values_in * values_in, axis=-1, keepdims=True) + 1e-06)


def mixer_inputs(pair_padded, value_padded, pair_filter, value_filter, padded_ids, kernel):
    pair_act = causal_filter(pair_padded, pair_filter.reshape(kernel, -1), padded_ids, kernel)
    length = pair_act.shape[0]
    pair_heads = pair_act.reshape(length, 2, -1, DK)
    queries = unit_rows(pair_heads[:, 0]) * DK ** (-0.5)
    key_rows = unit_rows(pair_heads[:, 1])
    value_rows = causal_filter(value_padded, value_filter, padded_ids, kernel).reshape(
        length, -1, DV
    )
    repeat_factor = value_rows.shape[1] // key_rows.shape[1]
    return (
        jnp.repeat(queries, repeat_factor, axis=1),
        jnp.repeat(key_rows, repeat_factor, axis=1),
        value_rows,
    )


def unit_lower_inverse(system):
    size = system.shape[-1]
    row_index = lax.broadcasted_iota(jnp.int32, (size, size), 0)
    col_index = lax.broadcasted_iota(jnp.int32, (size, size), 1)
    inverse = jnp.broadcast_to(jnp.eye(size, dtype=system.dtype), system.shape)
    width = 1
    while width < size:
        linking = (
            (row_index // (2 * width) == col_index // (2 * width))
            & ((row_index // width) % 2 == 1)
            & ((col_index // width) % 2 == 0)
        )
        lower_left = jnp.where(linking, system, 0.0)
        inverse = inverse - precise_dot(inverse, precise_dot(lower_left, inverse))
        width *= 2
    return inverse


def block_setup(queries, key_rows, value_rows, strength, decay_rows, segment_here, prior_id):
    cumulative = jnp.cumsum(decay_rows)
    row_index = lax.broadcasted_iota(jnp.int32, (BLOCK, BLOCK), 0)
    col_index = lax.broadcasted_iota(jnp.int32, (BLOCK, BLOCK), 1)
    same_segment = segment_here[:, None] == segment_here[None, :]
    causal = (row_index >= col_index) & same_segment
    strictly = (row_index > col_index) & same_segment
    decay_matrix = jnp.where(
        causal, jnp.exp(jnp.where(causal, cumulative[:, None] - cumulative[None, :], 0.0)), 0.0
    )
    carried_in = (segment_here == prior_id).astype(jnp.float32)
    keyed_beta = key_rows * strength[:, None]
    coupling = jnp.where(strictly, precise_dot(keyed_beta, key_rows.T) * decay_matrix, 0.0)
    system = jnp.eye(BLOCK, dtype=jnp.float32) + coupling
    stacked = jnp.concatenate(
        [value_rows * strength[:, None], keyed_beta * (jnp.exp(cumulative) * carried_in)[:, None]],
        axis=1,
    )
    solved = precise_dot(unit_lower_inverse(system), stacked)
    targets = solved[:, :DV]
    corrector = solved[:, DV:]
    within = jnp.where(causal, precise_dot(queries, key_rows.T) * decay_matrix, 0.0)
    query_decayed = queries * (jnp.exp(cumulative) * carried_in)[:, None]
    final_log = cumulative[BLOCK - 1]
    weighting = (segment_here == segment_here[BLOCK - 1]).astype(jnp.float32) * jnp.exp(
        final_log - cumulative
    )
    keys_weighted = key_rows * weighting[:, None]
    transition = jnp.exp(final_log) * carried_in[BLOCK - 1] * jnp.eye(
        DK, dtype=jnp.float32
    ) - precise_dot(keys_weighted.T, corrector)
    increment = precise_dot(keys_weighted.T, targets)
    return (within, query_decayed, targets, corrector, transition, increment)


def head_major(array_in, block_count):
    moved = jnp.moveaxis(array_in, 1, 0)
    return moved.reshape((array_in.shape[1], block_count, BLOCK) + array_in.shape[2:])


def block_tables(queries, key_rows, value_rows, strength, decay_rows, padded_ids, kernel):
    length = queries.shape[0]
    block_count = length // BLOCK
    current_ids = padded_ids[kernel - 1 :].reshape(block_count, BLOCK)
    prior_ids = padded_ids[kernel - 2 : kernel - 2 + length : BLOCK]
    per_block = jax.vmap(block_setup, in_axes=(0, 0, 0, 0, 0, 0, 0))
    per_head = jax.vmap(per_block, in_axes=(0, 0, 0, 0, 0, None, None))
    return per_head(
        head_major(queries, block_count),
        head_major(key_rows, block_count),
        head_major(value_rows, block_count),
        head_major(strength, block_count),
        head_major(decay_rows, block_count),
        current_ids,
        prior_ids,
    )


def blockwise(left, right):
    return jnp.einsum("hbij,hbjk->hbik", left, right, precision=HIGHEST)


def batched(left, right):
    return jnp.einsum("hij,hjk->hik", left, right, precision=HIGHEST)


def sweep_blocks(block_terms, start_state):
    blocks_first = tuple((jnp.swapaxes(member, 0, 1) for member in block_terms))

    def advance(carry_state, pieces):
        within, query_decayed, targets, corrector, transition, increment = pieces
        fresh_values = targets - batched(corrector, carry_state)
        emitted = batched(query_decayed, carry_state) + batched(within, fresh_values)
        updated = batched(transition, carry_state) + increment
        return (updated, emitted)

    final_state, emitted = lax.scan(advance, start_state, blocks_first)
    return emitted


def tokens_first(emitted):
    heads_count = emitted.shape[1]
    return jnp.transpose(emitted, (0, 2, 1, 3)).reshape(-1, heads_count, emitted.shape[3])


def gate_output(mixed_heads, gate_raw, norm_gain):
    square_mean = jnp.mean(mixed_heads * mixed_heads, axis=-1, keepdims=True)
    gate_values = jax.nn.silu(gate_raw.reshape(mixed_heads.shape).astype(jnp.float32))
    normed = mixed_heads / jnp.sqrt(square_mean + 1e-06) * norm_gain * gate_values
    return normed.astype(jnp.bfloat16).reshape(mixed_heads.shape[0], -1)


def post_norm(hidden, post_gain):
    hidden_full = hidden.astype(jnp.float32)
    square_mean = jnp.mean(hidden_full * hidden_full, axis=-1, keepdims=True)
    return (hidden_full / jnp.sqrt(square_mean + 1e-06) * post_gain).astype(jnp.bfloat16)


def expert_apply_rows(rows_in, up_matrix, down_matrix):
    hidden_units = down_matrix.shape[0]
    gate_up = jnp.dot(rows_in, up_matrix, preferred_element_type=jnp.float32)
    activated = (jax.nn.silu(gate_up[:, :hidden_units]) * gate_up[:, hidden_units:]).astype(
        jnp.bfloat16
    )
    return jnp.dot(activated, down_matrix, preferred_element_type=jnp.float32).astype(jnp.bfloat16)


def expert_apply(arrived, expert_up, expert_down):
    member_rows = arrived[:, 0]
    flattened = member_rows.reshape(-1, member_rows.shape[-1])
    result = expert_apply_rows(flattened, expert_up[0], expert_down[0])
    outputs = [result.reshape(member_rows.shape)]
    return jnp.stack(outputs, axis=1)


def route_slots(routes, experts_all, capacity):
    assigned = routes.reshape(-1)
    expert_ids = jnp.arange(experts_all, dtype=jnp.int32)
    onehot = (assigned[:, None] == expert_ids[None, :]).astype(jnp.int32)
    slot_rank = jnp.sum((jnp.cumsum(onehot, axis=0) - 1) * onehot, axis=1)
    return assigned * capacity + slot_rank


def per_device(
    pair_raw,
    value_raw,
    gate_raw,
    write_strength,
    log_decay,
    segment_ids,
    pair_filter,
    value_filter,
    norm_gain,
    out_weight,
    residual,
    post_gain,
    routes,
    route_weights,
    expert_up,
    expert_down,
):
    local_tokens = pair_raw.shape[0]
    kernel = value_filter.shape[0]
    pair_flat = pair_raw.reshape(local_tokens, -1)
    pair_width = pair_flat.shape[1]
    rim_rows = jnp.concatenate(
        [pair_flat[local_tokens - (kernel - 1) :], value_raw[local_tokens - (kernel - 1) :]], axis=1
    )
    before = passed_along(rim_rows, CTX, 1)
    first_token = lax.axis_index(CTX) * local_tokens
    padded_ids = jnp.concatenate([jnp.full((kernel - 1,), -1, jnp.int32), segment_ids])
    window_ids = lax.dynamic_slice_in_dim(padded_ids, first_token, local_tokens + kernel - 1)
    pair_padded = jnp.concatenate([before[:, :pair_width], pair_flat])
    value_padded = jnp.concatenate([before[:, pair_width:], value_raw])
    queries, key_rows, value_rows = mixer_inputs(
        pair_padded, value_padded, pair_filter, value_filter, window_ids, kernel
    )
    block_terms = block_tables(
        queries, key_rows, value_rows, write_strength, log_decay, window_ids, kernel
    )
    within, query_decayed, targets, corrector, transition, increment = block_terms
    heads_here, block_count = transition.shape[:2]
    prefix_map = jnp.broadcast_to(jnp.eye(DK, dtype=jnp.float32), (heads_here, DK, DK))
    prefix_shift = jnp.zeros((heads_here, DK, DV), jnp.float32)
    prefix_maps, prefix_shifts = ([], [])
    for block in range(block_count):
        prefix_maps.append(prefix_map)
        prefix_shifts.append(prefix_shift)
        prefix_map = batched(transition[:, block], prefix_map)
        prefix_shift = batched(transition[:, block], prefix_shift) + increment[:, block]
    stacked_maps = jnp.stack(prefix_maps, axis=1)
    stacked_shifts = jnp.stack(prefix_shifts, axis=1)
    query_effective = query_decayed - blockwise(within, corrector)
    through_entry = blockwise(query_effective, stacked_maps)
    fixed_part = blockwise(query_effective, stacked_shifts) + blockwise(within, targets)
    entering = scanned_entry(prefix_map, prefix_shift, CTX)
    emitted = (
        jnp.einsum("hbtk,hkv->hbtv", through_entry, entering, precision=HIGHEST) + fixed_part
    )
    mixed_heads = jnp.transpose(emitted, (1, 2, 0, 3)).reshape(-1, heads_here, DV)
    gated_out = gate_output(mixed_heads, gate_raw, norm_gain)
    partial_out = jnp.dot(gated_out, out_weight, preferred_element_type=jnp.float32)
    pairs = lax.axis_size("head")
    if pairs == 2:
        side = lax.axis_index("head")
        halves = partial_out.reshape(2, -1, partial_out.shape[1])
        kept = lax.dynamic_index_in_dim(halves, side, keepdims=False)
        given = lax.dynamic_index_in_dim(halves, 1 - side, keepdims=False)
        attention = kept + lax.ppermute(
            given.astype(jnp.bfloat16), "head", [(0, 1), (1, 0)]
        ).astype(jnp.float32)
    else:
        attention = lax.psum_scatter(
            partial_out.astype(jnp.bfloat16), "head", scatter_dimension=0, tiled=True
        ).astype(jnp.float32)
    hidden = (residual.astype(jnp.float32) + attention).astype(jnp.bfloat16)
    expert_in = post_norm(hidden, post_gain)
    levels = lax.axis_size("ctx_hi")
    level = lax.axis_index("ctx_hi")
    local_experts = expert_up.shape[0]
    per_level = lax.axis_size("ctx_lo") * lax.axis_size("head") * local_experts
    experts_all = levels * per_level
    local_rows = routes.shape[0]
    top_count = routes.shape[1]
    capacity = local_rows * top_count * 5 // (4 * experts_all)
    own_high = route_weights.astype(jnp.bfloat16)
    own_low = (route_weights - own_high.astype(jnp.float32)).astype(jnp.bfloat16)
    spare = -(-(3 * top_count) // 128) * 128 - 3 * top_count
    packed = jnp.concatenate(
        [
            expert_in,
            routes.astype(jnp.bfloat16),
            own_high,
            own_low,
            jnp.zeros((local_rows, spare), jnp.bfloat16),
        ],
        axis=1,
    )
    expert_ids = jnp.arange(experts_all, dtype=jnp.int32)
    earlier_rows = (
        lax.broadcasted_iota(jnp.int32, (local_rows, local_rows), 0)
        > lax.broadcasted_iota(jnp.int32, (local_rows, local_rows), 1)
    ).astype(jnp.bfloat16)
    slots_total = per_level * capacity
    slot_ids = jnp.arange(slots_total, dtype=jnp.int32)
    level_axes = ("ctx_lo", "head")
    routed = None
    for turn in range(levels):
        if turn == 0:
            chunk = packed
        else:
            chunk = lax.ppermute(
                packed, "ctx_hi", [(i, (i - turn) % levels) for i in range(levels)]
            )
        chunk_in = chunk[:, :D]
        chunk_routes = chunk[:, D : D + top_count].astype(jnp.int32)
        chunk_high = chunk[:, D + top_count : D + 2 * top_count]
        chunk_low = chunk[:, D + 2 * top_count : D + 3 * top_count]
        route_hot = chunk_routes[:, :, None] == expert_ids[None, None, :]
        row_hot = jnp.any(route_hot, axis=1).astype(jnp.bfloat16)
        earlier = jnp.dot(earlier_rows, row_hot, preferred_element_type=jnp.float32)
        slot_rank = jnp.sum(jnp.where(route_hot, earlier[:, None, :], 0.0), axis=2).astype(
            jnp.int32
        )
        slot_index = jnp.where(
            chunk_routes // per_level == level,
            (chunk_routes % per_level) * capacity + slot_rank,
            -1,
        )
        hits = slot_index[:, :, None] == slot_ids[None, None, :]
        picker = jnp.any(hits, axis=1).astype(jnp.bfloat16)
        outgoing = lax.dot_general(
            picker, chunk_in, (((0,), (0,)), ((), ())), preferred_element_type=jnp.float32
        ).astype(jnp.bfloat16)
        outgoing = outgoing.reshape(per_level // local_experts, local_experts * capacity, D)
        arrived = lax.all_to_all(outgoing, level_axes, split_axis=0, concat_axis=0, tiled=True)
        arrived = arrived.reshape(per_level // local_experts, local_experts, capacity, D)
        answered = jnp.stack(
            [
                expert_apply_rows(
                    arrived[:, member].reshape(-1, D), expert_up[member], expert_down[member]
                ).reshape(arrived.shape[0], capacity, D)
                for member in range(local_experts)
            ],
            axis=1,
        ).reshape(per_level // local_experts, local_experts * capacity, D)
        returned = lax.all_to_all(answered, level_axes, split_axis=0, concat_axis=0, tiled=True)
        result_rows = returned.reshape(slots_total, D)
        weight_high = jnp.sum(jnp.where(hits, chunk_high[:, :, None], 0.0), axis=1).astype(
            jnp.bfloat16
        )
        weight_low = jnp.sum(jnp.where(hits, chunk_low[:, :, None], 0.0), axis=1).astype(
            jnp.bfloat16
        )
        partial = jnp.dot(weight_high, result_rows, preferred_element_type=jnp.float32) + jnp.dot(
            weight_low, result_rows, preferred_element_type=jnp.float32
        )
        if turn == 0:
            routed = partial
        else:
            routed = routed + lax.ppermute(
                partial.astype(jnp.bfloat16),
                "ctx_hi",
                [(i, (i + turn) % levels) for i in range(levels)],
            ).astype(jnp.float32)
    combined = hidden.astype(jnp.float32) + routed
    return combined.astype(jnp.bfloat16)


def split_mesh(mesh):
    groups, peers, pairs = (mesh.shape["group"], mesh.shape["ctx"], mesh.shape["head"])
    low = 4 if peers % 4 == 0 else 1
    devices = mesh.devices.reshape(groups, peers // low, low, pairs)
    return Mesh(devices, ("group", "ctx_hi", "ctx_lo", "head"))


def solution(mesh):
    return jax.shard_map(
        per_device,
        mesh=split_mesh(mesh),
        in_specs=(
            P(("group", "ctx_hi", "ctx_lo"), None, "head"),
            P(("group", "ctx_hi", "ctx_lo"), "head"),
            P(("group", "ctx_hi", "ctx_lo"), "head"),
            P(("group", "ctx_hi", "ctx_lo"), "head"),
            P(("group", "ctx_hi", "ctx_lo"), "head"),
            P("group"),
            P(None, None, "head"),
            P(None, "head"),
            P(),
            P("head", None),
            P(("group", "ctx_hi", "ctx_lo", "head"), None),
            P(),
            P(("group", "ctx_hi", "ctx_lo", "head"), None),
            P(("group", "ctx_hi", "ctx_lo", "head"), None),
            P(("ctx_hi", "ctx_lo", "head"), None, None),
            P(("ctx_hi", "ctx_lo", "head"), None, None),
        ),
        out_specs=P(("group", "ctx_hi", "ctx_lo", "head"), None),
        check_vma=False,
    )
```

```python
import jax
import jax.numpy as jnp
from jax import lax
from jax.sharding import Mesh, PartitionSpec as P

D = 2048
DK = 128
DV = 128
BLOCK = 64
CTX = ("ctx_hi", "ctx_lo")


HIGHEST = lax.Precision.HIGH


def passed_along(block, axis, distance):
    devices = range(lax.axis_size(axis))
    route = [(i - distance, i) for i in devices if i - distance in devices]
    return lax.ppermute(block, axis, route)


def scanned_entry(whole_map, whole_shift, axis):
    peers, position = (lax.axis_size(axis), lax.axis_index(axis))
    distance = 1
    while distance < peers:
        last = 2 * distance >= peers
        reached = position >= distance
        if last:
            shift_in = passed_along(whole_shift.astype(jnp.bfloat16), axis, distance)
            shift_in = shift_in.astype(jnp.float32)
        else:
            both = jnp.stack([whole_map, whole_shift]).astype(jnp.bfloat16)
            both_in = passed_along(both, axis, distance).astype(jnp.float32)
            map_in, shift_in = (both_in[0], both_in[1])
        new_shift = batched(whole_map, shift_in) + whole_shift
        if not last:
            whole_map = jnp.where(reached, batched(whole_map, map_in), whole_map)
        whole_shift = jnp.where(reached, new_shift, whole_shift)
        distance *= 2
    return passed_along(whole_shift.astype(jnp.bfloat16), axis, 1).astype(jnp.float32)


def precise_dot(left, right):
    return jnp.dot(left, right, precision=HIGHEST, preferred_element_type=jnp.float32)


def causal_filter(padded_raw, filter_taps, padded_ids, kernel):
    length = padded_raw.shape[0] - (kernel - 1)
    source = padded_raw.astype(jnp.float32)
    current_ids = padded_ids[kernel - 1 :]
    summed = jnp.zeros((length, padded_raw.shape[1]), jnp.float32)
    for lag_step in range(kernel):
        offset_start = kernel - 1 - lag_step
        shifted = source[offset_start : offset_start + length]
        matching = (padded_ids[offset_start : offset_start + length] == current_ids).astype(
            jnp.float32
        )
        summed = summed + filter_taps[lag_step] * shifted * matching[:, None]
    return jax.nn.silu(summed)


def unit_rows(values_in):
    return values_in / jnp.sqrt(jnp.sum(values_in * values_in, axis=-1, keepdims=True) + 1e-06)


def mixer_inputs(pair_padded, value_padded, pair_filter, value_filter, padded_ids, kernel):
    pair_act = causal_filter(pair_padded, pair_filter.reshape(kernel, -1), padded_ids, kernel)
    length = pair_act.shape[0]
    pair_heads = pair_act.reshape(length, 2, -1, DK)
    queries = unit_rows(pair_heads[:, 0]) * DK ** (-0.5)
    key_rows = unit_rows(pair_heads[:, 1])
    value_rows = causal_filter(value_padded, value_filter, padded_ids, kernel).reshape(
        length, -1, DV
    )
    repeat_factor = value_rows.shape[1] // key_rows.shape[1]
    return (
        jnp.repeat(queries, repeat_factor, axis=1),
        jnp.repeat(key_rows, repeat_factor, axis=1),
        value_rows,
    )


def unit_lower_inverse(system):
    size = system.shape[-1]
    row_index = lax.broadcasted_iota(jnp.int32, (size, size), 0)
    col_index = lax.broadcasted_iota(jnp.int32, (size, size), 1)
    inverse = jnp.broadcast_to(jnp.eye(size, dtype=system.dtype), system.shape)
    width = 1
    while width < size:
        linking = (
            (row_index // (2 * width) == col_index // (2 * width))
            & ((row_index // width) % 2 == 1)
            & ((col_index // width) % 2 == 0)
        )
        lower_left = jnp.where(linking, system, 0.0)
        inverse = inverse - precise_dot(inverse, precise_dot(lower_left, inverse))
        width *= 2
    return inverse


def block_setup(queries, key_rows, value_rows, strength, decay_rows, segment_here, prior_id):
    cumulative = jnp.cumsum(decay_rows)
    row_index = lax.broadcasted_iota(jnp.int32, (BLOCK, BLOCK), 0)
    col_index = lax.broadcasted_iota(jnp.int32, (BLOCK, BLOCK), 1)
    same_segment = segment_here[:, None] == segment_here[None, :]
    causal = (row_index >= col_index) & same_segment
    strictly = (row_index > col_index) & same_segment
    decay_matrix = jnp.where(
        causal, jnp.exp(jnp.where(causal, cumulative[:, None] - cumulative[None, :], 0.0)), 0.0
    )
    carried_in = (segment_here == prior_id).astype(jnp.float32)
    keyed_beta = key_rows * strength[:, None]
    coupling = jnp.where(strictly, precise_dot(keyed_beta, key_rows.T) * decay_matrix, 0.0)
    system = jnp.eye(BLOCK, dtype=jnp.float32) + coupling
    stacked = jnp.concatenate(
        [value_rows * strength[:, None], keyed_beta * (jnp.exp(cumulative) * carried_in)[:, None]],
        axis=1,
    )
    solved = precise_dot(unit_lower_inverse(system), stacked)
    targets = solved[:, :DV]
    corrector = solved[:, DV:]
    within = jnp.where(causal, precise_dot(queries, key_rows.T) * decay_matrix, 0.0)
    query_decayed = queries * (jnp.exp(cumulative) * carried_in)[:, None]
    final_log = cumulative[BLOCK - 1]
    weighting = (segment_here == segment_here[BLOCK - 1]).astype(jnp.float32) * jnp.exp(
        final_log - cumulative
    )
    keys_weighted = key_rows * weighting[:, None]
    transition = jnp.exp(final_log) * carried_in[BLOCK - 1] * jnp.eye(
        DK, dtype=jnp.float32
    ) - precise_dot(keys_weighted.T, corrector)
    increment = precise_dot(keys_weighted.T, targets)
    return (within, query_decayed, targets, corrector, transition, increment)


def head_major(array_in, block_count):
    moved = jnp.moveaxis(array_in, 1, 0)
    return moved.reshape((array_in.shape[1], block_count, BLOCK) + array_in.shape[2:])


def block_tables(queries, key_rows, value_rows, strength, decay_rows, padded_ids, kernel):
    length = queries.shape[0]
    block_count = length // BLOCK
    current_ids = padded_ids[kernel - 1 :].reshape(block_count, BLOCK)
    prior_ids = padded_ids[kernel - 2 : kernel - 2 + length : BLOCK]
    per_block = jax.vmap(block_setup, in_axes=(0, 0, 0, 0, 0, 0, 0))
    per_head = jax.vmap(per_block, in_axes=(0, 0, 0, 0, 0, None, None))
    return per_head(
        head_major(queries, block_count),
        head_major(key_rows, block_count),
        head_major(value_rows, block_count),
        head_major(strength, block_count),
        head_major(decay_rows, block_count),
        current_ids,
        prior_ids,
    )


def blockwise(left, right):
    return jnp.einsum("hbij,hbjk->hbik", left, right, precision=HIGHEST)


def batched(left, right):
    return jnp.einsum("hij,hjk->hik", left, right, precision=HIGHEST)


def sweep_blocks(block_terms, start_state):
    blocks_first = tuple((jnp.swapaxes(member, 0, 1) for member in block_terms))

    def advance(carry_state, pieces):
        within, query_decayed, targets, corrector, transition, increment = pieces
        fresh_values = targets - batched(corrector, carry_state)
        emitted = batched(query_decayed, carry_state) + batched(within, fresh_values)
        updated = batched(transition, carry_state) + increment
        return (updated, emitted)

    final_state, emitted = lax.scan(advance, start_state, blocks_first)
    return emitted


def tokens_first(emitted):
    heads_count = emitted.shape[1]
    return jnp.transpose(emitted, (0, 2, 1, 3)).reshape(-1, heads_count, emitted.shape[3])


def gate_output(mixed_heads, gate_raw, norm_gain):
    square_mean = jnp.mean(mixed_heads * mixed_heads, axis=-1, keepdims=True)
    gate_values = jax.nn.silu(gate_raw.reshape(mixed_heads.shape).astype(jnp.float32))
    normed = mixed_heads / jnp.sqrt(square_mean + 1e-06) * norm_gain * gate_values
    return normed.astype(jnp.bfloat16).reshape(mixed_heads.shape[0], -1)


def post_norm(hidden, post_gain):
    hidden_full = hidden.astype(jnp.float32)
    square_mean = jnp.mean(hidden_full * hidden_full, axis=-1, keepdims=True)
    return (hidden_full / jnp.sqrt(square_mean + 1e-06) * post_gain).astype(jnp.bfloat16)


def expert_apply_rows(rows_in, up_matrix, down_matrix):
    hidden_units = down_matrix.shape[0]
    gate_up = jnp.dot(rows_in, up_matrix, preferred_element_type=jnp.float32)
    activated = (jax.nn.silu(gate_up[:, :hidden_units]) * gate_up[:, hidden_units:]).astype(
        jnp.bfloat16
    )
    return jnp.dot(activated, down_matrix, preferred_element_type=jnp.float32).astype(jnp.bfloat16)


def expert_apply(arrived, expert_up, expert_down):
    member_rows = arrived[:, 0]
    flattened = member_rows.reshape(-1, member_rows.shape[-1])
    result = expert_apply_rows(flattened, expert_up[0], expert_down[0])
    outputs = [result.reshape(member_rows.shape)]
    return jnp.stack(outputs, axis=1)


def route_slots(routes, experts_all, capacity):
    assigned = routes.reshape(-1)
    expert_ids = jnp.arange(experts_all, dtype=jnp.int32)
    onehot = (assigned[:, None] == expert_ids[None, :]).astype(jnp.int32)
    slot_rank = jnp.sum((jnp.cumsum(onehot, axis=0) - 1) * onehot, axis=1)
    return assigned * capacity + slot_rank


def per_device(
    pair_raw,
    value_raw,
    gate_raw,
    write_strength,
    log_decay,
    segment_ids,
    pair_filter,
    value_filter,
    norm_gain,
    out_weight,
    residual,
    post_gain,
    routes,
    route_weights,
    expert_up,
    expert_down,
):
    local_tokens = pair_raw.shape[0]
    kernel = value_filter.shape[0]
    pair_flat = pair_raw.reshape(local_tokens, -1)
    pair_width = pair_flat.shape[1]
    rim_rows = jnp.concatenate(
        [pair_flat[local_tokens - (kernel - 1) :], value_raw[local_tokens - (kernel - 1) :]], axis=1
    )
    before = passed_along(rim_rows, CTX, 1)
    first_token = lax.axis_index(CTX) * local_tokens
    padded_ids = jnp.concatenate([jnp.full((kernel - 1,), -1, jnp.int32), segment_ids])
    window_ids = lax.dynamic_slice_in_dim(padded_ids, first_token, local_tokens + kernel - 1)
    pair_padded = jnp.concatenate([before[:, :pair_width], pair_flat])
    value_padded = jnp.concatenate([before[:, pair_width:], value_raw])
    queries, key_rows, value_rows = mixer_inputs(
        pair_padded, value_padded, pair_filter, value_filter, window_ids, kernel
    )
    block_terms = block_tables(
        queries, key_rows, value_rows, write_strength, log_decay, window_ids, kernel
    )
    within, query_decayed, targets, corrector, transition, increment = block_terms
    heads_here, block_count = transition.shape[:2]
    prefix_map = jnp.broadcast_to(jnp.eye(DK, dtype=jnp.float32), (heads_here, DK, DK))
    prefix_shift = jnp.zeros((heads_here, DK, DV), jnp.float32)
    prefix_maps, prefix_shifts = ([], [])
    for block in range(block_count):
        prefix_maps.append(prefix_map)
        prefix_shifts.append(prefix_shift)
        prefix_map = batched(transition[:, block], prefix_map)
        prefix_shift = batched(transition[:, block], prefix_shift) + increment[:, block]
    stacked_maps = jnp.stack(prefix_maps, axis=1)
    stacked_shifts = jnp.stack(prefix_shifts, axis=1)
    query_effective = query_decayed - blockwise(within, corrector)
    through_entry = blockwise(query_effective, stacked_maps)
    fixed_part = blockwise(query_effective, stacked_shifts) + blockwise(within, targets)
    entering = scanned_entry(prefix_map, prefix_shift, CTX)
    emitted = (
        jnp.einsum("hbtk,hkv->hbtv", through_entry, entering, precision=HIGHEST) + fixed_part
    )
    mixed_heads = jnp.transpose(emitted, (1, 2, 0, 3)).reshape(-1, heads_here, DV)
    gated_out = gate_output(mixed_heads, gate_raw, norm_gain)
    partial_out = jnp.dot(gated_out, out_weight, preferred_element_type=jnp.float32)
    pairs = lax.axis_size("head")
    if pairs == 2:
        side = lax.axis_index("head")
        halves = partial_out.reshape(2, -1, partial_out.shape[1])
        kept = lax.dynamic_index_in_dim(halves, side, keepdims=False)
        given = lax.dynamic_index_in_dim(halves, 1 - side, keepdims=False)
        attention = kept + lax.ppermute(
            given.astype(jnp.bfloat16), "head", [(0, 1), (1, 0)]
        ).astype(jnp.float32)
    else:
        attention = lax.psum_scatter(
            partial_out.astype(jnp.bfloat16), "head", scatter_dimension=0, tiled=True
        ).astype(jnp.float32)
    hidden = (residual.astype(jnp.float32) + attention).astype(jnp.bfloat16)
    expert_in = post_norm(hidden, post_gain)
    levels = lax.axis_size("ctx_hi")
    level = lax.axis_index("ctx_hi")
    local_experts = expert_up.shape[0]
    per_level = lax.axis_size("ctx_lo") * lax.axis_size("head") * local_experts
    experts_all = levels * per_level
    local_rows = routes.shape[0]
    top_count = routes.shape[1]
    capacity = local_rows * top_count * 5 // (4 * experts_all)
    own_high = route_weights.astype(jnp.bfloat16)
    own_low = (route_weights - own_high.astype(jnp.float32)).astype(jnp.bfloat16)
    spare = -(-(3 * top_count) // 128) * 128 - 3 * top_count
    packed = jnp.concatenate(
        [
            expert_in,
            routes.astype(jnp.bfloat16),
            own_high,
            own_low,
            jnp.zeros((local_rows, spare), jnp.bfloat16),
        ],
        axis=1,
    )
    expert_ids = jnp.arange(experts_all, dtype=jnp.int32)
    earlier_rows = (
        lax.broadcasted_iota(jnp.int32, (local_rows, local_rows), 0)
        > lax.broadcasted_iota(jnp.int32, (local_rows, local_rows), 1)
    ).astype(jnp.bfloat16)
    slots_total = per_level * capacity
    slot_ids = jnp.arange(slots_total, dtype=jnp.int32)
    level_axes = ("ctx_lo", "head")
    routed = None
    for turn in list(range(1, levels)) + [0]:
        if turn == 0:
            chunk = packed
        else:
            chunk = lax.ppermute(
                packed, "ctx_hi", [(i, (i - turn) % levels) for i in range(levels)]
            )
        chunk_in = chunk[:, :D]
        chunk_routes = chunk[:, D : D + top_count].astype(jnp.int32)
        chunk_high = chunk[:, D + top_count : D + 2 * top_count]
        chunk_low = chunk[:, D + 2 * top_count : D + 3 * top_count]
        route_hot = chunk_routes[:, :, None] == expert_ids[None, None, :]
        row_hot = jnp.any(route_hot, axis=1).astype(jnp.bfloat16)
        earlier = jnp.dot(earlier_rows, row_hot, preferred_element_type=jnp.float32)
        slot_rank = jnp.sum(jnp.where(route_hot, earlier[:, None, :], 0.0), axis=2).astype(
            jnp.int32
        )
        slot_index = jnp.where(
            chunk_routes // per_level == level,
            (chunk_routes % per_level) * capacity + slot_rank,
            -1,
        )
        hits = slot_index[:, :, None] == slot_ids[None, None, :]
        picker = jnp.any(hits, axis=1).astype(jnp.bfloat16)
        outgoing = lax.dot_general(
            picker, chunk_in, (((0,), (0,)), ((), ())), preferred_element_type=jnp.float32
        ).astype(jnp.bfloat16)
        outgoing = outgoing.reshape(per_level // local_experts, local_experts * capacity, D)
        arrived = lax.all_to_all(outgoing, level_axes, split_axis=0, concat_axis=0, tiled=True)
        arrived = arrived.reshape(per_level // local_experts, local_experts, capacity, D)
        answered = jnp.stack(
            [
                expert_apply_rows(
                    arrived[:, member].reshape(-1, D), expert_up[member], expert_down[member]
                ).reshape(arrived.shape[0], capacity, D)
                for member in range(local_experts)
            ],
            axis=1,
        ).reshape(per_level // local_experts, local_experts * capacity, D)
        returned = lax.all_to_all(answered, level_axes, split_axis=0, concat_axis=0, tiled=True)
        result_rows = returned.reshape(slots_total, D)
        weight_high = jnp.sum(jnp.where(hits, chunk_high[:, :, None], 0.0), axis=1).astype(
            jnp.bfloat16
        )
        weight_low = jnp.sum(jnp.where(hits, chunk_low[:, :, None], 0.0), axis=1).astype(
            jnp.bfloat16
        )
        partial = jnp.dot(weight_high, result_rows, preferred_element_type=jnp.float32) + jnp.dot(
            weight_low, result_rows, preferred_element_type=jnp.float32
        )
        if turn == 0:
            routed = partial if routed is None else routed + partial
        else:
            carried = lax.ppermute(
                partial.astype(jnp.bfloat16),
                "ctx_hi",
                [(i, (i + turn) % levels) for i in range(levels)],
            ).astype(jnp.float32)
            routed = carried if routed is None else routed + carried
    combined = hidden.astype(jnp.float32) + routed
    return combined.astype(jnp.bfloat16)


def split_mesh(mesh):
    groups, peers, pairs = (mesh.shape["group"], mesh.shape["ctx"], mesh.shape["head"])
    low = 4 if peers % 4 == 0 else 1
    devices = mesh.devices.reshape(groups, peers // low, low, pairs)
    return Mesh(devices, ("group", "ctx_hi", "ctx_lo", "head"))


def solution(mesh):
    return jax.shard_map(
        per_device,
        mesh=split_mesh(mesh),
        in_specs=(
            P(("group", "ctx_hi", "ctx_lo"), None, "head"),
            P(("group", "ctx_hi", "ctx_lo"), "head"),
            P(("group", "ctx_hi", "ctx_lo"), "head"),
            P(("group", "ctx_hi", "ctx_lo"), "head"),
            P(("group", "ctx_hi", "ctx_lo"), "head"),
            P("group"),
            P(None, None, "head"),
            P(None, "head"),
            P(),
            P("head", None),
            P(("group", "ctx_hi", "ctx_lo", "head"), None),
            P(),
            P(("group", "ctx_hi", "ctx_lo", "head"), None),
            P(("group", "ctx_hi", "ctx_lo", "head"), None),
            P(("ctx_hi", "ctx_lo", "head"), None, None),
            P(("ctx_hi", "ctx_lo", "head"), None, None),
        ),
        out_specs=P(("group", "ctx_hi", "ctx_lo", "head"), None),
        check_vma=False,
    )
```

```python
import jax
import jax.numpy as jnp
from jax import lax
from jax.sharding import Mesh, PartitionSpec as P

D = 2048
DK = 128
DV = 128
BLOCK = 64
CTX = ("ctx_hi", "ctx_lo")


HIGHEST = lax.Precision.HIGH
LEAF = lax.Precision.DEFAULT


def passed_along(block, axis, distance):
    devices = range(lax.axis_size(axis))
    route = [(i - distance, i) for i in devices if i - distance in devices]
    return lax.ppermute(block, axis, route)


def scanned_entry(whole_map, whole_shift, axis):
    peers, position = (lax.axis_size(axis), lax.axis_index(axis))
    distance = 1
    while distance < peers:
        last = 2 * distance >= peers
        reached = position >= distance
        if last:
            shift_in = passed_along(whole_shift.astype(jnp.bfloat16), axis, distance)
            shift_in = shift_in.astype(jnp.float32)
        else:
            both = jnp.stack([whole_map, whole_shift]).astype(jnp.bfloat16)
            both_in = passed_along(both, axis, distance).astype(jnp.float32)
            map_in, shift_in = (both_in[0], both_in[1])
        new_shift = batched(whole_map, shift_in) + whole_shift
        if not last:
            whole_map = jnp.where(reached, batched(whole_map, map_in), whole_map)
        whole_shift = jnp.where(reached, new_shift, whole_shift)
        distance *= 2
    return passed_along(whole_shift.astype(jnp.bfloat16), axis, 1).astype(jnp.float32)


def precise_dot(left, right):
    return jnp.dot(left, right, precision=HIGHEST, preferred_element_type=jnp.float32)


def causal_filter(padded_raw, filter_taps, padded_ids, kernel):
    length = padded_raw.shape[0] - (kernel - 1)
    source = padded_raw.astype(jnp.float32)
    current_ids = padded_ids[kernel - 1 :]
    summed = jnp.zeros((length, padded_raw.shape[1]), jnp.float32)
    for lag_step in range(kernel):
        offset_start = kernel - 1 - lag_step
        shifted = source[offset_start : offset_start + length]
        matching = (padded_ids[offset_start : offset_start + length] == current_ids).astype(
            jnp.float32
        )
        summed = summed + filter_taps[lag_step] * shifted * matching[:, None]
    return jax.nn.silu(summed)


def unit_rows(values_in):
    return values_in / jnp.sqrt(jnp.sum(values_in * values_in, axis=-1, keepdims=True) + 1e-06)


def mixer_inputs(pair_padded, value_padded, pair_filter, value_filter, padded_ids, kernel):
    pair_act = causal_filter(pair_padded, pair_filter.reshape(kernel, -1), padded_ids, kernel)
    length = pair_act.shape[0]
    pair_heads = pair_act.reshape(length, 2, -1, DK)
    queries = unit_rows(pair_heads[:, 0]) * DK ** (-0.5)
    key_rows = unit_rows(pair_heads[:, 1])
    value_rows = causal_filter(value_padded, value_filter, padded_ids, kernel).reshape(
        length, -1, DV
    )
    repeat_factor = value_rows.shape[1] // key_rows.shape[1]
    return (
        jnp.repeat(queries, repeat_factor, axis=1),
        jnp.repeat(key_rows, repeat_factor, axis=1),
        value_rows,
    )


def unit_lower_inverse(system):
    size = system.shape[-1]
    row_index = lax.broadcasted_iota(jnp.int32, (size, size), 0)
    col_index = lax.broadcasted_iota(jnp.int32, (size, size), 1)
    inverse = jnp.broadcast_to(jnp.eye(size, dtype=system.dtype), system.shape)
    width = 1
    while width < size:
        linking = (
            (row_index // (2 * width) == col_index // (2 * width))
            & ((row_index // width) % 2 == 1)
            & ((col_index // width) % 2 == 0)
        )
        lower_left = jnp.where(linking, system, 0.0)
        inverse = inverse - precise_dot(inverse, precise_dot(lower_left, inverse))
        width *= 2
    return inverse


def block_setup(queries, key_rows, value_rows, strength, decay_rows, segment_here, prior_id):
    cumulative = jnp.cumsum(decay_rows)
    row_index = lax.broadcasted_iota(jnp.int32, (BLOCK, BLOCK), 0)
    col_index = lax.broadcasted_iota(jnp.int32, (BLOCK, BLOCK), 1)
    same_segment = segment_here[:, None] == segment_here[None, :]
    causal = (row_index >= col_index) & same_segment
    strictly = (row_index > col_index) & same_segment
    decay_matrix = jnp.where(
        causal, jnp.exp(jnp.where(causal, cumulative[:, None] - cumulative[None, :], 0.0)), 0.0
    )
    carried_in = (segment_here == prior_id).astype(jnp.float32)
    keyed_beta = key_rows * strength[:, None]
    coupling = jnp.where(strictly, precise_dot(keyed_beta, key_rows.T) * decay_matrix, 0.0)
    system = jnp.eye(BLOCK, dtype=jnp.float32) + coupling
    stacked = jnp.concatenate(
        [value_rows * strength[:, None], keyed_beta * (jnp.exp(cumulative) * carried_in)[:, None]],
        axis=1,
    )
    solved = precise_dot(unit_lower_inverse(system), stacked)
    targets = solved[:, :DV]
    corrector = solved[:, DV:]
    within = jnp.where(causal, jnp.dot(queries, key_rows.T, preferred_element_type=jnp.float32) * decay_matrix, 0.0)
    query_decayed = queries * (jnp.exp(cumulative) * carried_in)[:, None]
    final_log = cumulative[BLOCK - 1]
    weighting = (segment_here == segment_here[BLOCK - 1]).astype(jnp.float32) * jnp.exp(
        final_log - cumulative
    )
    keys_weighted = key_rows * weighting[:, None]
    transition = jnp.exp(final_log) * carried_in[BLOCK - 1] * jnp.eye(
        DK, dtype=jnp.float32
    ) - precise_dot(keys_weighted.T, corrector)
    increment = precise_dot(keys_weighted.T, targets)
    return (within, query_decayed, targets, corrector, transition, increment)


def head_major(array_in, block_count):
    moved = jnp.moveaxis(array_in, 1, 0)
    return moved.reshape((array_in.shape[1], block_count, BLOCK) + array_in.shape[2:])


def block_tables(queries, key_rows, value_rows, strength, decay_rows, padded_ids, kernel):
    length = queries.shape[0]
    block_count = length // BLOCK
    current_ids = padded_ids[kernel - 1 :].reshape(block_count, BLOCK)
    prior_ids = padded_ids[kernel - 2 : kernel - 2 + length : BLOCK]
    per_block = jax.vmap(block_setup, in_axes=(0, 0, 0, 0, 0, 0, 0))
    per_head = jax.vmap(per_block, in_axes=(0, 0, 0, 0, 0, None, None))
    return per_head(
        head_major(queries, block_count),
        head_major(key_rows, block_count),
        head_major(value_rows, block_count),
        head_major(strength, block_count),
        head_major(decay_rows, block_count),
        current_ids,
        prior_ids,
    )


def blockwise(left, right, precision=HIGHEST):
    return jnp.einsum("hbij,hbjk->hbik", left, right, precision=precision)


def batched(left, right):
    return jnp.einsum("hij,hjk->hik", left, right, precision=HIGHEST)


def sweep_blocks(block_terms, start_state):
    blocks_first = tuple((jnp.swapaxes(member, 0, 1) for member in block_terms))

    def advance(carry_state, pieces):
        within, query_decayed, targets, corrector, transition, increment = pieces
        fresh_values = targets - batched(corrector, carry_state)
        emitted = batched(query_decayed, carry_state) + batched(within, fresh_values)
        updated = batched(transition, carry_state) + increment
        return (updated, emitted)

    final_state, emitted = lax.scan(advance, start_state, blocks_first)
    return emitted


def tokens_first(emitted):
    heads_count = emitted.shape[1]
    return jnp.transpose(emitted, (0, 2, 1, 3)).reshape(-1, heads_count, emitted.shape[3])


def gate_output(mixed_heads, gate_raw, norm_gain):
    square_mean = jnp.mean(mixed_heads * mixed_heads, axis=-1, keepdims=True)
    gate_values = jax.nn.silu(gate_raw.reshape(mixed_heads.shape).astype(jnp.float32))
    normed = mixed_heads / jnp.sqrt(square_mean + 1e-06) * norm_gain * gate_values
    return normed.astype(jnp.bfloat16).reshape(mixed_heads.shape[0], -1)


def post_norm(hidden, post_gain):
    hidden_full = hidden.astype(jnp.float32)
    square_mean = jnp.mean(hidden_full * hidden_full, axis=-1, keepdims=True)
    return (hidden_full / jnp.sqrt(square_mean + 1e-06) * post_gain).astype(jnp.bfloat16)


def expert_apply_rows(rows_in, up_matrix, down_matrix):
    hidden_units = down_matrix.shape[0]
    gate_up = jnp.dot(rows_in, up_matrix, preferred_element_type=jnp.float32)
    activated = (jax.nn.silu(gate_up[:, :hidden_units]) * gate_up[:, hidden_units:]).astype(
        jnp.bfloat16
    )
    return jnp.dot(activated, down_matrix, preferred_element_type=jnp.float32).astype(jnp.bfloat16)


def expert_apply(arrived, expert_up, expert_down):
    member_rows = arrived[:, 0]
    flattened = member_rows.reshape(-1, member_rows.shape[-1])
    result = expert_apply_rows(flattened, expert_up[0], expert_down[0])
    outputs = [result.reshape(member_rows.shape)]
    return jnp.stack(outputs, axis=1)


def route_slots(routes, experts_all, capacity):
    assigned = routes.reshape(-1)
    expert_ids = jnp.arange(experts_all, dtype=jnp.int32)
    onehot = (assigned[:, None] == expert_ids[None, :]).astype(jnp.int32)
    slot_rank = jnp.sum((jnp.cumsum(onehot, axis=0) - 1) * onehot, axis=1)
    return assigned * capacity + slot_rank


def per_device(
    pair_raw,
    value_raw,
    gate_raw,
    write_strength,
    log_decay,
    segment_ids,
    pair_filter,
    value_filter,
    norm_gain,
    out_weight,
    residual,
    post_gain,
    routes,
    route_weights,
    expert_up,
    expert_down,
):
    local_tokens = pair_raw.shape[0]
    kernel = value_filter.shape[0]
    pair_flat = pair_raw.reshape(local_tokens, -1)
    pair_width = pair_flat.shape[1]
    rim_rows = jnp.concatenate(
        [pair_flat[local_tokens - (kernel - 1) :], value_raw[local_tokens - (kernel - 1) :]], axis=1
    )
    before = passed_along(rim_rows, CTX, 1)
    first_token = lax.axis_index(CTX) * local_tokens
    padded_ids = jnp.concatenate([jnp.full((kernel - 1,), -1, jnp.int32), segment_ids])
    window_ids = lax.dynamic_slice_in_dim(padded_ids, first_token, local_tokens + kernel - 1)
    pair_padded = jnp.concatenate([before[:, :pair_width], pair_flat])
    value_padded = jnp.concatenate([before[:, pair_width:], value_raw])
    queries, key_rows, value_rows = mixer_inputs(
        pair_padded, value_padded, pair_filter, value_filter, window_ids, kernel
    )
    block_terms = block_tables(
        queries, key_rows, value_rows, write_strength, log_decay, window_ids, kernel
    )
    within, query_decayed, targets, corrector, transition, increment = block_terms
    heads_here, block_count = transition.shape[:2]
    prefix_map = jnp.broadcast_to(jnp.eye(DK, dtype=jnp.float32), (heads_here, DK, DK))
    prefix_shift = jnp.zeros((heads_here, DK, DV), jnp.float32)
    prefix_maps, prefix_shifts = ([], [])
    for block in range(block_count):
        prefix_maps.append(prefix_map)
        prefix_shifts.append(prefix_shift)
        prefix_map = batched(transition[:, block], prefix_map)
        prefix_shift = batched(transition[:, block], prefix_shift) + increment[:, block]
    stacked_maps = jnp.stack(prefix_maps, axis=1)
    stacked_shifts = jnp.stack(prefix_shifts, axis=1)
    query_effective = query_decayed - blockwise(within, corrector, LEAF)
    through_entry = blockwise(query_effective, stacked_maps, LEAF)
    fixed_part = blockwise(query_effective, stacked_shifts, LEAF) + blockwise(within, targets, LEAF)
    entering = scanned_entry(prefix_map, prefix_shift, CTX)
    emitted = (
        jnp.einsum("hbtk,hkv->hbtv", through_entry, entering, precision=LEAF) + fixed_part
    )
    mixed_heads = jnp.transpose(emitted, (1, 2, 0, 3)).reshape(-1, heads_here, DV)
    gated_out = gate_output(mixed_heads, gate_raw, norm_gain)
    partial_out = jnp.dot(gated_out, out_weight, preferred_element_type=jnp.float32)
    pairs = lax.axis_size("head")
    if pairs == 2:
        side = lax.axis_index("head")
        halves = partial_out.reshape(2, -1, partial_out.shape[1])
        kept = lax.dynamic_index_in_dim(halves, side, keepdims=False)
        given = lax.dynamic_index_in_dim(halves, 1 - side, keepdims=False)
        attention = kept + lax.ppermute(
            given.astype(jnp.bfloat16), "head", [(0, 1), (1, 0)]
        ).astype(jnp.float32)
    else:
        attention = lax.psum_scatter(
            partial_out.astype(jnp.bfloat16), "head", scatter_dimension=0, tiled=True
        ).astype(jnp.float32)
    hidden = (residual.astype(jnp.float32) + attention).astype(jnp.bfloat16)
    expert_in = post_norm(hidden, post_gain)
    levels = lax.axis_size("ctx_hi")
    level = lax.axis_index("ctx_hi")
    local_experts = expert_up.shape[0]
    per_level = lax.axis_size("ctx_lo") * lax.axis_size("head") * local_experts
    experts_all = levels * per_level
    local_rows = routes.shape[0]
    top_count = routes.shape[1]
    capacity = local_rows * top_count * 5 // (4 * experts_all)
    own_high = route_weights.astype(jnp.bfloat16)
    own_low = (route_weights - own_high.astype(jnp.float32)).astype(jnp.bfloat16)
    spare = -(-(3 * top_count) // 128) * 128 - 3 * top_count
    packed = jnp.concatenate(
        [
            expert_in,
            routes.astype(jnp.bfloat16),
            own_high,
            own_low,
            jnp.zeros((local_rows, spare), jnp.bfloat16),
        ],
        axis=1,
    )
    expert_ids = jnp.arange(experts_all, dtype=jnp.int32)
    earlier_rows = (
        lax.broadcasted_iota(jnp.int32, (local_rows, local_rows), 0)
        > lax.broadcasted_iota(jnp.int32, (local_rows, local_rows), 1)
    ).astype(jnp.bfloat16)
    slots_total = per_level * capacity
    slot_ids = jnp.arange(slots_total, dtype=jnp.int32)
    level_axes = ("ctx_lo", "head")
    routed = None
    for turn in range(levels):
        if turn == 0:
            chunk = packed
        else:
            chunk = lax.ppermute(
                packed, "ctx_hi", [(i, (i - turn) % levels) for i in range(levels)]
            )
        chunk_in = chunk[:, :D]
        chunk_routes = chunk[:, D : D + top_count].astype(jnp.int32)
        chunk_high = chunk[:, D + top_count : D + 2 * top_count]
        chunk_low = chunk[:, D + 2 * top_count : D + 3 * top_count]
        route_hot = chunk_routes[:, :, None] == expert_ids[None, None, :]
        row_hot = jnp.any(route_hot, axis=1).astype(jnp.bfloat16)
        earlier = jnp.dot(earlier_rows, row_hot, preferred_element_type=jnp.float32)
        slot_rank = jnp.sum(jnp.where(route_hot, earlier[:, None, :], 0.0), axis=2).astype(
            jnp.int32
        )
        slot_index = jnp.where(
            chunk_routes // per_level == level,
            (chunk_routes % per_level) * capacity + slot_rank,
            -1,
        )
        hits = slot_index[:, :, None] == slot_ids[None, None, :]
        picker = jnp.any(hits, axis=1).astype(jnp.bfloat16)
        outgoing = lax.dot_general(
            picker, chunk_in, (((0,), (0,)), ((), ())), preferred_element_type=jnp.float32
        ).astype(jnp.bfloat16)
        outgoing = outgoing.reshape(per_level // local_experts, local_experts * capacity, D)
        arrived = lax.all_to_all(outgoing, level_axes, split_axis=0, concat_axis=0, tiled=True)
        arrived = arrived.reshape(per_level // local_experts, local_experts, capacity, D)
        answered = jnp.stack(
            [
                expert_apply_rows(
                    arrived[:, member].reshape(-1, D), expert_up[member], expert_down[member]
                ).reshape(arrived.shape[0], capacity, D)
                for member in range(local_experts)
            ],
            axis=1,
        ).reshape(per_level // local_experts, local_experts * capacity, D)
        returned = lax.all_to_all(answered, level_axes, split_axis=0, concat_axis=0, tiled=True)
        result_rows = returned.reshape(slots_total, D)
        weight_high = jnp.sum(jnp.where(hits, chunk_high[:, :, None], 0.0), axis=1).astype(
            jnp.bfloat16
        )
        weight_low = jnp.sum(jnp.where(hits, chunk_low[:, :, None], 0.0), axis=1).astype(
            jnp.bfloat16
        )
        partial = jnp.dot(weight_high, result_rows, preferred_element_type=jnp.float32) + jnp.dot(
            weight_low, result_rows, preferred_element_type=jnp.float32
        )
        if turn == 0:
            routed = partial
        else:
            routed = routed + lax.ppermute(
                partial.astype(jnp.bfloat16),
                "ctx_hi",
                [(i, (i + turn) % levels) for i in range(levels)],
            ).astype(jnp.float32)
    combined = hidden.astype(jnp.float32) + routed
    return combined.astype(jnp.bfloat16)


def split_mesh(mesh):
    groups, peers, pairs = (mesh.shape["group"], mesh.shape["ctx"], mesh.shape["head"])
    low = 4 if peers % 4 == 0 else 1
    devices = mesh.devices.reshape(groups, peers // low, low, pairs)
    return Mesh(devices, ("group", "ctx_hi", "ctx_lo", "head"))


def solution(mesh):
    return jax.shard_map(
        per_device,
        mesh=split_mesh(mesh),
        in_specs=(
            P(("group", "ctx_hi", "ctx_lo"), None, "head"),
            P(("group", "ctx_hi", "ctx_lo"), "head"),
            P(("group", "ctx_hi", "ctx_lo"), "head"),
            P(("group", "ctx_hi", "ctx_lo"), "head"),
            P(("group", "ctx_hi", "ctx_lo"), "head"),
            P("group"),
            P(None, None, "head"),
            P(None, "head"),
            P(),
            P("head", None),
            P(("group", "ctx_hi", "ctx_lo", "head"), None),
            P(),
            P(("group", "ctx_hi", "ctx_lo", "head"), None),
            P(("group", "ctx_hi", "ctx_lo", "head"), None),
            P(("ctx_hi", "ctx_lo", "head"), None, None),
            P(("ctx_hi", "ctx_lo", "head"), None, None),
        ),
        out_specs=P(("group", "ctx_hi", "ctx_lo", "head"), None),
        check_vma=False,
    )
```

```python
import jax
import jax.numpy as jnp
from jax import lax
from jax.sharding import Mesh, PartitionSpec as P

D = 2048
DK = 128
DV = 128
BLOCK = 64
CTX = ("ctx_hi", "ctx_lo")


HIGHEST = lax.Precision.HIGH


def passed_along(block, axis, distance):
    devices = range(lax.axis_size(axis))
    route = [(i - distance, i) for i in devices if i - distance in devices]
    return lax.ppermute(block, axis, route)


def scanned_entry(whole_map, whole_shift, axis):
    peers, position = (lax.axis_size(axis), lax.axis_index(axis))
    distance = 1
    while distance < peers:
        last = 2 * distance >= peers
        reached = position >= distance
        if last:
            shift_in = passed_along(whole_shift.astype(jnp.bfloat16), axis, distance)
            shift_in = shift_in.astype(jnp.float32)
        else:
            both = jnp.stack([whole_map, whole_shift]).astype(jnp.bfloat16)
            both_in = passed_along(both, axis, distance).astype(jnp.float32)
            map_in, shift_in = (both_in[0], both_in[1])
        new_shift = batched(whole_map, shift_in) + whole_shift
        if not last:
            whole_map = jnp.where(reached, batched(whole_map, map_in), whole_map)
        whole_shift = jnp.where(reached, new_shift, whole_shift)
        distance *= 2
    return passed_along(whole_shift.astype(jnp.bfloat16), axis, 1).astype(jnp.float32)


def precise_dot(left, right):
    return jnp.dot(left, right, precision=HIGHEST, preferred_element_type=jnp.float32)


def causal_filter(padded_raw, filter_taps, padded_ids, kernel):
    length = padded_raw.shape[0] - (kernel - 1)
    source = padded_raw.astype(jnp.float32)
    current_ids = padded_ids[kernel - 1 :]
    summed = jnp.zeros((length, padded_raw.shape[1]), jnp.float32)
    for lag_step in range(kernel):
        offset_start = kernel - 1 - lag_step
        shifted = source[offset_start : offset_start + length]
        matching = (padded_ids[offset_start : offset_start + length] == current_ids).astype(
            jnp.float32
        )
        summed = summed + filter_taps[lag_step] * shifted * matching[:, None]
    return jax.nn.silu(summed)


def unit_rows(values_in):
    return values_in / jnp.sqrt(jnp.sum(values_in * values_in, axis=-1, keepdims=True) + 1e-06)


def mixer_inputs(pair_padded, value_padded, pair_filter, value_filter, padded_ids, kernel):
    pair_act = causal_filter(pair_padded, pair_filter.reshape(kernel, -1), padded_ids, kernel)
    length = pair_act.shape[0]
    pair_heads = pair_act.reshape(length, 2, -1, DK)
    queries = unit_rows(pair_heads[:, 0]) * DK ** (-0.5)
    key_rows = unit_rows(pair_heads[:, 1])
    value_rows = causal_filter(value_padded, value_filter, padded_ids, kernel).reshape(
        length, -1, DV
    )
    repeat_factor = value_rows.shape[1] // key_rows.shape[1]
    return (
        jnp.repeat(queries, repeat_factor, axis=1),
        jnp.repeat(key_rows, repeat_factor, axis=1),
        value_rows,
    )


def unit_lower_inverse(system):
    size = system.shape[-1]
    row_index = lax.broadcasted_iota(jnp.int32, (size, size), 0)
    col_index = lax.broadcasted_iota(jnp.int32, (size, size), 1)
    inverse = jnp.broadcast_to(jnp.eye(size, dtype=system.dtype), system.shape)
    width = 1
    while width < size:
        linking = (
            (row_index // (2 * width) == col_index // (2 * width))
            & ((row_index // width) % 2 == 1)
            & ((col_index // width) % 2 == 0)
        )
        lower_left = jnp.where(linking, system, 0.0)
        inverse = inverse - precise_dot(inverse, precise_dot(lower_left, inverse))
        width *= 2
    return inverse


def block_setup(queries, key_rows, value_rows, strength, decay_rows, segment_here, prior_id):
    cumulative = jnp.cumsum(decay_rows)
    row_index = lax.broadcasted_iota(jnp.int32, (BLOCK, BLOCK), 0)
    col_index = lax.broadcasted_iota(jnp.int32, (BLOCK, BLOCK), 1)
    same_segment = segment_here[:, None] == segment_here[None, :]
    causal = (row_index >= col_index) & same_segment
    strictly = (row_index > col_index) & same_segment
    decay_matrix = jnp.where(
        causal, jnp.exp(jnp.where(causal, cumulative[:, None] - cumulative[None, :], 0.0)), 0.0
    )
    carried_in = (segment_here == prior_id).astype(jnp.float32)
    keyed_beta = key_rows * strength[:, None]
    coupling = jnp.where(strictly, precise_dot(keyed_beta, key_rows.T) * decay_matrix, 0.0)
    system = jnp.eye(BLOCK, dtype=jnp.float32) + coupling
    stacked = jnp.concatenate(
        [value_rows * strength[:, None], keyed_beta * (jnp.exp(cumulative) * carried_in)[:, None]],
        axis=1,
    )
    solved = precise_dot(unit_lower_inverse(system), stacked)
    targets = solved[:, :DV]
    corrector = solved[:, DV:]
    within = jnp.where(causal, precise_dot(queries, key_rows.T) * decay_matrix, 0.0)
    query_decayed = queries * (jnp.exp(cumulative) * carried_in)[:, None]
    final_log = cumulative[BLOCK - 1]
    weighting = (segment_here == segment_here[BLOCK - 1]).astype(jnp.float32) * jnp.exp(
        final_log - cumulative
    )
    keys_weighted = key_rows * weighting[:, None]
    transition = jnp.exp(final_log) * carried_in[BLOCK - 1] * jnp.eye(
        DK, dtype=jnp.float32
    ) - precise_dot(keys_weighted.T, corrector)
    increment = precise_dot(keys_weighted.T, targets)
    return (within, query_decayed, targets, corrector, transition, increment)


def head_major(array_in, block_count):
    moved = jnp.moveaxis(array_in, 1, 0)
    return moved.reshape((array_in.shape[1], block_count, BLOCK) + array_in.shape[2:])


def block_tables(queries, key_rows, value_rows, strength, decay_rows, padded_ids, kernel):
    length = queries.shape[0]
    block_count = length // BLOCK
    current_ids = padded_ids[kernel - 1 :].reshape(block_count, BLOCK)
    prior_ids = padded_ids[kernel - 2 : kernel - 2 + length : BLOCK]
    per_block = jax.vmap(block_setup, in_axes=(0, 0, 0, 0, 0, 0, 0))
    per_head = jax.vmap(per_block, in_axes=(0, 0, 0, 0, 0, None, None))
    return per_head(
        head_major(queries, block_count),
        head_major(key_rows, block_count),
        head_major(value_rows, block_count),
        head_major(strength, block_count),
        head_major(decay_rows, block_count),
        current_ids,
        prior_ids,
    )


def blockwise(left, right):
    return jnp.einsum("hbij,hbjk->hbik", left, right, precision=HIGHEST)


def batched(left, right):
    return jnp.einsum("hij,hjk->hik", left, right, precision=HIGHEST)


def sweep_blocks(block_terms, start_state):
    blocks_first = tuple((jnp.swapaxes(member, 0, 1) for member in block_terms))

    def advance(carry_state, pieces):
        within, query_decayed, targets, corrector, transition, increment = pieces
        fresh_values = targets - batched(corrector, carry_state)
        emitted = batched(query_decayed, carry_state) + batched(within, fresh_values)
        updated = batched(transition, carry_state) + increment
        return (updated, emitted)

    final_state, emitted = lax.scan(advance, start_state, blocks_first)
    return emitted


def tokens_first(emitted):
    heads_count = emitted.shape[1]
    return jnp.transpose(emitted, (0, 2, 1, 3)).reshape(-1, heads_count, emitted.shape[3])


def gate_output(mixed_heads, gate_raw, norm_gain):
    square_mean = jnp.mean(mixed_heads * mixed_heads, axis=-1, keepdims=True)
    gate_values = jax.nn.silu(gate_raw.reshape(mixed_heads.shape).astype(jnp.float32))
    normed = mixed_heads / jnp.sqrt(square_mean + 1e-06) * norm_gain * gate_values
    return normed.astype(jnp.bfloat16).reshape(mixed_heads.shape[0], -1)


def post_norm(hidden, post_gain):
    hidden_full = hidden.astype(jnp.float32)
    square_mean = jnp.mean(hidden_full * hidden_full, axis=-1, keepdims=True)
    return (hidden_full / jnp.sqrt(square_mean + 1e-06) * post_gain).astype(jnp.bfloat16)


def expert_apply_rows(rows_in, up_matrix, down_matrix):
    hidden_units = down_matrix.shape[0]
    gate_up = jnp.dot(rows_in, up_matrix, preferred_element_type=jnp.float32)
    activated = (jax.nn.silu(gate_up[:, :hidden_units]) * gate_up[:, hidden_units:]).astype(
        jnp.bfloat16
    )
    return jnp.dot(activated, down_matrix, preferred_element_type=jnp.float32).astype(jnp.bfloat16)


def expert_apply(arrived, expert_up, expert_down):
    member_rows = arrived[:, 0]
    flattened = member_rows.reshape(-1, member_rows.shape[-1])
    result = expert_apply_rows(flattened, expert_up[0], expert_down[0])
    outputs = [result.reshape(member_rows.shape)]
    return jnp.stack(outputs, axis=1)


def route_slots(routes, experts_all, capacity):
    assigned = routes.reshape(-1)
    expert_ids = jnp.arange(experts_all, dtype=jnp.int32)
    onehot = (assigned[:, None] == expert_ids[None, :]).astype(jnp.int32)
    slot_rank = jnp.sum((jnp.cumsum(onehot, axis=0) - 1) * onehot, axis=1)
    return assigned * capacity + slot_rank


def per_device(
    pair_raw,
    value_raw,
    gate_raw,
    write_strength,
    log_decay,
    segment_ids,
    pair_filter,
    value_filter,
    norm_gain,
    out_weight,
    residual,
    post_gain,
    routes,
    route_weights,
    expert_up,
    expert_down,
):
    local_tokens = pair_raw.shape[0]
    kernel = value_filter.shape[0]
    pair_flat = pair_raw.reshape(local_tokens, -1)
    pair_width = pair_flat.shape[1]
    rim_rows = jnp.concatenate(
        [pair_flat[local_tokens - (kernel - 1) :], value_raw[local_tokens - (kernel - 1) :]], axis=1
    )
    before = passed_along(rim_rows, CTX, 1)
    first_token = lax.axis_index(CTX) * local_tokens
    padded_ids = jnp.concatenate([jnp.full((kernel - 1,), -1, jnp.int32), segment_ids])
    window_ids = lax.dynamic_slice_in_dim(padded_ids, first_token, local_tokens + kernel - 1)
    pair_padded = jnp.concatenate([before[:, :pair_width], pair_flat])
    value_padded = jnp.concatenate([before[:, pair_width:], value_raw])
    queries, key_rows, value_rows = mixer_inputs(
        pair_padded, value_padded, pair_filter, value_filter, window_ids, kernel
    )
    block_terms = block_tables(
        queries, key_rows, value_rows, write_strength, log_decay, window_ids, kernel
    )
    within, query_decayed, targets, corrector, transition, increment = block_terms
    heads_here, block_count = transition.shape[:2]
    prefix_map, prefix_shift = (transition[:, 0], increment[:, 0])
    prefix_maps, prefix_shifts = ([], [])
    for block in range(1, block_count):
        prefix_maps.append(prefix_map)
        prefix_shifts.append(prefix_shift)
        prefix_map = batched(transition[:, block], prefix_map)
        prefix_shift = batched(transition[:, block], prefix_shift) + increment[:, block]
    query_effective = query_decayed - blockwise(within, corrector)
    through_entry = query_effective
    fixed_part = blockwise(within, targets)
    if block_count > 1:
        stacked_maps = jnp.stack(prefix_maps, axis=1)
        stacked_shifts = jnp.stack(prefix_shifts, axis=1)
        later = query_effective[:, 1:]
        through_entry = jnp.concatenate(
            [query_effective[:, :1], blockwise(later, stacked_maps)], axis=1
        )
        fixed_part = fixed_part + jnp.concatenate(
            [jnp.zeros_like(later[:, :1]), blockwise(later, stacked_shifts)], axis=1
        )
    entering = scanned_entry(prefix_map, prefix_shift, CTX)
    emitted = (
        jnp.einsum("hbtk,hkv->hbtv", through_entry, entering, precision=HIGHEST) + fixed_part
    )
    mixed_heads = jnp.transpose(emitted, (1, 2, 0, 3)).reshape(-1, heads_here, DV)
    gated_out = gate_output(mixed_heads, gate_raw, norm_gain)
    partial_out = jnp.dot(gated_out, out_weight, preferred_element_type=jnp.float32)
    pairs = lax.axis_size("head")
    if pairs == 2:
        side = lax.axis_index("head")
        halves = partial_out.reshape(2, -1, partial_out.shape[1])
        kept = lax.dynamic_index_in_dim(halves, side, keepdims=False)
        given = lax.dynamic_index_in_dim(halves, 1 - side, keepdims=False)
        attention = kept + lax.ppermute(
            given.astype(jnp.bfloat16), "head", [(0, 1), (1, 0)]
        ).astype(jnp.float32)
    else:
        attention = lax.psum_scatter(
            partial_out.astype(jnp.bfloat16), "head", scatter_dimension=0, tiled=True
        ).astype(jnp.float32)
    hidden = (residual.astype(jnp.float32) + attention).astype(jnp.bfloat16)
    expert_in = post_norm(hidden, post_gain)
    levels = lax.axis_size("ctx_hi")
    level = lax.axis_index("ctx_hi")
    local_experts = expert_up.shape[0]
    per_level = lax.axis_size("ctx_lo") * lax.axis_size("head") * local_experts
    experts_all = levels * per_level
    local_rows = routes.shape[0]
    top_count = routes.shape[1]
    capacity = local_rows * top_count * 5 // (4 * experts_all)
    own_high = route_weights.astype(jnp.bfloat16)
    own_low = (route_weights - own_high.astype(jnp.float32)).astype(jnp.bfloat16)
    spare = -(-(3 * top_count) // 128) * 128 - 3 * top_count
    packed = jnp.concatenate(
        [
            expert_in,
            routes.astype(jnp.bfloat16),
            own_high,
            own_low,
            jnp.zeros((local_rows, spare), jnp.bfloat16),
        ],
        axis=1,
    )
    expert_ids = jnp.arange(experts_all, dtype=jnp.int32)
    earlier_rows = (
        lax.broadcasted_iota(jnp.int32, (local_rows, local_rows), 0)
        > lax.broadcasted_iota(jnp.int32, (local_rows, local_rows), 1)
    ).astype(jnp.bfloat16)
    slots_total = per_level * capacity
    slot_ids = jnp.arange(slots_total, dtype=jnp.int32)
    level_axes = ("ctx_lo", "head")
    routed = None
    for turn in range(levels):
        if turn == 0:
            chunk = packed
        else:
            chunk = lax.ppermute(
                packed, "ctx_hi", [(i, (i - turn) % levels) for i in range(levels)]
            )
        chunk_in = chunk[:, :D]
        chunk_routes = chunk[:, D : D + top_count].astype(jnp.int32)
        chunk_high = chunk[:, D + top_count : D + 2 * top_count]
        chunk_low = chunk[:, D + 2 * top_count : D + 3 * top_count]
        route_hot = chunk_routes[:, :, None] == expert_ids[None, None, :]
        row_hot = jnp.any(route_hot, axis=1).astype(jnp.bfloat16)
        earlier = jnp.dot(earlier_rows, row_hot, preferred_element_type=jnp.float32)
        slot_rank = jnp.sum(jnp.where(route_hot, earlier[:, None, :], 0.0), axis=2).astype(
            jnp.int32
        )
        slot_index = jnp.where(
            chunk_routes // per_level == level,
            (chunk_routes % per_level) * capacity + slot_rank,
            -1,
        )
        hits = slot_index[:, :, None] == slot_ids[None, None, :]
        picker = jnp.any(hits, axis=1).astype(jnp.bfloat16)
        outgoing = lax.dot_general(
            picker, chunk_in, (((0,), (0,)), ((), ())), preferred_element_type=jnp.float32
        ).astype(jnp.bfloat16)
        outgoing = outgoing.reshape(per_level // local_experts, local_experts * capacity, D)
        arrived = lax.all_to_all(outgoing, level_axes, split_axis=0, concat_axis=0, tiled=True)
        arrived = arrived.reshape(per_level // local_experts, local_experts, capacity, D)
        answered = jnp.stack(
            [
                expert_apply_rows(
                    arrived[:, member].reshape(-1, D), expert_up[member], expert_down[member]
                ).reshape(arrived.shape[0], capacity, D)
                for member in range(local_experts)
            ],
            axis=1,
        ).reshape(per_level // local_experts, local_experts * capacity, D)
        returned = lax.all_to_all(answered, level_axes, split_axis=0, concat_axis=0, tiled=True)
        result_rows = returned.reshape(slots_total, D)
        weight_high = jnp.sum(jnp.where(hits, chunk_high[:, :, None], 0.0), axis=1).astype(
            jnp.bfloat16
        )
        weight_low = jnp.sum(jnp.where(hits, chunk_low[:, :, None], 0.0), axis=1).astype(
            jnp.bfloat16
        )
        partial = jnp.dot(weight_high, result_rows, preferred_element_type=jnp.float32) + jnp.dot(
            weight_low, result_rows, preferred_element_type=jnp.float32
        )
        if turn == 0:
            routed = partial
        else:
            routed = routed + lax.ppermute(
                partial.astype(jnp.bfloat16),
                "ctx_hi",
                [(i, (i + turn) % levels) for i in range(levels)],
            ).astype(jnp.float32)
    combined = hidden.astype(jnp.float32) + routed
    return combined.astype(jnp.bfloat16)


def split_mesh(mesh):
    groups, peers, pairs = (mesh.shape["group"], mesh.shape["ctx"], mesh.shape["head"])
    low = 4 if peers % 4 == 0 else 1
    devices = mesh.devices.reshape(groups, peers // low, low, pairs)
    return Mesh(devices, ("group", "ctx_hi", "ctx_lo", "head"))


def solution(mesh):
    return jax.shard_map(
        per_device,
        mesh=split_mesh(mesh),
        in_specs=(
            P(("group", "ctx_hi", "ctx_lo"), None, "head"),
            P(("group", "ctx_hi", "ctx_lo"), "head"),
            P(("group", "ctx_hi", "ctx_lo"), "head"),
            P(("group", "ctx_hi", "ctx_lo"), "head"),
            P(("group", "ctx_hi", "ctx_lo"), "head"),
            P("group"),
            P(None, None, "head"),
            P(None, "head"),
            P(),
            P("head", None),
            P(("group", "ctx_hi", "ctx_lo", "head"), None),
            P(),
            P(("group", "ctx_hi", "ctx_lo", "head"), None),
            P(("group", "ctx_hi", "ctx_lo", "head"), None),
            P(("ctx_hi", "ctx_lo", "head"), None, None),
            P(("ctx_hi", "ctx_lo", "head"), None, None),
        ),
        out_specs=P(("group", "ctx_hi", "ctx_lo", "head"), None),
        check_vma=False,
    )
```
